32 devices in a mesh: seq: 2 (over y), fsdp: 16 (over z, x, core).
Axes of the slice: x: 2, y: 2, z: 4, core: 2. Of those that a mesh axis runs over, the one named last changes fastest.
Arguments:
- layer_input: bfloat16 [16, 256, 8192], P('fsdp', 'seq'), may hold values from -6 to 6
- queries: bfloat16 [16, 256, 4096], P('fsdp', 'seq'), may hold values from -24 to 24
- key_states: bfloat16 [16, 256, 512], P('fsdp', 'seq'), may hold values from -24 to 24
- out_grad: bfloat16 [16, 256, 4096], P('fsdp', 'seq'), may hold values from -6 to 6
- doc_positions: int32 [16, 256], P('fsdp'), may hold values from 0 to 127, as said below
- drop_seed: int32 [], replicated, may hold values from 0 to 2147483646
- value_weight: bfloat16 [8192, 512], P(('seq', 'fsdp')), may hold values from -0.0625 to 0.0625
Outputs:
- query_grad: bfloat16 [16, 256, 4096], P('fsdp', 'seq')
- key_grad: bfloat16 [16, 256, 512], P('fsdp', 'seq')
- input_grad: bfloat16 [16, 256, 8192], P('fsdp', 'seq')
- weight_grad: bfloat16 [8192, 512], P(('seq', 'fsdp'))
The draws below stay inside these ranges and needn't reach their ends.
Inputs may be any that keep to these rules, and one draw needn't show every extreme that they name: `doc_positions`: the value at a token is its distance from the first token of its document; documents are runs of consecutive tokens of at most 128 tokens, and each sequence has one of exactly 128.
All inputs are finite; a program needn't handle non-finite values.
Results may differ from the reference program's by a relative error of at most 0.0078.
Values may be sent and summed in bfloat16 or wider, within the bound.
No kernel may reach another device: no remote copies, remote signals or barrier semaphores. Data moves between devices by JAX's collectives and lax.ppermute only.
A program may use at most 128 MiB of HBM per device.

```python
import math
import jax
import jax.numpy as jnp
from jax import lax

D = 8192
HD = 128
QH = 32
KVH = 4
GROUP = 8
SEQ = 256
BATCH = 16
DOC = 128


def drawn_parts(key):
    key_base = jax.random.normal(jax.random.fold_in(key, 101), (BATCH, SEQ, KVH, HD), jnp.float32)
    return key_base


def draw_queries(key, part):
    drawn = jax.random.normal(jax.random.fold_in(key, 107), (BATCH, SEQ, QH, HD), jnp.float32)
    result = jnp.clip(drawn, -6.0, 6.0)
    return result.reshape(BATCH, SEQ, QH * HD).astype(jnp.bfloat16)


def draw_key_states(key, part):
    key_base = drawn_parts(key)
    result = jnp.clip(key_base, -6.0, 6.0)
    return result.reshape(BATCH, SEQ, KVH * HD).astype(jnp.bfloat16)


def draw_doc_positions(key, part):
    index_row = jnp.arange(SEQ, dtype=jnp.int32)

    def one_row(row_key):
        cuts = jax.random.randint(jax.random.fold_in(row_key, 1), (SEQ,), 0, 97) == 0
        start = jax.random.randint(jax.random.fold_in(row_key, 2), (), 0, SEQ - DOC + 1)
        inside = (index_row > start) & (index_row < start + DOC)
        cuts = cuts & jnp.logical_not(inside) | (index_row == start) | (index_row == start + DOC) | (index_row == 0)

        def advance(previous, cut_here):
            following = jnp.where(cut_here | (previous + 1 >= DOC), 0, previous + 1)
            return (following, following)
        unused, positions = lax.scan(advance, jnp.int32(-1), cuts)
        return positions
    row_keys = jax.vmap(lambda number: jax.random.fold_in(key, number))(jnp.arange(BATCH, dtype=jnp.int32))
    return jax.vmap(one_row)(row_keys)


def with_spikes(values, rng, source, target, parts, factor):
    owner, partner = [(jnp.arange(values.shape[axis_at]) // (values.shape[axis_at] // parts)).reshape([-1 if axis == axis_at else 1 for axis in range(values.ndim)]) for axis_at in (source, target)]
    chosen = jax.random.permutation(rng, parts)[partner]
    strong = (owner == chosen) | (owner == (partner + parts // 2) % parts)
    return jnp.where(strong, factor * values, values)


def levels(key, extent, pieces, least, high):
    level, own = 1.0, jax.random.fold_in(key, 6)
    for axis_at, parts in pieces:
        draws = jnp.exp(jax.random.uniform(jax.random.fold_in(own, axis_at), (parts,), jnp.float32, least / len(pieces), high / len(pieces)))
        level = level * jnp.repeat(draws, extent[axis_at] // parts).reshape([-1 if axis == axis_at else 1 for axis in range(len(extent))])
    return level


def scatter_about(rng, shape, width, bound, pieces=(), kind=jnp.bfloat16):
    factor_of = levels(rng, shape, pieces, -0.22, 0.18) if pieces else 1.0
    array = jax.random.normal(rng, shape, jnp.float32) * width * factor_of
    return jnp.minimum(jnp.maximum(array, -bound), bound).astype(kind)


def bell_draw_with(key, shape, width, reach, shards, heavy, kind=jnp.bfloat16):
    array = width * jax.random.normal(key, shape, jnp.float32)
    if shards:
        array = array * levels(key, shape, shards, -0.22, 0.18)
    return jnp.clip(with_spikes(array, jax.random.fold_in(key, 3), *heavy), -reach, reach).astype(kind)


def setup_inputs(seed: int = 0) -> dict:
    key_list = jax.random.split(jax.random.key(seed), 8)
    return {
        "layer_input": bell_draw_with(key_list[0], (BATCH, SEQ, D), 1.0, 6.0, ((0, 16), (1, 2)), (0, 2, 16, 2.0)),
        "queries": draw_queries(jax.random.fold_in(key_list[7], 71), 0),
        "key_states": draw_key_states(jax.random.fold_in(key_list[7], 71), 0),
        "out_grad": scatter_about(key_list[3], (BATCH, SEQ, QH * HD), 1.0, 6.0, ((0, 16), (1, 2))),
        "doc_positions": draw_doc_positions(jax.random.fold_in(key_list[7], 71), 0),
        "drop_seed": jax.random.randint(key_list[5], (), 0, 2147483647).astype(jnp.int32),
        "value_weight": scatter_about(key_list[6], (D, KVH * HD), D ** -0.5, 0.0625, ((0, 32),)),
    }


drop_cut = 1677722
keep_scale = 1.0 / 0.9

def mixing(state):
    state = state ^ lax.shift_right_logical(state, jnp.full_like(state, 16))
    state = state * 2146121005
    state = state ^ lax.shift_right_logical(state, jnp.full_like(state, 15))
    state = state * 739982445
    state = state ^ lax.shift_right_logical(state, jnp.full_like(state, 16))
    return state

def head_pass(query_h, grad_h, key_h, value_h, visible, cells, head_seed):
    inverse_root = 1.0 / math.sqrt(query_h.shape[1])
    scores = jnp.dot(query_h, key_h.T, preferred_element_type=jnp.float32) * inverse_root
    masked = jnp.where(visible, scores, -jnp.inf)
    row_max = lax.optimization_barrier(jnp.max(masked, axis=1, keepdims=True))
    exp_terms = jnp.where(visible, jnp.exp(scores - row_max), 0.0)
    attn_probs = exp_terms / lax.optimization_barrier(jnp.sum(exp_terms, axis=1, keepdims=True))
    kept_mask = mixing(cells + head_seed) & 16777215 >= drop_cut
    dropped = jnp.where(kept_mask, attn_probs * keep_scale, 0.0).astype(jnp.bfloat16)
    raw_grad = jnp.dot(grad_h, value_h.T, preferred_element_type=jnp.float32)
    prob_grad = jnp.where(kept_mask, raw_grad * keep_scale, 0.0)
    row_delta = lax.optimization_barrier(jnp.sum(attn_probs * prob_grad, axis=1, keepdims=True))
    score_grad = (attn_probs * (prob_grad - row_delta)).astype(jnp.bfloat16)
    query_part = jnp.dot(score_grad, key_h, preferred_element_type=jnp.float32) * inverse_root
    key_part = jnp.dot(score_grad.T, query_h, preferred_element_type=jnp.float32) * inverse_root
    value_part = jnp.dot(dropped.T, grad_h, preferred_element_type=jnp.float32)
    return (query_part, key_part, value_part)

def reference(layer_input, queries, key_states, out_grad, doc_positions, drop_seed, value_weight):
    rows_idx = lax.broadcasted_iota(jnp.int32, (SEQ, SEQ), 0)
    cols_idx = lax.broadcasted_iota(jnp.int32, (SEQ, SEQ), 1)
    cells = rows_idx * SEQ + cols_idx

    def one_sequence(total, items):
        batch_index, inputs_b, query_b, key_b, grad_b, position_b = items
        values_b = jnp.dot(inputs_b, value_weight, preferred_element_type=jnp.float32).astype(jnp.bfloat16)
        visible = (cols_idx <= rows_idx) & (rows_idx - cols_idx <= position_b[:, None])
        base_seed = mixing(drop_seed + batch_index * 1000003)

        def one_group(group_index):
            key_h = lax.dynamic_slice_in_dim(key_b, group_index * HD, HD, 1)
            value_h = lax.dynamic_slice_in_dim(values_b, group_index * HD, HD, 1)

            def one_query(global_head):
                head_seed = mixing(base_seed ^ global_head * 1640531527)
                query_h = lax.dynamic_slice_in_dim(query_b, global_head * HD, HD, 1)
                grad_h = lax.dynamic_slice_in_dim(grad_b, global_head * HD, HD, 1)
                return head_pass(query_h, grad_h, key_h, value_h, visible, cells, head_seed)
            heads = group_index * GROUP + jnp.arange(GROUP, dtype=jnp.int32)
            query_parts, key_parts, value_parts = lax.map(one_query, heads)
            return (query_parts.astype(jnp.bfloat16), lax.optimization_barrier(jnp.sum(key_parts, axis=0)), lax.optimization_barrier(jnp.sum(value_parts, axis=0)))
        query_all, key_all, value_all = lax.map(one_group, jnp.arange(KVH, dtype=jnp.int32))
        query_grad_b = jnp.transpose(query_all.reshape(QH, SEQ, HD), (1, 0, 2)).reshape(SEQ, QH * HD)
        key_grad_b = jnp.transpose(key_all, (1, 0, 2)).reshape(SEQ, KVH * HD).astype(jnp.bfloat16)
        value_grad_b = jnp.transpose(value_all, (1, 0, 2)).reshape(SEQ, KVH * HD).astype(jnp.bfloat16)
        input_grad_b = jnp.dot(value_grad_b, value_weight.T, preferred_element_type=jnp.float32).astype(jnp.bfloat16)
        total = total + jnp.dot(inputs_b.T, value_grad_b, preferred_element_type=jnp.float32)
        return (total, (query_grad_b, key_grad_b, input_grad_b))
    start_total = jnp.zeros((D, KVH * HD), jnp.float32)
    batch_ids = jnp.arange(BATCH, dtype=jnp.int32)
    total, outputs = lax.scan(one_sequence, start_total, (batch_ids, layer_input, queries, key_states, out_grad, doc_positions))
    query_grad, key_grad, input_grad = outputs
    weight_grad = (total * (1.0 / math.sqrt(BATCH * SEQ))).astype(jnp.bfloat16)
    return (query_grad, key_grad, input_grad, weight_grad)
```

```python
import functools
import math

import jax
import jax.numpy as jnp
from jax import lax
from jax.experimental import pallas as pl
from jax.experimental.pallas import tpu as pltpu
from jax.sharding import PartitionSpec as P

HD = 128
QH = 32
KVH = 4
ROWS = 128


drop_cut = 1677722
keep_scale = 1.0 / 0.9


def mixing(state):
    state = state ^ lax.shift_right_logical(state, jnp.full_like(state, 16))
    state = state * 2146121005
    state = state ^ lax.shift_right_logical(state, jnp.full_like(state, 15))
    state = state * 739982445
    state = state ^ lax.shift_right_logical(state, jnp.full_like(state, 16))
    return state


def attention_kernel(seeds_ref, pos_ref, q_ref, do_ref, k_ref, v_ref, dq_ref, dk_ref, dv_ref, *,
                     seq_len, per_copy):
    c = pl.program_id(0)
    h = pl.program_id(1)
    head_seed = seeds_ref[c * per_copy + h]
    inverse_root = 1.0 / math.sqrt(HD)
    last_dims = (((1,), (1,)), ((), ()))
    first_dims = (((0,), (0,)), ((), ()))

    @pl.when(h == 0)
    def _():
        dk_ref[...] = jnp.zeros_like(dk_ref)
        dv_ref[...] = jnp.zeros_like(dv_ref)

    for r in range(seq_len // ROWS):
        width = (r + 1) * ROWS
        lo = r * ROWS
        q = q_ref[lo:lo + ROWS, :]
        do = do_ref[lo:lo + ROWS, :]
        k = k_ref[0:width, :]
        v = v_ref[0:width, :]
        pos = pos_ref[lo:lo + ROWS, :]
        scores = lax.dot_general(q, k, last_dims, preferred_element_type=jnp.float32) * inverse_root
        rows = lax.broadcasted_iota(jnp.int32, (ROWS, width), 0) + lo
        cols = lax.broadcasted_iota(jnp.int32, (ROWS, width), 1)
        visible = (cols <= rows) & (rows - cols <= pos)
        masked = jnp.where(visible, scores, -jnp.inf)
        row_max = jnp.max(masked, axis=1, keepdims=True)
        exp_terms = jnp.where(visible, jnp.exp(scores - row_max), 0.0)
        probs = exp_terms / jnp.sum(exp_terms, axis=1, keepdims=True)
        kept = (mixing(rows * seq_len + cols + head_seed) & 16777215) >= drop_cut
        dropped = jnp.where(kept, probs * keep_scale, 0.0).astype(jnp.bfloat16)
        raw = lax.dot_general(do, v, last_dims, preferred_element_type=jnp.float32)
        prob_grad = jnp.where(kept, raw * keep_scale, 0.0)
        row_delta = jnp.sum(probs * prob_grad, axis=1, keepdims=True)
        score_grad = (probs * (prob_grad - row_delta)).astype(jnp.bfloat16)
        dq = jnp.dot(score_grad, k, preferred_element_type=jnp.float32) * inverse_root
        dq_ref[lo:lo + ROWS, :] = dq.astype(dq_ref.dtype)
        dk_ref[0:width, :] += (
            lax.dot_general(score_grad, q, first_dims, preferred_element_type=jnp.float32)
            * inverse_root
        )
        dv_ref[0:width, :] += lax.dot_general(
            dropped, do, first_dims, preferred_element_type=jnp.float32
        )


def attention(seeds, pos, query_dev, grad_dev, key_dev, value_dev, copies_dev, per_copy):
    seq_len = query_dev.shape[0]
    head_map = lambda c, h, s: (0, c * per_copy + h)
    copy_map = lambda c, h, s: (0, c)
    whole_map = lambda c, h, s: (0, 0)
    kernel = functools.partial(attention_kernel, seq_len=seq_len, per_copy=per_copy)
    return pl.pallas_call(
        kernel,
        grid_spec=pltpu.PrefetchScalarGridSpec(
            num_scalar_prefetch=1,
            grid=(copies_dev, per_copy),
            in_specs=[
                pl.BlockSpec((seq_len, 1), whole_map),
                pl.BlockSpec((seq_len, HD), head_map),
                pl.BlockSpec((seq_len, HD), head_map),
                pl.BlockSpec((seq_len, HD), copy_map),
                pl.BlockSpec((seq_len, HD), copy_map),
            ],
            out_specs=[
                pl.BlockSpec((seq_len, HD), head_map),
                pl.BlockSpec((seq_len, HD), copy_map),
                pl.BlockSpec((seq_len, HD), copy_map),
            ],
        ),
        out_shape=[
            jax.ShapeDtypeStruct(query_dev.shape, jnp.bfloat16),
            jax.ShapeDtypeStruct(key_dev.shape, jnp.float32),
            jax.ShapeDtypeStruct(key_dev.shape, jnp.float32),
        ],
        compiler_params=pltpu.CompilerParams(
            dimension_semantics=("arbitrary", "arbitrary"),
            vmem_limit_bytes=48 * 1024 * 1024,
        ),
    )(seeds, pos, query_dev, grad_dev, key_dev, value_dev)


def per_device(layer_input, queries, key_states, out_grad, doc_positions, drop_seed, value_weight):
    seq_devices = lax.axis_size("seq")
    fsdp_devices = lax.axis_size("fsdp")
    seq_index = lax.axis_index("seq")
    batch_index = lax.axis_index("fsdp")
    tok_rows = layer_input.shape[1]
    seq_len = tok_rows * seq_devices
    local_input = layer_input[0]
    copies_total = max(KVH, seq_devices)
    copies_dev = copies_total // seq_devices
    per_copy = QH // copies_total
    heads_dev = QH // seq_devices
    repeat_count = copies_total // KVH
    full_weight = lax.all_gather(value_weight, ("seq", "fsdp"), axis=0, tiled=True)
    values_loc = jnp.dot(local_input, full_weight, preferred_element_type=jnp.float32).astype(
        jnp.bfloat16
    )
    key_rep = jnp.repeat(key_states[0].reshape(tok_rows, KVH, HD), repeat_count, axis=1).reshape(
        tok_rows, copies_total * HD
    )
    value_rep = jnp.repeat(values_loc.reshape(tok_rows, KVH, HD), repeat_count, axis=1).reshape(
        tok_rows, copies_total * HD
    )
    query_dev, grad_dev, key_dev, value_dev = (
        lax.all_to_all(queries[0], "seq", split_axis=1, concat_axis=0, tiled=True),
        lax.all_to_all(out_grad[0], "seq", split_axis=1, concat_axis=0, tiled=True),
        lax.all_to_all(key_rep, "seq", split_axis=1, concat_axis=0, tiled=True),
        lax.all_to_all(value_rep, "seq", split_axis=1, concat_axis=0, tiled=True),
    )
    base_seed = mixing(drop_seed + batch_index * 1000003)
    global_heads = seq_index * heads_dev + jnp.arange(heads_dev, dtype=jnp.int32)
    seeds = mixing(base_seed ^ global_heads * 1640531527)
    pos = doc_positions[0][:, None]
    dq, dk, dv = attention(seeds, pos, query_dev, grad_dev, key_dev, value_dev, copies_dev, per_copy)

    query_grad = lax.all_to_all(dq, "seq", split_axis=0, concat_axis=1, tiled=True)
    key_back = lax.all_to_all(
        dk.astype(jnp.bfloat16), "seq", split_axis=0, concat_axis=1, tiled=True
    ).astype(jnp.float32)
    key_grad = (
        jnp.sum(key_back.reshape(tok_rows, KVH, repeat_count, HD), axis=2)
        .reshape(tok_rows, KVH * HD)
        .astype(jnp.bfloat16)
    )

    last_dims = (((1,), (1,)), ((), ()))
    total_tokens = fsdp_devices * seq_len
    if total_tokens * 2 <= full_weight.shape[0] * 4:
        vg_all = lax.all_gather(dv.astype(jnp.bfloat16), ("seq", "fsdp"), axis=0, tiled=False)
        vg_all = vg_all.reshape(seq_devices, fsdp_devices, seq_len, copies_dev, HD)
        vg_tok = jnp.transpose(vg_all, (1, 2, 0, 3, 4)).reshape(
            fsdp_devices, seq_len, KVH, repeat_count, HD
        )
        vg_tok = jnp.sum(vg_tok.astype(jnp.float32), axis=3).astype(jnp.bfloat16).reshape(
            fsdp_devices, seq_devices, tok_rows, KVH * HD
        )
        value_grad = lax.dynamic_index_in_dim(
            lax.dynamic_index_in_dim(vg_tok, batch_index, 0, keepdims=False),
            seq_index,
            0,
            keepdims=False,
        )
        input_cols = lax.all_to_all(
            local_input, ("seq", "fsdp"), split_axis=1, concat_axis=0, tiled=True
        )
        cols_in = input_cols.reshape(seq_devices, fsdp_devices, tok_rows, input_cols.shape[1])
        summed = lax.dot_general(
            cols_in,
            vg_tok,
            (((0, 1, 2), (1, 0, 2)), ((), ())),
            preferred_element_type=jnp.float32,
        )
    else:
        value_back = lax.all_to_all(
            dv.astype(jnp.bfloat16), "seq", split_axis=0, concat_axis=1, tiled=True
        ).astype(jnp.float32)
        value_grad = (
            jnp.sum(value_back.reshape(tok_rows, KVH, repeat_count, HD), axis=2)
            .reshape(tok_rows, KVH * HD)
            .astype(jnp.bfloat16)
        )
        summed = lax.psum_scatter(
            lax.dot_general(
                local_input, value_grad, (((0,), (0,)), ((), ())),
                preferred_element_type=jnp.float32,
            ),
            ("seq", "fsdp"),
            scatter_dimension=0,
            tiled=True,
        )
    input_grad = lax.dot_general(
        value_grad, full_weight, last_dims, preferred_element_type=jnp.float32
    ).astype(jnp.bfloat16)
    weight_grad = (summed * (1.0 / math.sqrt(fsdp_devices * seq_len))).astype(jnp.bfloat16)
    return (query_grad[None], key_grad[None], input_grad[None], weight_grad)


def solution(mesh):
    return jax.shard_map(
        per_device,
        mesh=mesh,
        in_specs=(
            P("fsdp", "seq", None),
            P("fsdp", "seq", None),
            P("fsdp", "seq", None),
            P("fsdp", "seq", None),
            P("fsdp", None),
            P(),
            P(("seq", "fsdp"), None),
        ),
        out_specs=(
            P("fsdp", "seq", None),
            P("fsdp", "seq", None),
            P("fsdp", "seq", None),
            P(("seq", "fsdp"), None),
        ),
        check_vma=False,
    )
```

```python
import functools
import math

import jax
import jax.numpy as jnp
from jax import lax
from jax.experimental import pallas as pl
from jax.experimental.pallas import tpu as pltpu
from jax.sharding import PartitionSpec as P

HD = 128
QH = 32
KVH = 4
ROWS = 128


drop_cut = 1677722
keep_scale = 1.0 / 0.9


def mixing(state):
    state = state ^ lax.shift_right_logical(state, jnp.full_like(state, 16))
    state = state * 2146121005
    state = state ^ lax.shift_right_logical(state, jnp.full_like(state, 15))
    state = state * 739982445
    state = state ^ lax.shift_right_logical(state, jnp.full_like(state, 16))
    return state


def attention_kernel(seeds_ref, pos_ref, q_ref, do_ref, k_ref, *refs, seq_len, per_copy, first):
    if first:
        (dv_ref,) = refs
    else:
        v_ref, dq_ref, dk_ref = refs
    c = pl.program_id(0)
    h = pl.program_id(1)
    head_seed = seeds_ref[c * per_copy + h]
    inverse_root = 1.0 / math.sqrt(HD)
    last_dims = (((1,), (1,)), ((), ()))
    first_dims = (((0,), (0,)), ((), ()))

    acc_ref = dv_ref if first else dk_ref

    @pl.when(h == 0)
    def _():
        acc_ref[...] = jnp.zeros_like(acc_ref)

    for r in range(seq_len // ROWS):
        width = (r + 1) * ROWS
        lo = r * ROWS
        q = q_ref[lo:lo + ROWS, :]
        do = do_ref[lo:lo + ROWS, :]
        k = k_ref[0:width, :]
        pos = pos_ref[lo:lo + ROWS, :]
        scores = lax.dot_general(q, k, last_dims, preferred_element_type=jnp.float32) * inverse_root
        rows = lax.broadcasted_iota(jnp.int32, (ROWS, width), 0) + lo
        cols = lax.broadcasted_iota(jnp.int32, (ROWS, width), 1)
        visible = (cols <= rows) & (rows - cols <= pos)
        masked = jnp.where(visible, scores, -jnp.inf)
        row_max = jnp.max(masked, axis=1, keepdims=True)
        exp_terms = jnp.where(visible, jnp.exp(scores - row_max), 0.0)
        probs = exp_terms / jnp.sum(exp_terms, axis=1, keepdims=True)
        kept = (mixing(rows * seq_len + cols + head_seed) & 16777215) >= drop_cut
        if first:
            dropped = jnp.where(kept, probs * keep_scale, 0.0).astype(jnp.bfloat16)
            dv_ref[0:width, :] += lax.dot_general(
                dropped, do, first_dims, preferred_element_type=jnp.float32
            )
            continue
        v = v_ref[0:width, :]
        raw = lax.dot_general(do, v, last_dims, preferred_element_type=jnp.float32)
        prob_grad = jnp.where(kept, raw * keep_scale, 0.0)
        row_delta = jnp.sum(probs * prob_grad, axis=1, keepdims=True)
        score_grad = (probs * (prob_grad - row_delta)).astype(jnp.bfloat16)
        dq = jnp.dot(score_grad, k, preferred_element_type=jnp.float32) * inverse_root
        dq_ref[lo:lo + ROWS, :] = dq.astype(dq_ref.dtype)
        dk_ref[0:width, :] += (
            lax.dot_general(score_grad, q, first_dims, preferred_element_type=jnp.float32)
            * inverse_root
        )


def attention(seeds, pos, query_dev, grad_dev, key_dev, value_dev, copies_dev, per_copy):
    seq_len = query_dev.shape[0]
    head_map = lambda c, h, s: (0, c * per_copy + h)
    copy_map = lambda c, h, s: (0, c)
    whole_map = lambda c, h, s: (0, 0)
    first = value_dev is None
    kernel = functools.partial(
        attention_kernel, seq_len=seq_len, per_copy=per_copy, first=first
    )
    in_specs = [
        pl.BlockSpec((seq_len, 1), whole_map),
        pl.BlockSpec((seq_len, HD), head_map),
        pl.BlockSpec((seq_len, HD), head_map),
        pl.BlockSpec((seq_len, HD), copy_map),
    ]
    operands = [seeds, pos, query_dev, grad_dev, key_dev]
    acc = jax.ShapeDtypeStruct(key_dev.shape, jnp.float32)
    if first:
        out_specs = [pl.BlockSpec((seq_len, HD), copy_map)]
        out_shape = [acc]
    else:
        in_specs.append(pl.BlockSpec((seq_len, HD), copy_map))
        operands.append(value_dev)
        out_specs = [pl.BlockSpec((seq_len, HD), head_map), pl.BlockSpec((seq_len, HD), copy_map)]
        out_shape = [jax.ShapeDtypeStruct(query_dev.shape, jnp.bfloat16), acc]
    return pl.pallas_call(
        kernel,
        grid_spec=pltpu.PrefetchScalarGridSpec(
            num_scalar_prefetch=1,
            grid=(copies_dev, per_copy),
            in_specs=in_specs,
            out_specs=out_specs,
        ),
        out_shape=out_shape,
        compiler_params=pltpu.CompilerParams(
            dimension_semantics=("arbitrary", "arbitrary"),
            vmem_limit_bytes=48 * 1024 * 1024,
        ),
    )(*operands)


def per_device(layer_input, queries, key_states, out_grad, doc_positions, drop_seed, value_weight):
    seq_devices = lax.axis_size("seq")
    fsdp_devices = lax.axis_size("fsdp")
    seq_index = lax.axis_index("seq")
    batch_index = lax.axis_index("fsdp")
    tok_rows = layer_input.shape[1]
    seq_len = tok_rows * seq_devices
    local_input = layer_input[0]
    copies_total = max(KVH, seq_devices)
    copies_dev = copies_total // seq_devices
    per_copy = QH // copies_total
    heads_dev = QH // seq_devices
    repeat_count = copies_total // KVH
    full_weight = lax.all_gather(value_weight, ("seq", "fsdp"), axis=0, tiled=True)
    block_rows = value_weight.shape[0]
    input_cols = lax.all_to_all(
        local_input.reshape(tok_rows, seq_devices, fsdp_devices, block_rows),
        "fsdp",
        split_axis=2,
        concat_axis=0,
        tiled=True,
    ).reshape(fsdp_devices * tok_rows, seq_devices * block_rows)
    key_rep = jnp.repeat(key_states[0].reshape(tok_rows, KVH, HD), repeat_count, axis=1).reshape(
        tok_rows, copies_total * HD
    )
    query_dev, grad_dev, key_dev = (
        lax.all_to_all(queries[0], "seq", split_axis=1, concat_axis=0, tiled=True),
        lax.all_to_all(out_grad[0], "seq", split_axis=1, concat_axis=0, tiled=True),
        lax.all_to_all(key_rep, "seq", split_axis=1, concat_axis=0, tiled=True),
    )
    base_seed = mixing(drop_seed + batch_index * 1000003)
    global_heads = seq_index * heads_dev + jnp.arange(heads_dev, dtype=jnp.int32)
    seeds = mixing(base_seed ^ global_heads * 1640531527)
    pos = doc_positions[0][:, None]
    (dv,) = attention(seeds, pos, query_dev, grad_dev, key_dev, None, copies_dev, per_copy)
    dv, full_weight = lax.optimization_barrier((dv, full_weight))
    value_back = lax.all_to_all(
        dv.astype(jnp.bfloat16), "seq", split_axis=0, concat_axis=1, tiled=True
    ).astype(jnp.float32)
    value_grad = (
        jnp.sum(value_back.reshape(tok_rows, KVH, repeat_count, HD), axis=2)
        .reshape(tok_rows, KVH * HD)
        .astype(jnp.bfloat16)
    )
    value_grads = lax.all_gather(value_grad, "fsdp", axis=0, tiled=True)

    values_loc = jnp.dot(local_input, full_weight, preferred_element_type=jnp.float32).astype(
        jnp.bfloat16
    )
    value_rep = jnp.repeat(values_loc.reshape(tok_rows, KVH, HD), repeat_count, axis=1).reshape(
        tok_rows, copies_total * HD
    )
    value_dev = lax.all_to_all(value_rep, "seq", split_axis=1, concat_axis=0, tiled=True)
    dq, dk = attention(seeds, pos, query_dev, grad_dev, key_dev, value_dev, copies_dev, per_copy)
    value_grads, input_cols, dq, dk = lax.optimization_barrier((value_grads, input_cols, dq, dk))
    partial = lax.dot_general(
        input_cols, value_grads, (((0,), (0,)), ((), ())), preferred_element_type=jnp.float32
    )
    summed = lax.psum_scatter(partial, "seq", scatter_dimension=0, tiled=True)
    weight_grad = (summed * (1.0 / math.sqrt(fsdp_devices * seq_len))).astype(jnp.bfloat16)
    query_grad = lax.all_to_all(dq, "seq", split_axis=0, concat_axis=1, tiled=True)
    key_back = lax.all_to_all(
        dk.astype(jnp.bfloat16), "seq", split_axis=0, concat_axis=1, tiled=True
    ).astype(jnp.float32)
    key_grad = (
        jnp.sum(key_back.reshape(tok_rows, KVH, repeat_count, HD), axis=2)
        .reshape(tok_rows, KVH * HD)
        .astype(jnp.bfloat16)
    )
    last_dims = (((1,), (1,)), ((), ()))
    input_grad = lax.dot_general(
        value_grad, full_weight, last_dims, preferred_element_type=jnp.float32
    ).astype(jnp.bfloat16)
    return (query_grad[None], key_grad[None], input_grad[None], weight_grad)


def solution(mesh):
    return jax.shard_map(
        per_device,
        mesh=mesh,
        in_specs=(
            P("fsdp", "seq", None),
            P("fsdp", "seq", None),
            P("fsdp", "seq", None),
            P("fsdp", "seq", None),
            P("fsdp", None),
            P(),
            P(("seq", "fsdp"), None),
        ),
        out_specs=(
            P("fsdp", "seq", None),
            P("fsdp", "seq", None),
            P("fsdp", "seq", None),
            P(("seq", "fsdp"), None),
        ),
        check_vma=False,
    )
```

```python
import functools
import math

import jax
import jax.numpy as jnp
from jax import lax
from jax.experimental import pallas as pl
from jax.experimental.pallas import tpu as pltpu
from jax.sharding import PartitionSpec as P

HD = 128
QH = 32
KVH = 4
ROWS = 128


drop_cut = 1677722
keep_scale = 1.0 / 0.9


def mixing(state):
    state = state ^ lax.shift_right_logical(state, jnp.full_like(state, 16))
    state = state * 2146121005
    state = state ^ lax.shift_right_logical(state, jnp.full_like(state, 15))
    state = state * 739982445
    state = state ^ lax.shift_right_logical(state, jnp.full_like(state, 16))
    return state


def attention_kernel(seeds_ref, pos_ref, q_ref, do_ref, k_ref, *refs, seq_len, per_copy, first):
    if first:
        (dv_ref,) = refs
    else:
        v_ref, dq_ref, dk_ref = refs
    c = pl.program_id(0)
    h = pl.program_id(1)
    head_seed = seeds_ref[c * per_copy + h]
    inverse_root = 1.0 / math.sqrt(HD)
    last_dims = (((1,), (1,)), ((), ()))
    first_dims = (((0,), (0,)), ((), ()))

    acc_ref = dv_ref if first else dk_ref

    @pl.when(h == 0)
    def _():
        acc_ref[...] = jnp.zeros_like(acc_ref)

    for r in range(seq_len // ROWS):
        width = (r + 1) * ROWS
        lo = r * ROWS
        q = q_ref[lo:lo + ROWS, :]
        do = do_ref[lo:lo + ROWS, :]
        k = k_ref[0:width, :]
        pos = pos_ref[lo:lo + ROWS, :]
        scores = lax.dot_general(q, k, last_dims, preferred_element_type=jnp.float32) * inverse_root
        rows = lax.broadcasted_iota(jnp.int32, (ROWS, width), 0) + lo
        cols = lax.broadcasted_iota(jnp.int32, (ROWS, width), 1)
        visible = (cols <= rows) & (rows - cols <= pos)
        masked = jnp.where(visible, scores, -jnp.inf)
        row_max = jnp.max(masked, axis=1, keepdims=True)
        exp_terms = jnp.where(visible, jnp.exp(scores - row_max), 0.0)
        probs = exp_terms / jnp.sum(exp_terms, axis=1, keepdims=True)
        kept = (mixing(rows * seq_len + cols + head_seed) & 16777215) >= drop_cut
        if first:
            dropped = jnp.where(kept, probs * keep_scale, 0.0).astype(jnp.bfloat16)
            dv_ref[0:width, :] += lax.dot_general(
                dropped, do, first_dims, preferred_element_type=jnp.float32
            )
            continue
        v = v_ref[0:width, :]
        raw = lax.dot_general(do, v, last_dims, preferred_element_type=jnp.float32)
        prob_grad = jnp.where(kept, raw * keep_scale, 0.0)
        row_delta = jnp.sum(probs * prob_grad, axis=1, keepdims=True)
        score_grad = (probs * (prob_grad - row_delta)).astype(jnp.bfloat16)
        dq = jnp.dot(score_grad, k, preferred_element_type=jnp.float32) * inverse_root
        dq_ref[lo:lo + ROWS, :] = dq.astype(dq_ref.dtype)
        dk_ref[0:width, :] += (
            lax.dot_general(score_grad, q, first_dims, preferred_element_type=jnp.float32)
            * inverse_root
        )


def attention(seeds, pos, query_dev, grad_dev, key_dev, value_dev, copies_dev, per_copy):
    seq_len = query_dev.shape[0]
    head_map = lambda c, h, s: (0, c * per_copy + h)
    copy_map = lambda c, h, s: (0, c)
    whole_map = lambda c, h, s: (0, 0)
    first = value_dev is None
    kernel = functools.partial(
        attention_kernel, seq_len=seq_len, per_copy=per_copy, first=first
    )
    in_specs = [
        pl.BlockSpec((seq_len, 1), whole_map),
        pl.BlockSpec((seq_len, HD), head_map),
        pl.BlockSpec((seq_len, HD), head_map),
        pl.BlockSpec((seq_len, HD), copy_map),
    ]
    operands = [seeds, pos, query_dev, grad_dev, key_dev]
    acc = jax.ShapeDtypeStruct(key_dev.shape, jnp.float32)
    if first:
        out_specs = [pl.BlockSpec((seq_len, HD), copy_map)]
        out_shape = [acc]
    else:
        in_specs.append(pl.BlockSpec((seq_len, HD), copy_map))
        operands.append(value_dev)
        out_specs = [pl.BlockSpec((seq_len, HD), head_map), pl.BlockSpec((seq_len, HD), copy_map)]
        out_shape = [jax.ShapeDtypeStruct(query_dev.shape, jnp.bfloat16), acc]
    return pl.pallas_call(
        kernel,
        grid_spec=pltpu.PrefetchScalarGridSpec(
            num_scalar_prefetch=1,
            grid=(copies_dev, per_copy),
            in_specs=in_specs,
            out_specs=out_specs,
        ),
        out_shape=out_shape,
        compiler_params=pltpu.CompilerParams(
            dimension_semantics=("arbitrary", "arbitrary"),
            vmem_limit_bytes=48 * 1024 * 1024,
        ),
    )(*operands)


def per_device(layer_input, queries, key_states, out_grad, doc_positions, drop_seed, value_weight):
    seq_devices = lax.axis_size("seq")
    fsdp_devices = lax.axis_size("fsdp")
    seq_index = lax.axis_index("seq")
    batch_index = lax.axis_index("fsdp")
    tok_rows = layer_input.shape[1]
    seq_len = tok_rows * seq_devices
    local_input = layer_input[0]
    copies_total = max(KVH, seq_devices)
    copies_dev = copies_total // seq_devices
    per_copy = QH // copies_total
    heads_dev = QH // seq_devices
    repeat_count = copies_total // KVH
    full_weight = lax.all_gather(value_weight, ("seq", "fsdp"), axis=0, tiled=True)
    block_rows = value_weight.shape[0]
    input_cols = lax.all_to_all(
        local_input.reshape(tok_rows, seq_devices, fsdp_devices, block_rows),
        "fsdp",
        split_axis=2,
        concat_axis=0,
        tiled=True,
    ).reshape(fsdp_devices * tok_rows, seq_devices * block_rows)
    key_rep = jnp.repeat(key_states[0].reshape(tok_rows, KVH, HD), repeat_count, axis=1).reshape(
        tok_rows, copies_total * HD
    )
    query_dev, grad_dev, key_dev = (
        lax.all_to_all(queries[0], "seq", split_axis=1, concat_axis=0, tiled=True),
        lax.all_to_all(out_grad[0], "seq", split_axis=1, concat_axis=0, tiled=True),
        lax.all_to_all(key_rep, "seq", split_axis=1, concat_axis=0, tiled=True),
    )
    base_seed = mixing(drop_seed + batch_index * 1000003)
    global_heads = seq_index * heads_dev + jnp.arange(heads_dev, dtype=jnp.int32)
    seeds = mixing(base_seed ^ global_heads * 1640531527)
    pos = doc_positions[0][:, None]
    (dv,) = attention(seeds, pos, query_dev, grad_dev, key_dev, None, copies_dev, per_copy)
    value_back = lax.all_to_all(
        dv.astype(jnp.bfloat16), "seq", split_axis=0, concat_axis=1, tiled=True
    ).astype(jnp.float32)
    value_grad = (
        jnp.sum(value_back.reshape(tok_rows, KVH, repeat_count, HD), axis=2)
        .reshape(tok_rows, KVH * HD)
        .astype(jnp.bfloat16)
    )
    value_grads = lax.all_to_all(
        jnp.broadcast_to(value_grad[None], (fsdp_devices,) + value_grad.shape),
        "fsdp",
        split_axis=0,
        concat_axis=0,
        tiled=True,
    ).reshape(fsdp_devices * tok_rows, KVH * HD)

    partial = lax.dot_general(
        input_cols, value_grads, (((0,), (0,)), ((), ())), preferred_element_type=jnp.float32
    ).reshape(seq_devices, block_rows, KVH * HD)
    summed = lax.dynamic_index_in_dim(partial, seq_index, 0, keepdims=False)
    for shift in range(1, seq_devices):
        piece = lax.dynamic_index_in_dim(
            partial, (seq_index + shift) % seq_devices, 0, keepdims=False
        )
        summed = summed + lax.ppermute(
            piece, "seq", [(i, (i + shift) % seq_devices) for i in range(seq_devices)]
        )
    weight_grad = (summed * (1.0 / math.sqrt(fsdp_devices * seq_len))).astype(jnp.bfloat16)

    values_loc = jnp.dot(local_input, full_weight, preferred_element_type=jnp.float32).astype(
        jnp.bfloat16
    )
    value_rep = jnp.repeat(values_loc.reshape(tok_rows, KVH, HD), repeat_count, axis=1).reshape(
        tok_rows, copies_total * HD
    )
    value_dev = lax.all_to_all(value_rep, "seq", split_axis=1, concat_axis=0, tiled=True)
    dq, dk = attention(seeds, pos, query_dev, grad_dev, key_dev, value_dev, copies_dev, per_copy)
    query_grad = lax.all_to_all(dq, "seq", split_axis=0, concat_axis=1, tiled=True)
    key_back = lax.all_to_all(
        dk.astype(jnp.bfloat16), "seq", split_axis=0, concat_axis=1, tiled=True
    ).astype(jnp.float32)
    key_grad = (
        jnp.sum(key_back.reshape(tok_rows, KVH, repeat_count, HD), axis=2)
        .reshape(tok_rows, KVH * HD)
        .astype(jnp.bfloat16)
    )
    last_dims = (((1,), (1,)), ((), ()))
    input_grad = lax.dot_general(
        value_grad, full_weight, last_dims, preferred_element_type=jnp.float32
    ).astype(jnp.bfloat16)
    return (query_grad[None], key_grad[None], input_grad[None], weight_grad)


def solution(mesh):
    return jax.shard_map(
        per_device,
        mesh=mesh,
        in_specs=(
            P("fsdp", "seq", None),
            P("fsdp", "seq", None),
            P("fsdp", "seq", None),
            P("fsdp", "seq", None),
            P("fsdp", None),
            P(),
            P(("seq", "fsdp"), None),
        ),
        out_specs=(
            P("fsdp", "seq", None),
            P("fsdp", "seq", None),
            P("fsdp", "seq", None),
            P(("seq", "fsdp"), None),
        ),
        check_vma=False,
    )
```

```python
import functools
import math

import jax
import jax.numpy as jnp
from jax import lax
from jax.experimental import pallas as pl
from jax.experimental.pallas import tpu as pltpu
from jax.sharding import PartitionSpec as P

HD = 128
QH = 32
KVH = 4
ROWS = 128
FSDP = ("zx", "core")


drop_cut = 1677722
keep_scale = 1.0 / 0.9


def mixing(state):
    state = state ^ lax.shift_right_logical(state, jnp.full_like(state, 16))
    state = state * 2146121005
    state = state ^ lax.shift_right_logical(state, jnp.full_like(state, 15))
    state = state * 739982445
    state = state ^ lax.shift_right_logical(state, jnp.full_like(state, 16))
    return state


def attention_kernel(seeds_ref, pos_ref, q_ref, do_ref, k_ref, *refs, seq_len, per_copy, first):
    if first:
        (dv_ref,) = refs
    else:
        v_ref, dq_ref, dk_ref = refs
    c = pl.program_id(0)
    h = pl.program_id(1)
    head_seed = seeds_ref[c * per_copy + h]
    inverse_root = 1.0 / math.sqrt(HD)
    last_dims = (((1,), (1,)), ((), ()))
    first_dims = (((0,), (0,)), ((), ()))

    acc_ref = dv_ref if first else dk_ref

    @pl.when(h == 0)
    def _():
        acc_ref[...] = jnp.zeros_like(acc_ref)

    for r in range(seq_len // ROWS):
        width = (r + 1) * ROWS
        lo = r * ROWS
        q = q_ref[lo:lo + ROWS, :]
        do = do_ref[lo:lo + ROWS, :]
        k = k_ref[0:width, :]
        pos = pos_ref[lo:lo + ROWS, :]
        scores = lax.dot_general(q, k, last_dims, preferred_element_type=jnp.float32) * inverse_root
        rows = lax.broadcasted_iota(jnp.int32, (ROWS, width), 0) + lo
        cols = lax.broadcasted_iota(jnp.int32, (ROWS, width), 1)
        visible = (cols <= rows) & (rows - cols <= pos)
        masked = jnp.where(visible, scores, -jnp.inf)
        row_max = jnp.max(masked, axis=1, keepdims=True)
        exp_terms = jnp.where(visible, jnp.exp(scores - row_max), 0.0)
        probs = exp_terms / jnp.sum(exp_terms, axis=1, keepdims=True)
        kept = (mixing(rows * seq_len + cols + head_seed) & 16777215) >= drop_cut
        if first:
            dropped = jnp.where(kept, probs * keep_scale, 0.0).astype(jnp.bfloat16)
            dv_ref[0:width, :] += lax.dot_general(
                dropped, do, first_dims, preferred_element_type=jnp.float32
            )
            continue
        v = v_ref[0:width, :]
        raw = lax.dot_general(do, v, last_dims, preferred_element_type=jnp.float32)
        prob_grad = jnp.where(kept, raw * keep_scale, 0.0)
        row_delta = jnp.sum(probs * prob_grad, axis=1, keepdims=True)
        score_grad = (probs * (prob_grad - row_delta)).astype(jnp.bfloat16)
        dq = jnp.dot(score_grad, k, preferred_element_type=jnp.float32) * inverse_root
        dq_ref[lo:lo + ROWS, :] = dq.astype(dq_ref.dtype)
        dk_ref[0:width, :] += (
            lax.dot_general(score_grad, q, first_dims, preferred_element_type=jnp.float32)
            * inverse_root
        )


def attention(seeds, pos, query_dev, grad_dev, key_dev, value_dev, copies_dev, per_copy):
    seq_len = query_dev.shape[0]
    head_map = lambda c, h, s: (0, c * per_copy + h)
    copy_map = lambda c, h, s: (0, c)
    whole_map = lambda c, h, s: (0, 0)
    first = value_dev is None
    kernel = functools.partial(
        attention_kernel, seq_len=seq_len, per_copy=per_copy, first=first
    )
    in_specs = [
        pl.BlockSpec((seq_len, 1), whole_map),
        pl.BlockSpec((seq_len, HD), head_map),
        pl.BlockSpec((seq_len, HD), head_map),
        pl.BlockSpec((seq_len, HD), copy_map),
    ]
    operands = [seeds, pos, query_dev, grad_dev, key_dev]
    acc = jax.ShapeDtypeStruct(key_dev.shape, jnp.float32)
    if first:
        out_specs = [pl.BlockSpec((seq_len, HD), copy_map)]
        out_shape = [acc]
    else:
        in_specs.append(pl.BlockSpec((seq_len, HD), copy_map))
        operands.append(value_dev)
        out_specs = [pl.BlockSpec((seq_len, HD), head_map), pl.BlockSpec((seq_len, HD), copy_map)]
        out_shape = [jax.ShapeDtypeStruct(query_dev.shape, jnp.bfloat16), acc]
    return pl.pallas_call(
        kernel,
        grid_spec=pltpu.PrefetchScalarGridSpec(
            num_scalar_prefetch=1,
            grid=(copies_dev, per_copy),
            in_specs=in_specs,
            out_specs=out_specs,
        ),
        out_shape=out_shape,
        compiler_params=pltpu.CompilerParams(
            dimension_semantics=("arbitrary", "arbitrary"),
            vmem_limit_bytes=48 * 1024 * 1024,
        ),
    )(*operands)


def per_device(layer_input, queries, key_states, out_grad, doc_positions, drop_seed, value_weight):
    seq_devices = lax.axis_size("seq")
    zx_devices = lax.axis_size("zx")
    fsdp_devices = zx_devices * 2
    core_index = lax.axis_index("core")
    seq_index = lax.axis_index("seq")
    batch_index = lax.axis_index(FSDP)
    tok_rows = layer_input.shape[1]
    seq_len = tok_rows * seq_devices
    local_input = layer_input[0]
    copies_total = max(KVH, seq_devices)
    copies_dev = copies_total // seq_devices
    per_copy = QH // copies_total
    heads_dev = QH // seq_devices
    repeat_count = copies_total // KVH
    block_rows = value_weight.shape[0]
    swap = [(0, 1), (1, 0)]
    weight_own = lax.all_gather(value_weight, ("seq", "zx"), axis=0, tiled=True)
    weight_other = lax.ppermute(weight_own, "core", swap)
    input_view = local_input.reshape(tok_rows, seq_devices * zx_devices, 2, block_rows)
    input_own = lax.dynamic_index_in_dim(input_view, core_index, 2, keepdims=False).reshape(
        tok_rows, -1
    )
    input_other = lax.dynamic_index_in_dim(input_view, 1 - core_index, 2, keepdims=False).reshape(
        tok_rows, -1
    )
    input_cols = lax.all_to_all(
        local_input.reshape(tok_rows, seq_devices, fsdp_devices, block_rows),
        FSDP,
        split_axis=2,
        concat_axis=0,
        tiled=True,
    ).reshape(zx_devices, 2, tok_rows, seq_devices * block_rows)
    key_rep = jnp.repeat(key_states[0].reshape(tok_rows, KVH, HD), repeat_count, axis=1).reshape(
        tok_rows, copies_total * HD
    )
    query_dev, grad_dev, key_dev = (
        lax.all_to_all(queries[0], "seq", split_axis=1, concat_axis=0, tiled=True),
        lax.all_to_all(out_grad[0], "seq", split_axis=1, concat_axis=0, tiled=True),
        lax.all_to_all(key_rep, "seq", split_axis=1, concat_axis=0, tiled=True),
    )
    base_seed = mixing(drop_seed + batch_index * 1000003)
    global_heads = seq_index * heads_dev + jnp.arange(heads_dev, dtype=jnp.int32)
    seeds = mixing(base_seed ^ global_heads * 1640531527)
    pos = doc_positions[0][:, None]
    (dv,) = attention(seeds, pos, query_dev, grad_dev, key_dev, None, copies_dev, per_copy)
    value_back = lax.all_to_all(
        dv.astype(jnp.bfloat16), "seq", split_axis=0, concat_axis=1, tiled=True
    ).astype(jnp.float32)
    value_grad = (
        jnp.sum(value_back.reshape(tok_rows, KVH, repeat_count, HD), axis=2)
        .reshape(tok_rows, KVH * HD)
        .astype(jnp.bfloat16)
    )
    grads_own = lax.all_to_all(
        jnp.broadcast_to(value_grad[None], (zx_devices,) + value_grad.shape),
        "zx",
        split_axis=0,
        concat_axis=0,
        tiled=True,
    ).reshape(zx_devices * tok_rows, KVH * HD)
    grads_other = lax.ppermute(grads_own, "core", swap)
    cols_own = lax.dynamic_index_in_dim(input_cols, core_index, 1, keepdims=False).reshape(
        zx_devices * tok_rows, -1
    )
    cols_other = lax.dynamic_index_in_dim(input_cols, 1 - core_index, 1, keepdims=False).reshape(
        zx_devices * tok_rows, -1
    )
    first_dims = (((0,), (0,)), ((), ()))
    partial = (
        lax.dot_general(cols_own, grads_own, first_dims, preferred_element_type=jnp.float32)
        + lax.dot_general(cols_other, grads_other, first_dims, preferred_element_type=jnp.float32)
    ).reshape(seq_devices, block_rows, KVH * HD)
    summed = lax.dynamic_index_in_dim(partial, seq_index, 0, keepdims=False)
    for shift in range(1, seq_devices):
        piece = lax.dynamic_index_in_dim(
            partial, (seq_index + shift) % seq_devices, 0, keepdims=False
        )
        summed = summed + lax.ppermute(
            piece, "seq", [(i, (i + shift) % seq_devices) for i in range(seq_devices)]
        )
    weight_grad = (summed * (1.0 / math.sqrt(fsdp_devices * seq_len))).astype(jnp.bfloat16)

    values_loc = (
        jnp.dot(input_own, weight_own, preferred_element_type=jnp.float32)
        + jnp.dot(input_other, weight_other, preferred_element_type=jnp.float32)
    ).astype(jnp.bfloat16)
    value_rep = jnp.repeat(values_loc.reshape(tok_rows, KVH, HD), repeat_count, axis=1).reshape(
        tok_rows, copies_total * HD
    )
    value_dev = lax.all_to_all(value_rep, "seq", split_axis=1, concat_axis=0, tiled=True)
    dq, dk = attention(seeds, pos, query_dev, grad_dev, key_dev, value_dev, copies_dev, per_copy)
    query_grad = lax.all_to_all(dq, "seq", split_axis=0, concat_axis=1, tiled=True)
    key_back = lax.all_to_all(
        dk.astype(jnp.bfloat16), "seq", split_axis=0, concat_axis=1, tiled=True
    ).astype(jnp.float32)
    key_grad = (
        jnp.sum(key_back.reshape(tok_rows, KVH, repeat_count, HD), axis=2)
        .reshape(tok_rows, KVH * HD)
        .astype(jnp.bfloat16)
    )
    last_dims = (((1,), (1,)), ((), ()))
    grad_own = lax.dot_general(
        value_grad, weight_own, last_dims, preferred_element_type=jnp.float32
    ).astype(jnp.bfloat16).reshape(tok_rows, seq_devices * zx_devices, 1, block_rows)
    grad_other = lax.dot_general(
        value_grad, weight_other, last_dims, preferred_element_type=jnp.float32
    ).astype(jnp.bfloat16).reshape(tok_rows, seq_devices * zx_devices, 1, block_rows)
    input_grad = jnp.where(
        core_index == 0,
        jnp.concatenate([grad_own, grad_other], axis=2),
        jnp.concatenate([grad_other, grad_own], axis=2),
    ).reshape(tok_rows, -1)
    return (query_grad[None], key_grad[None], input_grad[None], weight_grad)


def solution(mesh):
    seq_devices, fsdp_devices = mesh.devices.shape
    chips = jax.sharding.Mesh(
        mesh.devices.reshape(seq_devices, fsdp_devices // 2, 2), ("seq",) + FSDP
    )
    return jax.shard_map(
        per_device,
        mesh=chips,
        in_specs=(
            P(FSDP, "seq", None),
            P(FSDP, "seq", None),
            P(FSDP, "seq", None),
            P(FSDP, "seq", None),
            P(FSDP, None),
            P(),
            P(("seq",) + FSDP, None),
        ),
        out_specs=(
            P(FSDP, "seq", None),
            P(FSDP, "seq", None),
            P(FSDP, "seq", None),
            P(("seq",) + FSDP, None),
        ),
        check_vma=False,
    )
```

```python
import functools
import math

import jax
import jax.numpy as jnp
from jax import lax
from jax.experimental import pallas as pl
from jax.experimental.pallas import tpu as pltpu
from jax.sharding import PartitionSpec as P

HD = 128
QH = 32
KVH = 4
ROWS = 128
FSDP = ("zx", "core")


drop_cut = 1677722
keep_scale = 1.0 / 0.9


def mixing(state):
    state = state ^ lax.shift_right_logical(state, jnp.full_like(state, 16))
    state = state * 2146121005
    state = state ^ lax.shift_right_logical(state, jnp.full_like(state, 15))
    state = state * 739982445
    state = state ^ lax.shift_right_logical(state, jnp.full_like(state, 16))
    return state


def attention_kernel(seeds_ref, offset_ref, pos_ref, q_ref, do_ref, k_ref, *refs, seq_len,
                     per_group, first):
    if first:
        (dv_ref,) = refs
    else:
        v_ref, dq_ref, dk_ref = refs
    g = pl.program_id(0)
    h = pl.program_id(1)
    head_seed = seeds_ref[g * per_group + h]
    inverse_root = 1.0 / math.sqrt(HD)
    last_dims = (((1,), (1,)), ((), ()))
    first_dims = (((0,), (0,)), ((), ()))
    acc_ref = dv_ref if first else dk_ref

    @pl.when(h == 0)
    def _():
        acc_ref[...] = jnp.zeros_like(acc_ref)

    q = q_ref[...]
    do = do_ref[...]
    k = k_ref[...]
    pos = pos_ref[...]
    rows_here = q.shape[0]
    scores = lax.dot_general(q, k, last_dims, preferred_element_type=jnp.float32) * inverse_root
    rows = lax.broadcasted_iota(jnp.int32, (rows_here, seq_len), 0) + offset_ref[0]
    cols = lax.broadcasted_iota(jnp.int32, (rows_here, seq_len), 1)
    visible = (cols <= rows) & (rows - cols <= pos)
    masked = jnp.where(visible, scores, -jnp.inf)
    row_max = jnp.max(masked, axis=1, keepdims=True)
    exp_terms = jnp.where(visible, jnp.exp(scores - row_max), 0.0)
    probs = exp_terms / jnp.sum(exp_terms, axis=1, keepdims=True)
    kept = (mixing(rows * seq_len + cols + head_seed) & 16777215) >= drop_cut
    if first:
        dropped = jnp.where(kept, probs * keep_scale, 0.0).astype(jnp.bfloat16)
        dv_ref[...] += lax.dot_general(dropped, do, first_dims, preferred_element_type=jnp.float32)
        return
    v = v_ref[...]
    raw = lax.dot_general(do, v, last_dims, preferred_element_type=jnp.float32)
    prob_grad = jnp.where(kept, raw * keep_scale, 0.0)
    row_delta = jnp.sum(probs * prob_grad, axis=1, keepdims=True)
    score_grad = (probs * (prob_grad - row_delta)).astype(jnp.bfloat16)
    dq = jnp.dot(score_grad, k, preferred_element_type=jnp.float32) * inverse_root
    dq_ref[...] = dq.astype(dq_ref.dtype)
    dk_ref[...] += (
        lax.dot_general(score_grad, q, first_dims, preferred_element_type=jnp.float32)
        * inverse_root
    )


def attention(seeds, offset, pos, queries, grads, keys, values):
    rows_here = queries.shape[0]
    seq_len = keys.shape[0]
    groups = keys.shape[1] // HD
    per_group = queries.shape[1] // HD // groups
    head_map = lambda g, h, s, o: (0, g * per_group + h)
    group_map = lambda g, h, s, o: (0, g)
    whole_map = lambda g, h, s, o: (0, 0)
    first = values is None
    kernel = functools.partial(
        attention_kernel, seq_len=seq_len, per_group=per_group, first=first
    )
    in_specs = [
        pl.BlockSpec((rows_here, 1), whole_map),
        pl.BlockSpec((rows_here, HD), head_map),
        pl.BlockSpec((rows_here, HD), head_map),
        pl.BlockSpec((seq_len, HD), group_map),
    ]
    operands = [seeds, offset, pos, queries, grads, keys]
    acc = jax.ShapeDtypeStruct(keys.shape, jnp.float32)
    if first:
        out_specs = [pl.BlockSpec((seq_len, HD), group_map)]
        out_shape = [acc]
    else:
        in_specs.append(pl.BlockSpec((seq_len, HD), group_map))
        operands.append(values)
        out_specs = [pl.BlockSpec((rows_here, HD), head_map), pl.BlockSpec((seq_len, HD), group_map)]
        out_shape = [jax.ShapeDtypeStruct(queries.shape, jnp.bfloat16), acc]
    return pl.pallas_call(
        kernel,
        grid_spec=pltpu.PrefetchScalarGridSpec(
            num_scalar_prefetch=2,
            grid=(groups, per_group),
            in_specs=in_specs,
            out_specs=out_specs,
        ),
        out_shape=out_shape,
        compiler_params=pltpu.CompilerParams(
            dimension_semantics=("arbitrary", "arbitrary"),
            vmem_limit_bytes=48 * 1024 * 1024,
        ),
    )(*operands)


def gather_seq(piece, seq_index, seq_devices):
    received = [piece]
    for shift in range(1, seq_devices):
        received.append(
            lax.ppermute(piece, "seq", [(i, (i + shift) % seq_devices) for i in range(seq_devices)])
        )
    order = (seq_index - jnp.arange(seq_devices, dtype=jnp.int32)) % seq_devices
    stacked = jnp.take(jnp.stack(received), order, axis=0)
    return stacked.reshape((seq_devices * piece.shape[0],) + piece.shape[1:])


def reduce_seq(partial, seq_index, seq_devices):
    blocks = partial.reshape((seq_devices, partial.shape[0] // seq_devices) + partial.shape[1:])
    summed = lax.dynamic_index_in_dim(blocks, seq_index, 0, keepdims=False)
    for shift in range(1, seq_devices):
        piece = lax.dynamic_index_in_dim(blocks, (seq_index + shift) % seq_devices, 0, keepdims=False)
        summed = summed + lax.ppermute(
            piece, "seq", [(i, (i + shift) % seq_devices) for i in range(seq_devices)]
        )
    return summed


def per_device(layer_input, queries, key_states, out_grad, doc_positions, drop_seed, value_weight):
    seq_devices = lax.axis_size("seq")
    zx_devices = lax.axis_size("zx")
    fsdp_devices = zx_devices * 2
    core_index = lax.axis_index("core")
    seq_index = lax.axis_index("seq")
    batch_index = lax.axis_index(FSDP)
    tok_rows = layer_input.shape[1]
    seq_len = tok_rows * seq_devices
    local_input = layer_input[0]
    block_rows = value_weight.shape[0]
    swap = [(0, 1), (1, 0)]
    weight_own = lax.all_gather(value_weight, ("seq", "zx"), axis=0, tiled=True)
    weight_other = lax.ppermute(weight_own, "core", swap)
    input_view = local_input.reshape(tok_rows, seq_devices * zx_devices, 2, block_rows)
    input_own = lax.dynamic_index_in_dim(input_view, core_index, 2, keepdims=False).reshape(
        tok_rows, -1
    )
    input_other = lax.dynamic_index_in_dim(input_view, 1 - core_index, 2, keepdims=False).reshape(
        tok_rows, -1
    )
    input_cols = lax.all_to_all(
        local_input.reshape(tok_rows, seq_devices, fsdp_devices, block_rows),
        FSDP,
        split_axis=2,
        concat_axis=0,
        tiled=True,
    ).reshape(zx_devices, 2, tok_rows, seq_devices * block_rows)
    base_seed = mixing(drop_seed + batch_index * 1000003)
    seeds = mixing(base_seed ^ jnp.arange(QH, dtype=jnp.int32) * 1640531527)
    offset = (seq_index * tok_rows).reshape(1).astype(jnp.int32)
    pos = lax.dynamic_slice_in_dim(doc_positions[0], seq_index * tok_rows, tok_rows)[:, None]
    query_loc, grad_loc = queries[0], out_grad[0]
    key_full = gather_seq(key_states[0], seq_index, seq_devices)
    (dv,) = attention(seeds, offset, pos, query_loc, grad_loc, key_full, None)
    value_grad = reduce_seq(dv, seq_index, seq_devices).astype(jnp.bfloat16)
    grads_own = lax.all_to_all(
        jnp.broadcast_to(value_grad[None], (zx_devices,) + value_grad.shape),
        "zx",
        split_axis=0,
        concat_axis=0,
        tiled=True,
    ).reshape(zx_devices * tok_rows, KVH * HD)
    grads_other = lax.ppermute(grads_own, "core", swap)
    cols_own = lax.dynamic_index_in_dim(input_cols, core_index, 1, keepdims=False).reshape(
        zx_devices * tok_rows, -1
    )
    cols_other = lax.dynamic_index_in_dim(input_cols, 1 - core_index, 1, keepdims=False).reshape(
        zx_devices * tok_rows, -1
    )
    first_dims = (((0,), (0,)), ((), ()))
    partial = (
        lax.dot_general(cols_own, grads_own, first_dims, preferred_element_type=jnp.float32)
        + lax.dot_general(cols_other, grads_other, first_dims, preferred_element_type=jnp.float32)
    ).reshape(seq_devices, block_rows, KVH * HD)
    summed = lax.dynamic_index_in_dim(partial, seq_index, 0, keepdims=False)
    for shift in range(1, seq_devices):
        piece = lax.dynamic_index_in_dim(
            partial, (seq_index + shift) % seq_devices, 0, keepdims=False
        )
        summed = summed + lax.ppermute(
            piece, "seq", [(i, (i + shift) % seq_devices) for i in range(seq_devices)]
        )
    weight_grad = (summed * (1.0 / math.sqrt(fsdp_devices * seq_len))).astype(jnp.bfloat16)

    values_loc = (
        jnp.dot(input_own, weight_own, preferred_element_type=jnp.float32)
        + jnp.dot(input_other, weight_other, preferred_element_type=jnp.float32)
    ).astype(jnp.bfloat16)
    value_full = gather_seq(values_loc, seq_index, seq_devices)
    dq, dk = attention(seeds, offset, pos, query_loc, grad_loc, key_full, value_full)
    query_grad = dq
    key_grad = reduce_seq(dk, seq_index, seq_devices).astype(jnp.bfloat16)
    last_dims = (((1,), (1,)), ((), ()))
    grad_own = lax.dot_general(
        value_grad, weight_own, last_dims, preferred_element_type=jnp.float32
    ).astype(jnp.bfloat16).reshape(tok_rows, seq_devices * zx_devices, 1, block_rows)
    grad_other = lax.dot_general(
        value_grad, weight_other, last_dims, preferred_element_type=jnp.float32
    ).astype(jnp.bfloat16).reshape(tok_rows, seq_devices * zx_devices, 1, block_rows)
    input_grad = jnp.where(
        core_index == 0,
        jnp.concatenate([grad_own, grad_other], axis=2),
        jnp.concatenate([grad_other, grad_own], axis=2),
    ).reshape(tok_rows, -1)
    return (query_grad[None], key_grad[None], input_grad[None], weight_grad)


def solution(mesh):
    seq_devices, fsdp_devices = mesh.devices.shape
    chips = jax.sharding.Mesh(
        mesh.devices.reshape(seq_devices, fsdp_devices // 2, 2), ("seq",) + FSDP
    )
    return jax.shard_map(
        per_device,
        mesh=chips,
        in_specs=(
            P(FSDP, "seq", None),
            P(FSDP, "seq", None),
            P(FSDP, "seq", None),
            P(FSDP, "seq", None),
            P(FSDP, None),
            P(),
            P(("seq",) + FSDP, None),
        ),
        out_specs=(
            P(FSDP, "seq", None),
            P(FSDP, "seq", None),
            P(FSDP, "seq", None),
            P(("seq",) + FSDP, None),
        ),
        check_vma=False,
    )
```

```python
import functools
import math

import jax
import jax.numpy as jnp
from jax import lax
from jax.experimental import pallas as pl
from jax.experimental.pallas import tpu as pltpu
from jax.sharding import PartitionSpec as P

HD = 128
QH = 32
KVH = 4
ROWS = 128
FSDP = ("zx", "core")


drop_cut = 1677722
keep_scale = 1.0 / 0.9


def mixing(state):
    state = state ^ lax.shift_right_logical(state, jnp.full_like(state, 16))
    state = state * 2146121005
    state = state ^ lax.shift_right_logical(state, jnp.full_like(state, 15))
    state = state * 739982445
    state = state ^ lax.shift_right_logical(state, jnp.full_like(state, 16))
    return state


def attention_kernel(seeds_ref, offset_ref, pos_ref, q_ref, do_ref, k_ref, *refs, seq_len,
                     per_group, first):
    if first:
        (dv_ref,) = refs
    else:
        v_ref, dq_ref, dk_ref = refs
    g = pl.program_id(0)
    h = pl.program_id(1)
    head_seed = seeds_ref[g * per_group + h]
    inverse_root = 1.0 / math.sqrt(HD)
    last_dims = (((1,), (1,)), ((), ()))
    first_dims = (((0,), (0,)), ((), ()))
    acc_ref = dv_ref if first else dk_ref

    @pl.when(h == 0)
    def _():
        acc_ref[...] = jnp.zeros_like(acc_ref)

    q = q_ref[...]
    do = do_ref[...]
    k = k_ref[...]
    pos = pos_ref[...]
    rows_here = q.shape[0]
    scores = lax.dot_general(q, k, last_dims, preferred_element_type=jnp.float32) * inverse_root
    rows = lax.broadcasted_iota(jnp.int32, (rows_here, seq_len), 0) + offset_ref[0]
    cols = lax.broadcasted_iota(jnp.int32, (rows_here, seq_len), 1)
    visible = (cols <= rows) & (rows - cols <= pos)
    masked = jnp.where(visible, scores, -jnp.inf)
    row_max = jnp.max(masked, axis=1, keepdims=True)
    exp_terms = jnp.where(visible, jnp.exp(scores - row_max), 0.0)
    probs = exp_terms / jnp.sum(exp_terms, axis=1, keepdims=True)
    kept = (mixing(rows * seq_len + cols + head_seed) & 16777215) >= drop_cut
    if first:
        dropped = jnp.where(kept, probs * keep_scale, 0.0).astype(jnp.bfloat16)
        dv_ref[...] += lax.dot_general(dropped, do, first_dims, preferred_element_type=jnp.float32)
        return
    v = v_ref[...]
    raw = lax.dot_general(do, v, last_dims, preferred_element_type=jnp.float32)
    prob_grad = jnp.where(kept, raw * keep_scale, 0.0)
    row_delta = jnp.sum(probs * prob_grad, axis=1, keepdims=True)
    score_grad = (probs * (prob_grad - row_delta)).astype(jnp.bfloat16)
    dq = jnp.dot(score_grad, k, preferred_element_type=jnp.float32) * inverse_root
    dq_ref[...] = dq.astype(dq_ref.dtype)
    dk_ref[...] += (
        lax.dot_general(score_grad, q, first_dims, preferred_element_type=jnp.float32)
        * inverse_root
    )


def attention(seeds, offset, pos, queries, grads, keys, values):
    rows_here = queries.shape[0]
    seq_len = keys.shape[0]
    groups = keys.shape[1] // HD
    per_group = queries.shape[1] // HD // groups
    head_map = lambda g, h, s, o: (0, g * per_group + h)
    group_map = lambda g, h, s, o: (0, g)
    whole_map = lambda g, h, s, o: (0, 0)
    first = values is None
    kernel = functools.partial(
        attention_kernel, seq_len=seq_len, per_group=per_group, first=first
    )
    in_specs = [
        pl.BlockSpec((rows_here, 1), whole_map),
        pl.BlockSpec((rows_here, HD), head_map),
        pl.BlockSpec((rows_here, HD), head_map),
        pl.BlockSpec((seq_len, HD), group_map),
    ]
    operands = [seeds, offset, pos, queries, grads, keys]
    acc = jax.ShapeDtypeStruct(keys.shape, jnp.float32)
    if first:
        out_specs = [pl.BlockSpec((seq_len, HD), group_map)]
        out_shape = [acc]
    else:
        in_specs.append(pl.BlockSpec((seq_len, HD), group_map))
        operands.append(values)
        out_specs = [pl.BlockSpec((rows_here, HD), head_map), pl.BlockSpec((seq_len, HD), group_map)]
        out_shape = [jax.ShapeDtypeStruct(queries.shape, jnp.bfloat16), acc]
    return pl.pallas_call(
        kernel,
        grid_spec=pltpu.PrefetchScalarGridSpec(
            num_scalar_prefetch=2,
            grid=(groups, per_group),
            in_specs=in_specs,
            out_specs=out_specs,
        ),
        out_shape=out_shape,
        compiler_params=pltpu.CompilerParams(
            dimension_semantics=("arbitrary", "arbitrary"),
            vmem_limit_bytes=48 * 1024 * 1024,
        ),
    )(*operands)


def gather_seq(piece, seq_index, seq_devices):
    received = [piece]
    for shift in range(1, seq_devices):
        received.append(
            lax.ppermute(piece, "seq", [(i, (i + shift) % seq_devices) for i in range(seq_devices)])
        )
    order = (seq_index - jnp.arange(seq_devices, dtype=jnp.int32)) % seq_devices
    stacked = jnp.take(jnp.stack(received), order, axis=0)
    return stacked.reshape((seq_devices * piece.shape[0],) + piece.shape[1:])


def reduce_seq(partial, seq_index, seq_devices):
    blocks = partial.reshape((seq_devices, partial.shape[0] // seq_devices) + partial.shape[1:])
    summed = lax.dynamic_index_in_dim(blocks, seq_index, 0, keepdims=False)
    for shift in range(1, seq_devices):
        piece = lax.dynamic_index_in_dim(blocks, (seq_index + shift) % seq_devices, 0, keepdims=False)
        summed = summed + lax.ppermute(
            piece, "seq", [(i, (i + shift) % seq_devices) for i in range(seq_devices)]
        )
    return summed


def per_device(layer_input, queries, key_states, out_grad, doc_positions, drop_seed, value_weight):
    seq_devices = lax.axis_size("seq")
    zx_devices = lax.axis_size("zx")
    fsdp_devices = zx_devices * 2
    core_index = lax.axis_index("core")
    seq_index = lax.axis_index("seq")
    batch_index = lax.axis_index(FSDP)
    tok_rows = layer_input.shape[1]
    seq_len = tok_rows * seq_devices
    local_input = layer_input[0]
    block_rows = value_weight.shape[0]
    swap = [(0, 1), (1, 0)]
    weight_own = lax.all_gather(value_weight, ("seq", "zx"), axis=0, tiled=True)
    weight_other = lax.ppermute(weight_own, "core", swap)
    input_view = local_input.reshape(tok_rows, seq_devices * zx_devices, 2, block_rows)
    input_own = lax.dynamic_index_in_dim(input_view, core_index, 2, keepdims=False).reshape(
        tok_rows, -1
    )
    input_other = lax.dynamic_index_in_dim(input_view, 1 - core_index, 2, keepdims=False).reshape(
        tok_rows, -1
    )
    input_cols = lax.all_to_all(
        local_input.reshape(tok_rows, seq_devices, fsdp_devices, block_rows),
        FSDP,
        split_axis=2,
        concat_axis=0,
        tiled=True,
    ).reshape(zx_devices, 2, tok_rows, seq_devices * block_rows)
    base_seed = mixing(drop_seed + batch_index * 1000003)
    seeds = mixing(base_seed ^ jnp.arange(QH, dtype=jnp.int32) * 1640531527)
    offset = (seq_index * tok_rows).reshape(1).astype(jnp.int32)
    pos = lax.dynamic_slice_in_dim(doc_positions[0], seq_index * tok_rows, tok_rows)[:, None]
    query_loc, grad_loc = queries[0], out_grad[0]
    key_full = gather_seq(key_states[0], seq_index, seq_devices)
    (dv,) = attention(seeds, offset, pos, query_loc, grad_loc, key_full, None)
    dv, input_cols, weight_own = lax.optimization_barrier((dv, input_cols, weight_own))
    value_grad = reduce_seq(dv, seq_index, seq_devices).astype(jnp.bfloat16)
    grads_own = lax.all_to_all(
        jnp.broadcast_to(value_grad[None], (zx_devices,) + value_grad.shape),
        "zx",
        split_axis=0,
        concat_axis=0,
        tiled=True,
    ).reshape(zx_devices * tok_rows, KVH * HD)
    grads_other = lax.ppermute(grads_own, "core", swap)
    cols_own = lax.dynamic_index_in_dim(input_cols, core_index, 1, keepdims=False).reshape(
        zx_devices * tok_rows, -1
    )
    cols_other = lax.dynamic_index_in_dim(input_cols, 1 - core_index, 1, keepdims=False).reshape(
        zx_devices * tok_rows, -1
    )
    first_dims = (((0,), (0,)), ((), ()))
    partial = (
        lax.dot_general(cols_own, grads_own, first_dims, preferred_element_type=jnp.float32)
        + lax.dot_general(cols_other, grads_other, first_dims, preferred_element_type=jnp.float32)
    ).reshape(seq_devices, block_rows, KVH * HD)
    summed = lax.dynamic_index_in_dim(partial, seq_index, 0, keepdims=False)
    for shift in range(1, seq_devices):
        piece = lax.dynamic_index_in_dim(
            partial, (seq_index + shift) % seq_devices, 0, keepdims=False
        )
        summed = summed + lax.ppermute(
            piece, "seq", [(i, (i + shift) % seq_devices) for i in range(seq_devices)]
        )
    weight_grad = (summed * (1.0 / math.sqrt(fsdp_devices * seq_len))).astype(jnp.bfloat16)

    values_loc = (
        jnp.dot(input_own, weight_own, preferred_element_type=jnp.float32)
        + jnp.dot(input_other, weight_other, preferred_element_type=jnp.float32)
    ).astype(jnp.bfloat16)
    value_full = gather_seq(values_loc, seq_index, seq_devices)
    dq, dk = attention(seeds, offset, pos, query_loc, grad_loc, key_full, value_full)
    query_grad = dq
    key_grad = reduce_seq(dk, seq_index, seq_devices).astype(jnp.bfloat16)
    last_dims = (((1,), (1,)), ((), ()))
    grad_own = lax.dot_general(
        value_grad, weight_own, last_dims, preferred_element_type=jnp.float32
    ).astype(jnp.bfloat16).reshape(tok_rows, seq_devices * zx_devices, 1, block_rows)
    grad_other = lax.dot_general(
        value_grad, weight_other, last_dims, preferred_element_type=jnp.float32
    ).astype(jnp.bfloat16).reshape(tok_rows, seq_devices * zx_devices, 1, block_rows)
    input_grad = jnp.where(
        core_index == 0,
        jnp.concatenate([grad_own, grad_other], axis=2),
        jnp.concatenate([grad_other, grad_own], axis=2),
    ).reshape(tok_rows, -1)
    return (query_grad[None], key_grad[None], input_grad[None], weight_grad)


def solution(mesh):
    seq_devices, fsdp_devices = mesh.devices.shape
    chips = jax.sharding.Mesh(
        mesh.devices.reshape(seq_devices, fsdp_devices // 2, 2), ("seq",) + FSDP
    )
    return jax.shard_map(
        per_device,
        mesh=chips,
        in_specs=(
            P(FSDP, "seq", None),
            P(FSDP, "seq", None),
            P(FSDP, "seq", None),
            P(FSDP, "seq", None),
            P(FSDP, None),
            P(),
            P(("seq",) + FSDP, None),
        ),
        out_specs=(
            P(FSDP, "seq", None),
            P(FSDP, "seq", None),
            P(FSDP, "seq", None),
            P(("seq",) + FSDP, None),
        ),
        check_vma=False,
    )
```

```python
import functools
import math

import jax
import jax.numpy as jnp
from jax import lax
from jax.experimental import pallas as pl
from jax.experimental.pallas import tpu as pltpu
from jax.sharding import PartitionSpec as P

HD = 128
QH = 32
KVH = 4
ROWS = 128
FSDP = ("zx", "core")


drop_cut = 1677722
keep_scale = 1.0 / 0.9


def mixing(state):
    state = state ^ lax.shift_right_logical(state, jnp.full_like(state, 16))
    state = state * 2146121005
    state = state ^ lax.shift_right_logical(state, jnp.full_like(state, 15))
    state = state * 739982445
    state = state ^ lax.shift_right_logical(state, jnp.full_like(state, 16))
    return state


def attention_kernel(seeds_ref, offset_ref, pos_ref, q_ref, do_ref, k_ref, *refs, seq_len,
                     per_group, first):
    if first:
        (dv_ref,) = refs
    else:
        v_ref, dq_ref, dk_ref = refs
    g = pl.program_id(0)
    h = pl.program_id(1)
    head_seed = seeds_ref[g * per_group + h]
    inverse_root = 1.0 / math.sqrt(HD)
    last_dims = (((1,), (1,)), ((), ()))
    first_dims = (((0,), (0,)), ((), ()))
    acc_ref = dv_ref if first else dk_ref

    @pl.when(h == 0)
    def _():
        acc_ref[...] = jnp.zeros_like(acc_ref)

    q = q_ref[...]
    do = do_ref[...]
    k = k_ref[...]
    pos = pos_ref[...]
    rows_here = q.shape[0]
    scores = lax.dot_general(q, k, last_dims, preferred_element_type=jnp.float32) * inverse_root
    rows = lax.broadcasted_iota(jnp.int32, (rows_here, seq_len), 0) + offset_ref[0]
    cols = lax.broadcasted_iota(jnp.int32, (rows_here, seq_len), 1)
    visible = (cols <= rows) & (rows - cols <= pos)
    masked = jnp.where(visible, scores, -jnp.inf)
    row_max = jnp.max(masked, axis=1, keepdims=True)
    exp_terms = jnp.where(visible, jnp.exp(scores - row_max), 0.0)
    probs = exp_terms / jnp.sum(exp_terms, axis=1, keepdims=True)
    kept = (mixing(rows * seq_len + cols + head_seed) & 16777215) >= drop_cut
    if first:
        dropped = jnp.where(kept, probs * keep_scale, 0.0).astype(jnp.bfloat16)
        dv_ref[...] += lax.dot_general(dropped, do, first_dims, preferred_element_type=jnp.float32)
        return
    v = v_ref[...]
    raw = lax.dot_general(do, v, last_dims, preferred_element_type=jnp.float32)
    prob_grad = jnp.where(kept, raw * keep_scale, 0.0)
    row_delta = jnp.sum(probs * prob_grad, axis=1, keepdims=True)
    score_grad = (probs * (prob_grad - row_delta)).astype(jnp.bfloat16)
    dq = jnp.dot(score_grad, k, preferred_element_type=jnp.float32) * inverse_root
    dq_ref[...] = dq.astype(dq_ref.dtype)
    dk_ref[...] += (
        lax.dot_general(score_grad, q, first_dims, preferred_element_type=jnp.float32)
        * inverse_root
    )


def attention(seeds, offset, pos, queries, grads, keys, values):
    rows_here = queries.shape[0]
    seq_len = keys.shape[0]
    groups = keys.shape[1] // HD
    per_group = queries.shape[1] // HD // groups
    head_map = lambda g, h, s, o: (0, g * per_group + h)
    group_map = lambda g, h, s, o: (0, g)
    whole_map = lambda g, h, s, o: (0, 0)
    first = values is None
    kernel = functools.partial(
        attention_kernel, seq_len=seq_len, per_group=per_group, first=first
    )
    in_specs = [
        pl.BlockSpec((rows_here, 1), whole_map),
        pl.BlockSpec((rows_here, HD), head_map),
        pl.BlockSpec((rows_here, HD), head_map),
        pl.BlockSpec((seq_len, HD), group_map),
    ]
    operands = [seeds, offset, pos, queries, grads, keys]
    acc = jax.ShapeDtypeStruct(keys.shape, jnp.float32)
    if first:
        out_specs = [pl.BlockSpec((seq_len, HD), group_map)]
        out_shape = [acc]
    else:
        in_specs.append(pl.BlockSpec((seq_len, HD), group_map))
        operands.append(values)
        out_specs = [pl.BlockSpec((rows_here, HD), head_map), pl.BlockSpec((seq_len, HD), group_map)]
        out_shape = [jax.ShapeDtypeStruct(queries.shape, jnp.bfloat16), acc]
    return pl.pallas_call(
        kernel,
        grid_spec=pltpu.PrefetchScalarGridSpec(
            num_scalar_prefetch=2,
            grid=(groups, per_group),
            in_specs=in_specs,
            out_specs=out_specs,
        ),
        out_shape=out_shape,
        compiler_params=pltpu.CompilerParams(
            dimension_semantics=("arbitrary", "arbitrary"),
            vmem_limit_bytes=48 * 1024 * 1024,
        ),
    )(*operands)


def gather_seq(piece, seq_index, seq_devices):
    received = [piece]
    for shift in range(1, seq_devices):
        received.append(
            lax.ppermute(piece, "seq", [(i, (i + shift) % seq_devices) for i in range(seq_devices)])
        )
    order = (seq_index - jnp.arange(seq_devices, dtype=jnp.int32)) % seq_devices
    stacked = jnp.take(jnp.stack(received), order, axis=0)
    return stacked.reshape((seq_devices * piece.shape[0],) + piece.shape[1:])


def reduce_seq(partial, seq_index, seq_devices):
    blocks = partial.reshape((seq_devices, partial.shape[0] // seq_devices) + partial.shape[1:])
    summed = lax.dynamic_index_in_dim(blocks, seq_index, 0, keepdims=False)
    for shift in range(1, seq_devices):
        piece = lax.dynamic_index_in_dim(blocks, (seq_index + shift) % seq_devices, 0, keepdims=False)
        summed = summed + lax.ppermute(
            piece, "seq", [(i, (i + shift) % seq_devices) for i in range(seq_devices)]
        )
    return summed


def per_device(layer_input, queries, key_states, out_grad, doc_positions, drop_seed, value_weight):
    seq_devices = lax.axis_size("seq")
    zx_devices = lax.axis_size("zx")
    fsdp_devices = zx_devices * 2
    core_index = lax.axis_index("core")
    seq_index = lax.axis_index("seq")
    batch_index = lax.axis_index(FSDP)
    tok_rows = layer_input.shape[1]
    seq_len = tok_rows * seq_devices
    local_input = layer_input[0]
    block_rows = value_weight.shape[0]
    swap = [(0, 1), (1, 0)]
    weight_own = lax.all_gather(value_weight, ("seq", "zx"), axis=0, tiled=True)
    input_view = local_input.reshape(tok_rows, seq_devices * zx_devices, 2, block_rows)
    input_own = lax.dynamic_index_in_dim(input_view, core_index, 2, keepdims=False).reshape(
        tok_rows, -1
    )
    input_other = lax.dynamic_index_in_dim(input_view, 1 - core_index, 2, keepdims=False).reshape(
        tok_rows, -1
    )
    base_seed = mixing(drop_seed + batch_index * 1000003)
    seeds = mixing(base_seed ^ jnp.arange(QH, dtype=jnp.int32) * 1640531527)
    offset = (seq_index * tok_rows).reshape(1).astype(jnp.int32)
    pos = lax.dynamic_slice_in_dim(doc_positions[0], seq_index * tok_rows, tok_rows)[:, None]
    query_loc, grad_loc = queries[0], out_grad[0]
    key_full = gather_seq(key_states[0], seq_index, seq_devices)
    (dv,) = attention(seeds, offset, pos, query_loc, grad_loc, key_full, None)
    dv, weight_own, input_late = lax.optimization_barrier((dv, weight_own, local_input))
    weight_other = lax.ppermute(weight_own, "core", swap)
    input_cols = lax.all_to_all(
        input_late.reshape(tok_rows, seq_devices, fsdp_devices, block_rows),
        FSDP,
        split_axis=2,
        concat_axis=0,
        tiled=True,
    ).reshape(zx_devices, 2, tok_rows, seq_devices * block_rows)
    value_grad = reduce_seq(dv, seq_index, seq_devices).astype(jnp.bfloat16)
    grads_own = lax.all_gather(value_grad, "zx", axis=0, tiled=True)
    values_loc = (
        jnp.dot(input_own, weight_own, preferred_element_type=jnp.float32)
        + jnp.dot(input_other, weight_other, preferred_element_type=jnp.float32)
    ).astype(jnp.bfloat16)
    value_full = gather_seq(values_loc, seq_index, seq_devices)
    dq, dk = attention(seeds, offset, pos, query_loc, grad_loc, key_full, value_full)
    grads_own, input_cols, dq, dk = lax.optimization_barrier((grads_own, input_cols, dq, dk))
    query_grad = dq
    key_grad = reduce_seq(dk, seq_index, seq_devices).astype(jnp.bfloat16)
    grads_other = lax.ppermute(grads_own, "core", swap)
    cols_own = lax.dynamic_index_in_dim(input_cols, core_index, 1, keepdims=False).reshape(
        zx_devices * tok_rows, -1
    )
    cols_other = lax.dynamic_index_in_dim(input_cols, 1 - core_index, 1, keepdims=False).reshape(
        zx_devices * tok_rows, -1
    )
    first_dims = (((0,), (0,)), ((), ()))
    partial = (
        lax.dot_general(cols_own, grads_own, first_dims, preferred_element_type=jnp.float32)
        + lax.dot_general(cols_other, grads_other, first_dims, preferred_element_type=jnp.float32)
    ).reshape(seq_devices, block_rows, KVH * HD)
    summed = lax.dynamic_index_in_dim(partial, seq_index, 0, keepdims=False)
    for shift in range(1, seq_devices):
        piece = lax.dynamic_index_in_dim(
            partial, (seq_index + shift) % seq_devices, 0, keepdims=False
        )
        summed = summed + lax.ppermute(
            piece, "seq", [(i, (i + shift) % seq_devices) for i in range(seq_devices)]
        )
    weight_grad = (summed * (1.0 / math.sqrt(fsdp_devices * seq_len))).astype(jnp.bfloat16)

    last_dims = (((1,), (1,)), ((), ()))
    grad_own = lax.dot_general(
        value_grad, weight_own, last_dims, preferred_element_type=jnp.float32
    ).astype(jnp.bfloat16).reshape(tok_rows, seq_devices * zx_devices, 1, block_rows)
    grad_other = lax.dot_general(
        value_grad, weight_other, last_dims, preferred_element_type=jnp.float32
    ).astype(jnp.bfloat16).reshape(tok_rows, seq_devices * zx_devices, 1, block_rows)
    input_grad = jnp.where(
        core_index == 0,
        jnp.concatenate([grad_own, grad_other], axis=2),
        jnp.concatenate([grad_other, grad_own], axis=2),
    ).reshape(tok_rows, -1)
    return (query_grad[None], key_grad[None], input_grad[None], weight_grad)


def solution(mesh):
    seq_devices, fsdp_devices = mesh.devices.shape
    chips = jax.sharding.Mesh(
        mesh.devices.reshape(seq_devices, fsdp_devices // 2, 2), ("seq",) + FSDP
    )
    return jax.shard_map(
        per_device,
        mesh=chips,
        in_specs=(
            P(FSDP, "seq", None),
            P(FSDP, "seq", None),
            P(FSDP, "seq", None),
            P(FSDP, "seq", None),
            P(FSDP, None),
            P(),
            P(("seq",) + FSDP, None),
        ),
        out_specs=(
            P(FSDP, "seq", None),
            P(FSDP, "seq", None),
            P(FSDP, "seq", None),
            P(("seq",) + FSDP, None),
        ),
        check_vma=False,
    )
```

```python
import functools
import math

import jax
import jax.numpy as jnp
from jax import lax
from jax.experimental import pallas as pl
from jax.experimental.pallas import tpu as pltpu
from jax.sharding import PartitionSpec as P

HD = 128
QH = 32
KVH = 4
ROWS = 128
FSDP = ("zx", "core")


drop_cut = 1677722
keep_scale = 1.0 / 0.9


def mixing(state):
    state = state ^ lax.shift_right_logical(state, jnp.full_like(state, 16))
    state = state * 2146121005
    state = state ^ lax.shift_right_logical(state, jnp.full_like(state, 15))
    state = state * 739982445
    state = state ^ lax.shift_right_logical(state, jnp.full_like(state, 16))
    return state


def attention_kernel(seeds_ref, offset_ref, pos_ref, q_ref, do_ref, k_ref, *refs, seq_len,
                     per_group, first):
    if first:
        (dv_ref,) = refs
    else:
        v_ref, dq_ref, dk_ref = refs
    g = pl.program_id(0)
    h = pl.program_id(1)
    head_seed = seeds_ref[g * per_group + h]
    inverse_root = 1.0 / math.sqrt(HD)
    last_dims = (((1,), (1,)), ((), ()))
    first_dims = (((0,), (0,)), ((), ()))
    acc_ref = dv_ref if first else dk_ref

    @pl.when(h == 0)
    def _():
        acc_ref[...] = jnp.zeros_like(acc_ref)

    q = q_ref[...]
    do = do_ref[...]
    k = k_ref[...]
    pos = pos_ref[...]
    rows_here = q.shape[0]
    scores = lax.dot_general(q, k, last_dims, preferred_element_type=jnp.float32) * inverse_root
    rows = lax.broadcasted_iota(jnp.int32, (rows_here, seq_len), 0) + offset_ref[0]
    cols = lax.broadcasted_iota(jnp.int32, (rows_here, seq_len), 1)
    visible = (cols <= rows) & (rows - cols <= pos)
    masked = jnp.where(visible, scores, -jnp.inf)
    row_max = jnp.max(masked, axis=1, keepdims=True)
    exp_terms = jnp.where(visible, jnp.exp(scores - row_max), 0.0)
    probs = exp_terms / jnp.sum(exp_terms, axis=1, keepdims=True)
    kept = (mixing(rows * seq_len + cols + head_seed) & 16777215) >= drop_cut
    if first:
        dropped = jnp.where(kept, probs * keep_scale, 0.0).astype(jnp.bfloat16)
        dv_ref[...] += lax.dot_general(dropped, do, first_dims, preferred_element_type=jnp.float32)
        return
    v = v_ref[...]
    raw = lax.dot_general(do, v, last_dims, preferred_element_type=jnp.float32)
    prob_grad = jnp.where(kept, raw * keep_scale, 0.0)
    row_delta = jnp.sum(probs * prob_grad, axis=1, keepdims=True)
    score_grad = (probs * (prob_grad - row_delta)).astype(jnp.bfloat16)
    dq = jnp.dot(score_grad, k, preferred_element_type=jnp.float32) * inverse_root
    dq_ref[...] = dq.astype(dq_ref.dtype)
    dk_ref[...] += (
        lax.dot_general(score_grad, q, first_dims, preferred_element_type=jnp.float32)
        * inverse_root
    )


def attention(seeds, offset, pos, queries, grads, keys, values):
    rows_here = queries.shape[0]
    seq_len = keys.shape[0]
    groups = keys.shape[1] // HD
    per_group = queries.shape[1] // HD // groups
    head_map = lambda g, h, s, o: (0, g * per_group + h)
    group_map = lambda g, h, s, o: (0, g)
    whole_map = lambda g, h, s, o: (0, 0)
    first = values is None
    kernel = functools.partial(
        attention_kernel, seq_len=seq_len, per_group=per_group, first=first
    )
    in_specs = [
        pl.BlockSpec((rows_here, 1), whole_map),
        pl.BlockSpec((rows_here, HD), head_map),
        pl.BlockSpec((rows_here, HD), head_map),
        pl.BlockSpec((seq_len, HD), group_map),
    ]
    operands = [seeds, offset, pos, queries, grads, keys]
    acc = jax.ShapeDtypeStruct(keys.shape, jnp.float32)
    if first:
        out_specs = [pl.BlockSpec((seq_len, HD), group_map)]
        out_shape = [acc]
    else:
        in_specs.append(pl.BlockSpec((seq_len, HD), group_map))
        operands.append(values)
        out_specs = [pl.BlockSpec((rows_here, HD), head_map), pl.BlockSpec((seq_len, HD), group_map)]
        out_shape = [jax.ShapeDtypeStruct(queries.shape, jnp.bfloat16), acc]
    return pl.pallas_call(
        kernel,
        grid_spec=pltpu.PrefetchScalarGridSpec(
            num_scalar_prefetch=2,
            grid=(groups, per_group),
            in_specs=in_specs,
            out_specs=out_specs,
        ),
        out_shape=out_shape,
        compiler_params=pltpu.CompilerParams(
            dimension_semantics=("arbitrary", "arbitrary"),
            vmem_limit_bytes=48 * 1024 * 1024,
        ),
    )(*operands)


def gather_seq(piece, seq_index, seq_devices):
    received = [piece]
    for shift in range(1, seq_devices):
        received.append(
            lax.ppermute(piece, "seq", [(i, (i + shift) % seq_devices) for i in range(seq_devices)])
        )
    order = (seq_index - jnp.arange(seq_devices, dtype=jnp.int32)) % seq_devices
    stacked = jnp.take(jnp.stack(received), order, axis=0)
    return stacked.reshape((seq_devices * piece.shape[0],) + piece.shape[1:])


def reduce_seq(partial, seq_index, seq_devices):
    blocks = partial.reshape((seq_devices, partial.shape[0] // seq_devices) + partial.shape[1:])
    summed = lax.dynamic_index_in_dim(blocks, seq_index, 0, keepdims=False)
    for shift in range(1, seq_devices):
        piece = lax.dynamic_index_in_dim(blocks, (seq_index + shift) % seq_devices, 0, keepdims=False)
        summed = summed + lax.ppermute(
            piece, "seq", [(i, (i + shift) % seq_devices) for i in range(seq_devices)]
        )
    return summed


def per_device(layer_input, queries, key_states, out_grad, doc_positions, drop_seed, value_weight):
    seq_devices = lax.axis_size("seq")
    zx_devices = lax.axis_size("zx")
    fsdp_devices = zx_devices * 2
    core_index = lax.axis_index("core")
    seq_index = lax.axis_index("seq")
    batch_index = lax.axis_index(FSDP)
    tok_rows = layer_input.shape[1]
    seq_len = tok_rows * seq_devices
    local_input = layer_input[0]
    block_rows = value_weight.shape[0]
    swap = [(0, 1), (1, 0)]
    weight_own = lax.all_gather(value_weight, ("seq", "zx"), axis=0, tiled=True)
    input_view = local_input.reshape(tok_rows, seq_devices * zx_devices, 2, block_rows)
    input_own = lax.dynamic_index_in_dim(input_view, core_index, 2, keepdims=False).reshape(
        tok_rows, -1
    )
    input_other = lax.dynamic_index_in_dim(input_view, 1 - core_index, 2, keepdims=False).reshape(
        tok_rows, -1
    )
    base_seed = mixing(drop_seed + batch_index * 1000003)
    seeds = mixing(base_seed ^ jnp.arange(QH, dtype=jnp.int32) * 1640531527)
    offset = (seq_index * tok_rows).reshape(1).astype(jnp.int32)
    pos = lax.dynamic_slice_in_dim(doc_positions[0], seq_index * tok_rows, tok_rows)[:, None]
    query_loc, grad_loc = queries[0], out_grad[0]
    key_full = gather_seq(key_states[0], seq_index, seq_devices)
    (dv,) = attention(seeds, offset, pos, query_loc, grad_loc, key_full, None)
    value_grad = reduce_seq(dv, seq_index, seq_devices).astype(jnp.bfloat16)
    grads_own = lax.all_gather(value_grad, "zx", axis=0, tiled=True)
    value_grad, weight_own, input_late = lax.optimization_barrier(
        (value_grad, weight_own, local_input)
    )
    weight_other = lax.ppermute(weight_own, "core", swap)
    input_cols = lax.all_to_all(
        input_late.reshape(tok_rows, seq_devices, fsdp_devices, block_rows),
        FSDP,
        split_axis=2,
        concat_axis=0,
        tiled=True,
    ).reshape(zx_devices, 2, tok_rows, seq_devices * block_rows)
    values_loc = (
        jnp.dot(input_own, weight_own, preferred_element_type=jnp.float32)
        + jnp.dot(input_other, weight_other, preferred_element_type=jnp.float32)
    ).astype(jnp.bfloat16)
    last_dims = (((1,), (1,)), ((), ()))
    grad_own = lax.dot_general(
        value_grad, weight_own, last_dims, preferred_element_type=jnp.float32
    ).astype(jnp.bfloat16).reshape(tok_rows, seq_devices * zx_devices, 1, block_rows)
    grad_other = lax.dot_general(
        value_grad, weight_other, last_dims, preferred_element_type=jnp.float32
    ).astype(jnp.bfloat16).reshape(tok_rows, seq_devices * zx_devices, 1, block_rows)
    input_grad = jnp.where(
        core_index == 0,
        jnp.concatenate([grad_own, grad_other], axis=2),
        jnp.concatenate([grad_other, grad_own], axis=2),
    ).reshape(tok_rows, -1)
    value_full = gather_seq(values_loc, seq_index, seq_devices)
    input_grad, value_full = lax.optimization_barrier((input_grad, value_full))
    dq, dk = attention(seeds, offset, pos, query_loc, grad_loc, key_full, value_full)
    grads_own, input_cols, dq, dk = lax.optimization_barrier((grads_own, input_cols, dq, dk))
    query_grad = dq
    key_grad = reduce_seq(dk, seq_index, seq_devices).astype(jnp.bfloat16)
    grads_other = lax.ppermute(grads_own, "core", swap)
    cols_own = lax.dynamic_index_in_dim(input_cols, core_index, 1, keepdims=False).reshape(
        zx_devices * tok_rows, -1
    )
    cols_other = lax.dynamic_index_in_dim(input_cols, 1 - core_index, 1, keepdims=False).reshape(
        zx_devices * tok_rows, -1
    )
    first_dims = (((0,), (0,)), ((), ()))
    partial = (
        lax.dot_general(cols_own, grads_own, first_dims, preferred_element_type=jnp.float32)
        + lax.dot_general(cols_other, grads_other, first_dims, preferred_element_type=jnp.float32)
    ).reshape(seq_devices, block_rows, KVH * HD)
    summed = lax.dynamic_index_in_dim(partial, seq_index, 0, keepdims=False)
    for shift in range(1, seq_devices):
        piece = lax.dynamic_index_in_dim(
            partial, (seq_index + shift) % seq_devices, 0, keepdims=False
        )
        summed = summed + lax.ppermute(
            piece, "seq", [(i, (i + shift) % seq_devices) for i in range(seq_devices)]
        )
    weight_grad = (summed * (1.0 / math.sqrt(fsdp_devices * seq_len))).astype(jnp.bfloat16)

    return (query_grad[None], key_grad[None], input_grad[None], weight_grad)


def solution(mesh):
    seq_devices, fsdp_devices = mesh.devices.shape
    chips = jax.sharding.Mesh(
        mesh.devices.reshape(seq_devices, fsdp_devices // 2, 2), ("seq",) + FSDP
    )
    return jax.shard_map(
        per_device,
        mesh=chips,
        in_specs=(
            P(FSDP, "seq", None),
            P(FSDP, "seq", None),
            P(FSDP, "seq", None),
            P(FSDP, "seq", None),
            P(FSDP, None),
            P(),
            P(("seq",) + FSDP, None),
        ),
        out_specs=(
            P(FSDP, "seq", None),
            P(FSDP, "seq", None),
            P(FSDP, "seq", None),
            P(("seq",) + FSDP, None),
        ),
        check_vma=False,
    )
```

```python
import functools
import math

import jax
import jax.numpy as jnp
from jax import lax
from jax.experimental import pallas as pl
from jax.experimental.pallas import tpu as pltpu
from jax.sharding import PartitionSpec as P

HD = 128
QH = 32
KVH = 4
ROWS = 128
FSDP = ("zx", "core")


drop_cut = 1677722
keep_scale = 1.0 / 0.9


def mixing(state):
    state = state ^ lax.shift_right_logical(state, jnp.full_like(state, 16))
    state = state * 2146121005
    state = state ^ lax.shift_right_logical(state, jnp.full_like(state, 15))
    state = state * 739982445
    state = state ^ lax.shift_right_logical(state, jnp.full_like(state, 16))
    return state


def attention_kernel(seeds_ref, offset_ref, pos_ref, q_ref, do_ref, k_ref, *refs, seq_len,
                     per_group, first):
    if first:
        (dv_ref,) = refs
    else:
        v_ref, dq_ref, dk_ref = refs
    g = pl.program_id(0)
    h = pl.program_id(1)
    head_seed = seeds_ref[g * per_group + h]
    inverse_root = 1.0 / math.sqrt(HD)
    last_dims = (((1,), (1,)), ((), ()))
    first_dims = (((0,), (0,)), ((), ()))
    acc_ref = dv_ref if first else dk_ref

    @pl.when(h == 0)
    def _():
        acc_ref[...] = jnp.zeros_like(acc_ref)

    q = q_ref[...]
    do = do_ref[...]
    k = k_ref[...]
    pos = pos_ref[...]
    rows_here = q.shape[0]
    scores = lax.dot_general(q, k, last_dims, preferred_element_type=jnp.float32) * inverse_root
    rows = lax.broadcasted_iota(jnp.int32, (rows_here, seq_len), 0) + offset_ref[0]
    cols = lax.broadcasted_iota(jnp.int32, (rows_here, seq_len), 1)
    visible = (cols <= rows) & (rows - cols <= pos)
    masked = jnp.where(visible, scores, -jnp.inf)
    row_max = jnp.max(masked, axis=1, keepdims=True)
    exp_terms = jnp.where(visible, jnp.exp(scores - row_max), 0.0)
    probs = exp_terms / jnp.sum(exp_terms, axis=1, keepdims=True)
    kept = (mixing(rows * seq_len + cols + head_seed) & 16777215) >= drop_cut
    if first:
        dropped = jnp.where(kept, probs * keep_scale, 0.0).astype(jnp.bfloat16)
        dv_ref[...] += lax.dot_general(dropped, do, first_dims, preferred_element_type=jnp.float32)
        return
    v = v_ref[...]
    raw = lax.dot_general(do, v, last_dims, preferred_element_type=jnp.float32)
    prob_grad = jnp.where(kept, raw * keep_scale, 0.0)
    row_delta = jnp.sum(probs * prob_grad, axis=1, keepdims=True)
    score_grad = (probs * (prob_grad - row_delta)).astype(jnp.bfloat16)
    dq = jnp.dot(score_grad, k, preferred_element_type=jnp.float32) * inverse_root
    dq_ref[...] = dq.astype(dq_ref.dtype)
    dk_ref[...] += (
        lax.dot_general(score_grad, q, first_dims, preferred_element_type=jnp.float32)
        * inverse_root
    )


def attention(seeds, offset, pos, queries, grads, keys, values):
    rows_here = queries.shape[0]
    seq_len = keys.shape[0]
    groups = keys.shape[1] // HD
    per_group = queries.shape[1] // HD // groups
    head_map = lambda g, h, s, o: (0, g * per_group + h)
    group_map = lambda g, h, s, o: (0, g)
    whole_map = lambda g, h, s, o: (0, 0)
    first = values is None
    kernel = functools.partial(
        attention_kernel, seq_len=seq_len, per_group=per_group, first=first
    )
    in_specs = [
        pl.BlockSpec((rows_here, 1), whole_map),
        pl.BlockSpec((rows_here, HD), head_map),
        pl.BlockSpec((rows_here, HD), head_map),
        pl.BlockSpec((seq_len, HD), group_map),
    ]
    operands = [seeds, offset, pos, queries, grads, keys]
    acc = jax.ShapeDtypeStruct(keys.shape, jnp.float32)
    if first:
        out_specs = [pl.BlockSpec((seq_len, HD), group_map)]
        out_shape = [acc]
    else:
        in_specs.append(pl.BlockSpec((seq_len, HD), group_map))
        operands.append(values)
        out_specs = [pl.BlockSpec((rows_here, HD), head_map), pl.BlockSpec((seq_len, HD), group_map)]
        out_shape = [jax.ShapeDtypeStruct(queries.shape, jnp.bfloat16), acc]
    return pl.pallas_call(
        kernel,
        grid_spec=pltpu.PrefetchScalarGridSpec(
            num_scalar_prefetch=2,
            grid=(groups, per_group),
            in_specs=in_specs,
            out_specs=out_specs,
        ),
        out_shape=out_shape,
        compiler_params=pltpu.CompilerParams(
            dimension_semantics=("arbitrary", "arbitrary"),
            vmem_limit_bytes=48 * 1024 * 1024,
        ),
    )(*operands)


def gather_axis(piece, index, devices, axis):
    received = [piece]
    for shift in range(1, devices):
        received.append(
            lax.ppermute(piece, axis, [(i, (i + shift) % devices) for i in range(devices)])
        )
    order = (index - jnp.arange(devices, dtype=jnp.int32)) % devices
    stacked = jnp.take(jnp.stack(received), order, axis=0)
    return stacked.reshape((devices * piece.shape[0],) + piece.shape[1:])


def gather_seq(piece, seq_index, seq_devices):
    return gather_axis(piece, seq_index, seq_devices, "seq")


def reduce_seq(partial, seq_index, seq_devices):
    blocks = partial.reshape((seq_devices, partial.shape[0] // seq_devices) + partial.shape[1:])
    summed = lax.dynamic_index_in_dim(blocks, seq_index, 0, keepdims=False)
    for shift in range(1, seq_devices):
        piece = lax.dynamic_index_in_dim(blocks, (seq_index + shift) % seq_devices, 0, keepdims=False)
        summed = summed + lax.ppermute(
            piece, "seq", [(i, (i + shift) % seq_devices) for i in range(seq_devices)]
        )
    return summed


def per_device(layer_input, queries, key_states, out_grad, doc_positions, drop_seed, value_weight):
    seq_devices = lax.axis_size("seq")
    zx_devices = lax.axis_size("zx")
    fsdp_devices = zx_devices * 2
    core_index = lax.axis_index("core")
    seq_index = lax.axis_index("seq")
    batch_index = lax.axis_index(FSDP)
    tok_rows = layer_input.shape[1]
    seq_len = tok_rows * seq_devices
    local_input = layer_input[0]
    block_rows = value_weight.shape[0]
    swap = [(0, 1), (1, 0)]
    weight_own = lax.all_gather(value_weight, ("seq", "zx"), axis=0, tiled=True)
    input_view = local_input.reshape(tok_rows, seq_devices * zx_devices, 2, block_rows)
    input_own = lax.dynamic_index_in_dim(input_view, core_index, 2, keepdims=False).reshape(
        tok_rows, -1
    )
    input_other = lax.dynamic_index_in_dim(input_view, 1 - core_index, 2, keepdims=False).reshape(
        tok_rows, -1
    )
    base_seed = mixing(drop_seed + batch_index * 1000003)
    seeds = mixing(base_seed ^ jnp.arange(QH, dtype=jnp.int32) * 1640531527)
    offset = (seq_index * tok_rows).reshape(1).astype(jnp.int32)
    pos = lax.dynamic_slice_in_dim(doc_positions[0], seq_index * tok_rows, tok_rows)[:, None]
    query_loc, grad_loc = queries[0], out_grad[0]
    key_full = gather_seq(key_states[0], seq_index, seq_devices)
    (dv,) = attention(seeds, offset, pos, query_loc, grad_loc, key_full, None)
    value_grad = reduce_seq(dv, seq_index, seq_devices).astype(jnp.bfloat16)
    grads_own = gather_axis(value_grad, lax.axis_index("zx"), zx_devices, "zx")
    value_grad, weight_own, input_late = lax.optimization_barrier(
        (value_grad, weight_own, local_input)
    )
    weight_other = lax.ppermute(weight_own, "core", swap)
    input_cols = lax.all_to_all(
        input_late.reshape(tok_rows, seq_devices, fsdp_devices, block_rows),
        FSDP,
        split_axis=2,
        concat_axis=0,
        tiled=True,
    ).reshape(zx_devices, 2, tok_rows, seq_devices * block_rows)
    values_loc = (
        jnp.dot(input_own, weight_own, preferred_element_type=jnp.float32)
        + jnp.dot(input_other, weight_other, preferred_element_type=jnp.float32)
    ).astype(jnp.bfloat16)
    last_dims = (((1,), (1,)), ((), ()))
    grad_own = lax.dot_general(
        value_grad, weight_own, last_dims, preferred_element_type=jnp.float32
    ).astype(jnp.bfloat16).reshape(tok_rows, seq_devices * zx_devices, 1, block_rows)
    grad_other = lax.dot_general(
        value_grad, weight_other, last_dims, preferred_element_type=jnp.float32
    ).astype(jnp.bfloat16).reshape(tok_rows, seq_devices * zx_devices, 1, block_rows)
    input_grad = jnp.where(
        core_index == 0,
        jnp.concatenate([grad_own, grad_other], axis=2),
        jnp.concatenate([grad_other, grad_own], axis=2),
    ).reshape(tok_rows, -1)
    value_full = gather_seq(values_loc, seq_index, seq_devices)
    input_grad, value_full = lax.optimization_barrier((input_grad, value_full))
    dq, dk = attention(seeds, offset, pos, query_loc, grad_loc, key_full, value_full)
    grads_own, input_cols, dq = lax.optimization_barrier((grads_own, input_cols, dq))
    query_grad = dq
    key_grad = reduce_seq(dk, seq_index, seq_devices).astype(jnp.bfloat16)
    grads_other = lax.ppermute(grads_own, "core", swap)
    cols_own = lax.dynamic_index_in_dim(input_cols, core_index, 1, keepdims=False).reshape(
        zx_devices * tok_rows, -1
    )
    cols_other = lax.dynamic_index_in_dim(input_cols, 1 - core_index, 1, keepdims=False).reshape(
        zx_devices * tok_rows, -1
    )
    first_dims = (((0,), (0,)), ((), ()))
    partial = (
        lax.dot_general(cols_own, grads_own, first_dims, preferred_element_type=jnp.float32)
        + lax.dot_general(cols_other, grads_other, first_dims, preferred_element_type=jnp.float32)
    ).reshape(seq_devices, block_rows, KVH * HD)
    summed = lax.dynamic_index_in_dim(partial, seq_index, 0, keepdims=False)
    for shift in range(1, seq_devices):
        piece = lax.dynamic_index_in_dim(
            partial, (seq_index + shift) % seq_devices, 0, keepdims=False
        )
        summed = summed + lax.ppermute(
            piece, "seq", [(i, (i + shift) % seq_devices) for i in range(seq_devices)]
        )
    weight_grad = (summed * (1.0 / math.sqrt(fsdp_devices * seq_len))).astype(jnp.bfloat16)

    return (query_grad[None], key_grad[None], input_grad[None], weight_grad)


def solution(mesh):
    seq_devices, fsdp_devices = mesh.devices.shape
    chips = jax.sharding.Mesh(
        mesh.devices.reshape(seq_devices, fsdp_devices // 2, 2), ("seq",) + FSDP
    )
    return jax.shard_map(
        per_device,
        mesh=chips,
        in_specs=(
            P(FSDP, "seq", None),
            P(FSDP, "seq", None),
            P(FSDP, "seq", None),
            P(FSDP, "seq", None),
            P(FSDP, None),
            P(),
            P(("seq",) + FSDP, None),
        ),
        out_specs=(
            P(FSDP, "seq", None),
            P(FSDP, "seq", None),
            P(FSDP, "seq", None),
            P(("seq",) + FSDP, None),
        ),
        check_vma=False,
    )
```

```python
import functools
import math

import jax
import jax.numpy as jnp
from jax import lax
from jax.experimental import pallas as pl
from jax.experimental.pallas import tpu as pltpu
from jax.sharding import PartitionSpec as P

HD = 128
QH = 32
KVH = 4
ROWS = 128
FSDP = ("zx", "core")


drop_cut = 1677722
keep_scale = 1.0 / 0.9


def mixing(state):
    state = state ^ lax.shift_right_logical(state, jnp.full_like(state, 16))
    state = state * 2146121005
    state = state ^ lax.shift_right_logical(state, jnp.full_like(state, 15))
    state = state * 739982445
    state = state ^ lax.shift_right_logical(state, jnp.full_like(state, 16))
    return state


def attention_kernel(seeds_ref, offset_ref, pos_ref, q_ref, do_ref, k_ref, *refs, seq_len,
                     per_group, first):
    if first:
        (dv_ref,) = refs
    else:
        v_ref, dq_ref, dk_ref = refs
    g = pl.program_id(0)
    h = pl.program_id(1)
    head_seed = seeds_ref[g * per_group + h]
    inverse_root = 1.0 / math.sqrt(HD)
    last_dims = (((1,), (1,)), ((), ()))
    first_dims = (((0,), (0,)), ((), ()))
    acc_ref = dv_ref if first else dk_ref

    @pl.when(h == 0)
    def _():
        acc_ref[...] = jnp.zeros_like(acc_ref)

    q = q_ref[...]
    do = do_ref[...]
    k = k_ref[...]
    pos = pos_ref[...]
    rows_here = q.shape[0]
    scores = lax.dot_general(q, k, last_dims, preferred_element_type=jnp.float32) * inverse_root
    rows = lax.broadcasted_iota(jnp.int32, (rows_here, seq_len), 0) + offset_ref[0]
    cols = lax.broadcasted_iota(jnp.int32, (rows_here, seq_len), 1)
    visible = (cols <= rows) & (rows - cols <= pos)
    masked = jnp.where(visible, scores, -jnp.inf)
    row_max = jnp.max(masked, axis=1, keepdims=True)
    exp_terms = jnp.where(visible, jnp.exp(scores - row_max), 0.0)
    probs = exp_terms / jnp.sum(exp_terms, axis=1, keepdims=True)
    kept = (mixing(rows * seq_len + cols + head_seed) & 16777215) >= drop_cut
    if first:
        dropped = jnp.where(kept, probs * keep_scale, 0.0).astype(jnp.bfloat16)
        dv_ref[...] += lax.dot_general(dropped, do, first_dims, preferred_element_type=jnp.float32)
        return
    v = v_ref[...]
    raw = lax.dot_general(do, v, last_dims, preferred_element_type=jnp.float32)
    prob_grad = jnp.where(kept, raw * keep_scale, 0.0)
    row_delta = jnp.sum(probs * prob_grad, axis=1, keepdims=True)
    score_grad = (probs * (prob_grad - row_delta)).astype(jnp.bfloat16)
    dq = jnp.dot(score_grad, k, preferred_element_type=jnp.float32) * inverse_root
    dq_ref[...] = dq.astype(dq_ref.dtype)
    dk_ref[...] += (
        lax.dot_general(score_grad, q, first_dims, preferred_element_type=jnp.float32)
        * inverse_root
    )


def attention(seeds, offset, pos, queries, grads, keys, values):
    rows_here = queries.shape[0]
    seq_len = keys.shape[0]
    groups = keys.shape[1] // HD
    per_group = queries.shape[1] // HD // groups
    head_map = lambda g, h, s, o: (0, g * per_group + h)
    group_map = lambda g, h, s, o: (0, g)
    whole_map = lambda g, h, s, o: (0, 0)
    first = values is None
    kernel = functools.partial(
        attention_kernel, seq_len=seq_len, per_group=per_group, first=first
    )
    in_specs = [
        pl.BlockSpec((rows_here, 1), whole_map),
        pl.BlockSpec((rows_here, HD), head_map),
        pl.BlockSpec((rows_here, HD), head_map),
        pl.BlockSpec((seq_len, HD), group_map),
    ]
    operands = [seeds, offset, pos, queries, grads, keys]
    acc = jax.ShapeDtypeStruct(keys.shape, jnp.float32)
    if first:
        out_specs = [pl.BlockSpec((seq_len, HD), group_map)]
        out_shape = [acc]
    else:
        in_specs.append(pl.BlockSpec((seq_len, HD), group_map))
        operands.append(values)
        out_specs = [pl.BlockSpec((rows_here, HD), head_map), pl.BlockSpec((seq_len, HD), group_map)]
        out_shape = [jax.ShapeDtypeStruct(queries.shape, jnp.bfloat16), acc]
    return pl.pallas_call(
        kernel,
        grid_spec=pltpu.PrefetchScalarGridSpec(
            num_scalar_prefetch=2,
            grid=(groups, per_group),
            in_specs=in_specs,
            out_specs=out_specs,
        ),
        out_shape=out_shape,
        compiler_params=pltpu.CompilerParams(
            dimension_semantics=("arbitrary", "arbitrary"),
            vmem_limit_bytes=48 * 1024 * 1024,
        ),
    )(*operands)


def gather_seq(piece, seq_index, seq_devices):
    received = [piece]
    for shift in range(1, seq_devices):
        received.append(
            lax.ppermute(piece, "seq", [(i, (i + shift) % seq_devices) for i in range(seq_devices)])
        )
    order = (seq_index - jnp.arange(seq_devices, dtype=jnp.int32)) % seq_devices
    stacked = jnp.take(jnp.stack(received), order, axis=0)
    return stacked.reshape((seq_devices * piece.shape[0],) + piece.shape[1:])


def reduce_seq(partial, seq_index, seq_devices):
    blocks = partial.reshape((seq_devices, partial.shape[0] // seq_devices) + partial.shape[1:])
    summed = lax.dynamic_index_in_dim(blocks, seq_index, 0, keepdims=False)
    for shift in range(1, seq_devices):
        piece = lax.dynamic_index_in_dim(blocks, (seq_index + shift) % seq_devices, 0, keepdims=False)
        summed = summed + lax.ppermute(
            piece, "seq", [(i, (i + shift) % seq_devices) for i in range(seq_devices)]
        )
    return summed


def per_device(layer_input, queries, key_states, out_grad, doc_positions, drop_seed, value_weight):
    seq_devices = lax.axis_size("seq")
    zx_devices = lax.axis_size("zx")
    fsdp_devices = zx_devices * 2
    core_index = lax.axis_index("core")
    seq_index = lax.axis_index("seq")
    batch_index = lax.axis_index(FSDP)
    tok_rows = layer_input.shape[1]
    seq_len = tok_rows * seq_devices
    local_input = layer_input[0]
    block_rows = value_weight.shape[0]
    swap = [(0, 1), (1, 0)]
    weight_own = lax.all_gather(value_weight, ("seq", "zx"), axis=0, tiled=True)
    input_view = local_input.reshape(tok_rows, seq_devices * zx_devices, 2, block_rows)
    input_own = lax.dynamic_index_in_dim(input_view, core_index, 2, keepdims=False).reshape(
        tok_rows, -1
    )
    input_other = lax.dynamic_index_in_dim(input_view, 1 - core_index, 2, keepdims=False).reshape(
        tok_rows, -1
    )
    base_seed = mixing(drop_seed + batch_index * 1000003)
    seeds = mixing(base_seed ^ jnp.arange(QH, dtype=jnp.int32) * 1640531527)
    offset = (seq_index * tok_rows).reshape(1).astype(jnp.int32)
    pos = lax.dynamic_slice_in_dim(doc_positions[0], seq_index * tok_rows, tok_rows)[:, None]
    query_loc, grad_loc = queries[0], out_grad[0]
    key_full = gather_seq(key_states[0], seq_index, seq_devices)
    (dv,) = attention(seeds, offset, pos, query_loc, grad_loc, key_full, None)
    value_grad = reduce_seq(dv, seq_index, seq_devices).astype(jnp.bfloat16)
    grads_own = lax.all_gather(value_grad, "zx", axis=0, tiled=True)
    value_grad, weight_own, input_late = lax.optimization_barrier(
        (value_grad, weight_own, local_input)
    )
    weight_other = lax.ppermute(weight_own, "core", swap)
    input_cols = lax.all_to_all(
        input_late.reshape(tok_rows, seq_devices, fsdp_devices, block_rows),
        FSDP,
        split_axis=2,
        concat_axis=0,
        tiled=True,
    ).reshape(zx_devices, 2, tok_rows, seq_devices * block_rows)
    values_loc = (
        jnp.dot(input_own, weight_own, preferred_element_type=jnp.float32)
        + jnp.dot(input_other, weight_other, preferred_element_type=jnp.float32)
    ).astype(jnp.bfloat16)
    last_dims = (((1,), (1,)), ((), ()))
    grad_own = lax.dot_general(
        value_grad, weight_own, last_dims, preferred_element_type=jnp.float32
    ).astype(jnp.bfloat16).reshape(tok_rows, seq_devices * zx_devices, 1, block_rows)
    grad_other = lax.dot_general(
        value_grad, weight_other, last_dims, preferred_element_type=jnp.float32
    ).astype(jnp.bfloat16).reshape(tok_rows, seq_devices * zx_devices, 1, block_rows)
    input_grad = jnp.where(
        core_index == 0,
        jnp.concatenate([grad_own, grad_other], axis=2),
        jnp.concatenate([grad_other, grad_own], axis=2),
    ).reshape(tok_rows, -1)
    value_full = gather_seq(values_loc, seq_index, seq_devices)
    input_grad, value_full = lax.optimization_barrier((input_grad, value_full))
    dq, dk = attention(seeds, offset, pos, query_loc, grad_loc, key_full, value_full)
    key_grad = reduce_seq(dk, seq_index, seq_devices).astype(jnp.bfloat16)
    grads_own, input_cols, dq, key_grad = lax.optimization_barrier(
        (grads_own, input_cols, dq, key_grad)
    )
    query_grad = dq
    grads_other = lax.ppermute(grads_own, "core", swap)
    cols_own = lax.dynamic_index_in_dim(input_cols, core_index, 1, keepdims=False).reshape(
        zx_devices * tok_rows, -1
    )
    cols_other = lax.dynamic_index_in_dim(input_cols, 1 - core_index, 1, keepdims=False).reshape(
        zx_devices * tok_rows, -1
    )
    first_dims = (((0,), (0,)), ((), ()))
    partial = (
        lax.dot_general(cols_own, grads_own, first_dims, preferred_element_type=jnp.float32)
        + lax.dot_general(cols_other, grads_other, first_dims, preferred_element_type=jnp.float32)
    ).reshape(seq_devices, block_rows, KVH * HD)
    summed = lax.dynamic_index_in_dim(partial, seq_index, 0, keepdims=False)
    for shift in range(1, seq_devices):
        piece = lax.dynamic_index_in_dim(
            partial, (seq_index + shift) % seq_devices, 0, keepdims=False
        )
        summed = summed + lax.ppermute(
            piece, "seq", [(i, (i + shift) % seq_devices) for i in range(seq_devices)]
        )
    weight_grad = (summed * (1.0 / math.sqrt(fsdp_devices * seq_len))).astype(jnp.bfloat16)

    return (query_grad[None], key_grad[None], input_grad[None], weight_grad)


def solution(mesh):
    seq_devices, fsdp_devices = mesh.devices.shape
    chips = jax.sharding.Mesh(
        mesh.devices.reshape(seq_devices, fsdp_devices // 2, 2), ("seq",) + FSDP
    )
    return jax.shard_map(
        per_device,
        mesh=chips,
        in_specs=(
            P(FSDP, "seq", None),
            P(FSDP, "seq", None),
            P(FSDP, "seq", None),
            P(FSDP, "seq", None),
            P(FSDP, None),
            P(),
            P(("seq",) + FSDP, None),
        ),
        out_specs=(
            P(FSDP, "seq", None),
            P(FSDP, "seq", None),
            P(FSDP, "seq", None),
            P(("seq",) + FSDP, None),
        ),
        check_vma=False,
    )
```

```python
import functools
import math

import jax
import jax.numpy as jnp
from jax import lax
from jax.experimental import pallas as pl
from jax.experimental.pallas import tpu as pltpu
from jax.sharding import PartitionSpec as P

HD = 128
QH = 32
KVH = 4
ROWS = 128
FSDP = ("zx", "core")


drop_cut = 1677722
keep_scale = 1.0 / 0.9


def mixing(state):
    state = state ^ lax.shift_right_logical(state, jnp.full_like(state, 16))
    state = state * 2146121005
    state = state ^ lax.shift_right_logical(state, jnp.full_like(state, 15))
    state = state * 739982445
    state = state ^ lax.shift_right_logical(state, jnp.full_like(state, 16))
    return state


def attention_kernel(seeds_ref, offset_ref, pos_ref, q_ref, do_ref, k_ref, *refs, seq_len,
                     per_group, first):
    if first:
        (dv_ref,) = refs
    else:
        v_ref, dq_ref, dk_ref = refs
    g = pl.program_id(0)
    h = pl.program_id(1)
    head_seed = seeds_ref[g * per_group + h]
    inverse_root = 1.0 / math.sqrt(HD)
    last_dims = (((1,), (1,)), ((), ()))
    first_dims = (((0,), (0,)), ((), ()))
    acc_ref = dv_ref if first else dk_ref

    @pl.when(h == 0)
    def _():
        acc_ref[...] = jnp.zeros_like(acc_ref)

    q = q_ref[...]
    do = do_ref[...]
    k = k_ref[...]
    pos = pos_ref[...]
    rows_here = q.shape[0]
    scores = lax.dot_general(q, k, last_dims, preferred_element_type=jnp.float32) * inverse_root
    rows = lax.broadcasted_iota(jnp.int32, (rows_here, seq_len), 0) + offset_ref[0]
    cols = lax.broadcasted_iota(jnp.int32, (rows_here, seq_len), 1)
    visible = (cols <= rows) & (rows - cols <= pos)
    masked = jnp.where(visible, scores, -jnp.inf)
    row_max = jnp.max(masked, axis=1, keepdims=True)
    exp_terms = jnp.where(visible, jnp.exp(scores - row_max), 0.0)
    probs = exp_terms / jnp.sum(exp_terms, axis=1, keepdims=True)
    kept = (mixing(rows * seq_len + cols + head_seed) & 16777215) >= drop_cut
    if first:
        dropped = jnp.where(kept, probs * keep_scale, 0.0).astype(jnp.bfloat16)
        dv_ref[...] += lax.dot_general(dropped, do, first_dims, preferred_element_type=jnp.float32)
        return
    v = v_ref[...]
    raw = lax.dot_general(do, v, last_dims, preferred_element_type=jnp.float32)
    prob_grad = jnp.where(kept, raw * keep_scale, 0.0)
    row_delta = jnp.sum(probs * prob_grad, axis=1, keepdims=True)
    score_grad = (probs * (prob_grad - row_delta)).astype(jnp.bfloat16)
    dq = jnp.dot(score_grad, k, preferred_element_type=jnp.float32) * inverse_root
    dq_ref[...] = dq.astype(dq_ref.dtype)
    dk_ref[...] += (
        lax.dot_general(score_grad, q, first_dims, preferred_element_type=jnp.float32)
        * inverse_root
    )


def attention(seeds, offset, pos, queries, grads, keys, values):
    rows_here = queries.shape[0]
    seq_len = keys.shape[0]
    groups = keys.shape[1] // HD
    per_group = queries.shape[1] // HD // groups
    head_map = lambda g, h, s, o: (0, g * per_group + h)
    group_map = lambda g, h, s, o: (0, g)
    whole_map = lambda g, h, s, o: (0, 0)
    first = values is None
    kernel = functools.partial(
        attention_kernel, seq_len=seq_len, per_group=per_group, first=first
    )
    in_specs = [
        pl.BlockSpec((rows_here, 1), whole_map),
        pl.BlockSpec((rows_here, HD), head_map),
        pl.BlockSpec((rows_here, HD), head_map),
        pl.BlockSpec((seq_len, HD), group_map),
    ]
    operands = [seeds, offset, pos, queries, grads, keys]
    acc = jax.ShapeDtypeStruct(keys.shape, jnp.float32)
    if first:
        out_specs = [pl.BlockSpec((seq_len, HD), group_map)]
        out_shape = [acc]
    else:
        in_specs.append(pl.BlockSpec((seq_len, HD), group_map))
        operands.append(values)
        out_specs = [pl.BlockSpec((rows_here, HD), head_map), pl.BlockSpec((seq_len, HD), group_map)]
        out_shape = [jax.ShapeDtypeStruct(queries.shape, jnp.bfloat16), acc]
    return pl.pallas_call(
        kernel,
        grid_spec=pltpu.PrefetchScalarGridSpec(
            num_scalar_prefetch=2,
            grid=(groups, per_group),
            in_specs=in_specs,
            out_specs=out_specs,
        ),
        out_shape=out_shape,
        compiler_params=pltpu.CompilerParams(
            dimension_semantics=("arbitrary", "arbitrary"),
            vmem_limit_bytes=48 * 1024 * 1024,
        ),
    )(*operands)


def gather_seq(piece, seq_index, seq_devices):
    received = [piece]
    for shift in range(1, seq_devices):
        received.append(
            lax.ppermute(piece, "seq", [(i, (i + shift) % seq_devices) for i in range(seq_devices)])
        )
    order = (seq_index - jnp.arange(seq_devices, dtype=jnp.int32)) % seq_devices
    stacked = jnp.take(jnp.stack(received), order, axis=0)
    return stacked.reshape((seq_devices * piece.shape[0],) + piece.shape[1:])


def reduce_seq(partial, seq_index, seq_devices):
    blocks = partial.reshape((seq_devices, partial.shape[0] // seq_devices) + partial.shape[1:])
    summed = lax.dynamic_index_in_dim(blocks, seq_index, 0, keepdims=False)
    for shift in range(1, seq_devices):
        piece = lax.dynamic_index_in_dim(blocks, (seq_index + shift) % seq_devices, 0, keepdims=False)
        summed = summed + lax.ppermute(
            piece, "seq", [(i, (i + shift) % seq_devices) for i in range(seq_devices)]
        )
    return summed


def per_device(layer_input, queries, key_states, out_grad, doc_positions, drop_seed, value_weight):
    seq_devices = lax.axis_size("seq")
    zx_devices = lax.axis_size("zx")
    fsdp_devices = zx_devices * 2
    core_index = lax.axis_index("core")
    seq_index = lax.axis_index("seq")
    batch_index = lax.axis_index(FSDP)
    tok_rows = layer_input.shape[1]
    seq_len = tok_rows * seq_devices
    local_input = layer_input[0]
    block_rows = value_weight.shape[0]
    swap = [(0, 1), (1, 0)]
    weight_own = lax.all_gather(value_weight, ("seq", "zx"), axis=0, tiled=True)
    input_view = local_input.reshape(tok_rows, seq_devices * zx_devices, 2, block_rows)
    input_own = lax.dynamic_index_in_dim(input_view, core_index, 2, keepdims=False).reshape(
        tok_rows, -1
    )
    input_other = lax.dynamic_index_in_dim(input_view, 1 - core_index, 2, keepdims=False).reshape(
        tok_rows, -1
    )
    base_seed = mixing(drop_seed + batch_index * 1000003)
    seeds = mixing(base_seed ^ jnp.arange(QH, dtype=jnp.int32) * 1640531527)
    offset = (seq_index * tok_rows).reshape(1).astype(jnp.int32)
    pos = lax.dynamic_slice_in_dim(doc_positions[0], seq_index * tok_rows, tok_rows)[:, None]
    query_loc, grad_loc = queries[0], out_grad[0]
    key_full = gather_seq(key_states[0], seq_index, seq_devices)
    (dv,) = attention(seeds, offset, pos, query_loc, grad_loc, key_full, None)
    value_grad = reduce_seq(dv, seq_index, seq_devices).astype(jnp.bfloat16)
    grads_pair = gather_seq(value_grad, seq_index, seq_devices)
    grads_own = lax.all_gather(grads_pair, "zx", axis=0, tiled=True).reshape(
        zx_devices, seq_devices, tok_rows, KVH * HD
    )
    value_grad, weight_own, input_late = lax.optimization_barrier(
        (value_grad, weight_own, local_input)
    )
    weight_other = lax.ppermute(weight_own, "core", swap)
    input_cols = lax.all_to_all(
        input_late.reshape(tok_rows, seq_devices * fsdp_devices, block_rows),
        ("seq",) + FSDP,
        split_axis=1,
        concat_axis=0,
        tiled=True,
    ).reshape(seq_devices, zx_devices, 2, tok_rows, block_rows)
    values_loc = (
        jnp.dot(input_own, weight_own, preferred_element_type=jnp.float32)
        + jnp.dot(input_other, weight_other, preferred_element_type=jnp.float32)
    ).astype(jnp.bfloat16)
    last_dims = (((1,), (1,)), ((), ()))
    grad_own = lax.dot_general(
        value_grad, weight_own, last_dims, preferred_element_type=jnp.float32
    ).astype(jnp.bfloat16).reshape(tok_rows, seq_devices * zx_devices, 1, block_rows)
    grad_other = lax.dot_general(
        value_grad, weight_other, last_dims, preferred_element_type=jnp.float32
    ).astype(jnp.bfloat16).reshape(tok_rows, seq_devices * zx_devices, 1, block_rows)
    input_grad = jnp.where(
        core_index == 0,
        jnp.concatenate([grad_own, grad_other], axis=2),
        jnp.concatenate([grad_other, grad_own], axis=2),
    ).reshape(tok_rows, -1)
    value_full = gather_seq(values_loc, seq_index, seq_devices)
    input_grad, value_full = lax.optimization_barrier((input_grad, value_full))
    dq, dk = attention(seeds, offset, pos, query_loc, grad_loc, key_full, value_full)
    key_grad = reduce_seq(dk, seq_index, seq_devices).astype(jnp.bfloat16)
    grads_own, input_cols, dq, key_grad = lax.optimization_barrier(
        (grads_own, input_cols, dq, key_grad)
    )
    query_grad = dq
    grads_other = lax.ppermute(grads_own, "core", swap)
    cols_own = lax.dynamic_index_in_dim(input_cols, core_index, 2, keepdims=False)
    cols_other = lax.dynamic_index_in_dim(input_cols, 1 - core_index, 2, keepdims=False)
    token_dims = (((0, 1, 2), (1, 0, 2)), ((), ()))
    summed = lax.dot_general(
        cols_own, grads_own, token_dims, preferred_element_type=jnp.float32
    ) + lax.dot_general(cols_other, grads_other, token_dims, preferred_element_type=jnp.float32)
    weight_grad = (summed * (1.0 / math.sqrt(fsdp_devices * seq_len))).astype(jnp.bfloat16)

    return (query_grad[None], key_grad[None], input_grad[None], weight_grad)


def solution(mesh):
    seq_devices, fsdp_devices = mesh.devices.shape
    chips = jax.sharding.Mesh(
        mesh.devices.reshape(seq_devices, fsdp_devices // 2, 2), ("seq",) + FSDP
    )
    return jax.shard_map(
        per_device,
        mesh=chips,
        in_specs=(
            P(FSDP, "seq", None),
            P(FSDP, "seq", None),
            P(FSDP, "seq", None),
            P(FSDP, "seq", None),
            P(FSDP, None),
            P(),
            P(("seq",) + FSDP, None),
        ),
        out_specs=(
            P(FSDP, "seq", None),
            P(FSDP, "seq", None),
            P(FSDP, "seq", None),
            P(("seq",) + FSDP, None),
        ),
        check_vma=False,
    )
```

```python
import functools
import math

import jax
import jax.numpy as jnp
from jax import lax
from jax.experimental import pallas as pl
from jax.experimental.pallas import tpu as pltpu
from jax.sharding import PartitionSpec as P

HD = 128
QH = 32
KVH = 4
ROWS = 128
FSDP = ("zx", "core")


drop_cut = 1677722
keep_scale = 1.0 / 0.9


def mixing(state):
    state = state ^ lax.shift_right_logical(state, jnp.full_like(state, 16))
    state = state * 2146121005
    state = state ^ lax.shift_right_logical(state, jnp.full_like(state, 15))
    state = state * 739982445
    state = state ^ lax.shift_right_logical(state, jnp.full_like(state, 16))
    return state


def attention_kernel(seeds_ref, offset_ref, pos_ref, q_ref, do_ref, k_ref, *refs, seq_len,
                     per_group, first):
    if first:
        (dv_ref,) = refs
    else:
        v_ref, dq_ref, dk_ref = refs
    g = pl.program_id(0)
    h = pl.program_id(1)
    head_seed = seeds_ref[g * per_group + h]
    inverse_root = 1.0 / math.sqrt(HD)
    last_dims = (((1,), (1,)), ((), ()))
    first_dims = (((0,), (0,)), ((), ()))
    acc_ref = dv_ref if first else dk_ref

    @pl.when(h == 0)
    def _():
        acc_ref[...] = jnp.zeros_like(acc_ref)

    q = q_ref[...]
    do = do_ref[...]
    k = k_ref[...]
    pos = pos_ref[...]
    rows_here = q.shape[0]
    scores = lax.dot_general(q, k, last_dims, preferred_element_type=jnp.float32) * inverse_root
    rows = lax.broadcasted_iota(jnp.int32, (rows_here, seq_len), 0) + offset_ref[0]
    cols = lax.broadcasted_iota(jnp.int32, (rows_here, seq_len), 1)
    visible = (cols <= rows) & (rows - cols <= pos)
    masked = jnp.where(visible, scores, -jnp.inf)
    row_max = jnp.max(masked, axis=1, keepdims=True)
    exp_terms = jnp.where(visible, jnp.exp(scores - row_max), 0.0)
    probs = exp_terms / jnp.sum(exp_terms, axis=1, keepdims=True)
    kept = (mixing(rows * seq_len + cols + head_seed) & 16777215) >= drop_cut
    if first:
        dropped = jnp.where(kept, probs * keep_scale, 0.0).astype(jnp.bfloat16)
        dv_ref[...] += lax.dot_general(dropped, do, first_dims, preferred_element_type=jnp.float32)
        return
    v = v_ref[...]
    raw = lax.dot_general(do, v, last_dims, preferred_element_type=jnp.float32)
    prob_grad = jnp.where(kept, raw * keep_scale, 0.0)
    row_delta = jnp.sum(probs * prob_grad, axis=1, keepdims=True)
    score_grad = (probs * (prob_grad - row_delta)).astype(jnp.bfloat16)
    dq = jnp.dot(score_grad, k, preferred_element_type=jnp.float32) * inverse_root
    dq_ref[...] = dq.astype(dq_ref.dtype)
    dk_ref[...] += (
        lax.dot_general(score_grad, q, first_dims, preferred_element_type=jnp.float32)
        * inverse_root
    )


def attention(seeds, offset, pos, queries, grads, keys, values):
    rows_here = queries.shape[0]
    seq_len = keys.shape[0]
    groups = keys.shape[1] // HD
    per_group = queries.shape[1] // HD // groups
    head_map = lambda g, h, s, o: (0, g * per_group + h)
    group_map = lambda g, h, s, o: (0, g)
    whole_map = lambda g, h, s, o: (0, 0)
    first = values is None
    kernel = functools.partial(
        attention_kernel, seq_len=seq_len, per_group=per_group, first=first
    )
    in_specs = [
        pl.BlockSpec((rows_here, 1), whole_map),
        pl.BlockSpec((rows_here, HD), head_map),
        pl.BlockSpec((rows_here, HD), head_map),
        pl.BlockSpec((seq_len, HD), group_map),
    ]
    operands = [seeds, offset, pos, queries, grads, keys]
    acc = jax.ShapeDtypeStruct(keys.shape, jnp.float32)
    if first:
        out_specs = [pl.BlockSpec((seq_len, HD), group_map)]
        out_shape = [acc]
    else:
        in_specs.append(pl.BlockSpec((seq_len, HD), group_map))
        operands.append(values)
        out_specs = [pl.BlockSpec((rows_here, HD), head_map), pl.BlockSpec((seq_len, HD), group_map)]
        out_shape = [jax.ShapeDtypeStruct(queries.shape, jnp.bfloat16), acc]
    return pl.pallas_call(
        kernel,
        grid_spec=pltpu.PrefetchScalarGridSpec(
            num_scalar_prefetch=2,
            grid=(groups, per_group),
            in_specs=in_specs,
            out_specs=out_specs,
        ),
        out_shape=out_shape,
        compiler_params=pltpu.CompilerParams(
            dimension_semantics=("arbitrary", "arbitrary"),
            vmem_limit_bytes=48 * 1024 * 1024,
        ),
    )(*operands)


def gather_seq(piece, seq_index, seq_devices):
    received = [piece]
    for shift in range(1, seq_devices):
        received.append(
            lax.ppermute(piece, "seq", [(i, (i + shift) % seq_devices) for i in range(seq_devices)])
        )
    order = (seq_index - jnp.arange(seq_devices, dtype=jnp.int32)) % seq_devices
    stacked = jnp.take(jnp.stack(received), order, axis=0)
    return stacked.reshape((seq_devices * piece.shape[0],) + piece.shape[1:])


def reduce_seq(partial, seq_index, seq_devices):
    blocks = partial.reshape((seq_devices, partial.shape[0] // seq_devices) + partial.shape[1:])
    summed = lax.dynamic_index_in_dim(blocks, seq_index, 0, keepdims=False)
    for shift in range(1, seq_devices):
        piece = lax.dynamic_index_in_dim(blocks, (seq_index + shift) % seq_devices, 0, keepdims=False)
        summed = summed + lax.ppermute(
            piece, "seq", [(i, (i + shift) % seq_devices) for i in range(seq_devices)]
        )
    return summed


def per_device(layer_input, queries, key_states, out_grad, doc_positions, drop_seed, value_weight):
    seq_devices = lax.axis_size("seq")
    zx_devices = lax.axis_size("zx")
    fsdp_devices = zx_devices * 2
    core_index = lax.axis_index("core")
    seq_index = lax.axis_index("seq")
    batch_index = lax.axis_index(FSDP)
    tok_rows = layer_input.shape[1]
    seq_len = tok_rows * seq_devices
    local_input = layer_input[0]
    block_rows = value_weight.shape[0]
    swap = [(0, 1), (1, 0)]
    weight_own = lax.all_gather(value_weight, ("seq", "zx"), axis=0, tiled=True)
    input_view = local_input.reshape(tok_rows, seq_devices * zx_devices, 2, block_rows)
    input_own = lax.dynamic_index_in_dim(input_view, core_index, 2, keepdims=False).reshape(
        tok_rows, -1
    )
    input_other = lax.dynamic_index_in_dim(input_view, 1 - core_index, 2, keepdims=False).reshape(
        tok_rows, -1
    )
    base_seed = mixing(drop_seed + batch_index * 1000003)
    seeds = mixing(base_seed ^ jnp.arange(QH, dtype=jnp.int32) * 1640531527)
    offset = (seq_index * tok_rows).reshape(1).astype(jnp.int32)
    pos = lax.dynamic_slice_in_dim(doc_positions[0], seq_index * tok_rows, tok_rows)[:, None]
    query_loc, grad_loc = queries[0], out_grad[0]
    key_full = gather_seq(key_states[0], seq_index, seq_devices)
    (dv,) = attention(seeds, offset, pos, query_loc, grad_loc, key_full, None)
    value_grad = reduce_seq(dv, seq_index, seq_devices).astype(jnp.bfloat16)
    grads_pair = gather_seq(value_grad, seq_index, seq_devices)
    grads_own = lax.all_to_all(
        jnp.broadcast_to(grads_pair[None], (zx_devices,) + grads_pair.shape),
        "zx",
        split_axis=0,
        concat_axis=0,
        tiled=True,
    ).reshape(zx_devices, seq_devices, tok_rows, KVH * HD)
    input_cols = lax.all_to_all(
        local_input.reshape(tok_rows, seq_devices * fsdp_devices, block_rows),
        ("seq",) + FSDP,
        split_axis=1,
        concat_axis=0,
        tiled=True,
    ).reshape(seq_devices, zx_devices, 2, tok_rows, block_rows)
    value_grad, weight_own, input_cols = lax.optimization_barrier(
        (value_grad, weight_own, input_cols)
    )
    weight_other = lax.ppermute(weight_own, "core", swap)
    values_loc = (
        jnp.dot(input_own, weight_own, preferred_element_type=jnp.float32)
        + jnp.dot(input_other, weight_other, preferred_element_type=jnp.float32)
    ).astype(jnp.bfloat16)
    last_dims = (((1,), (1,)), ((), ()))
    grad_own = lax.dot_general(
        value_grad, weight_own, last_dims, preferred_element_type=jnp.float32
    ).astype(jnp.bfloat16).reshape(tok_rows, seq_devices * zx_devices, 1, block_rows)
    grad_other = lax.dot_general(
        value_grad, weight_other, last_dims, preferred_element_type=jnp.float32
    ).astype(jnp.bfloat16).reshape(tok_rows, seq_devices * zx_devices, 1, block_rows)
    input_grad = jnp.where(
        core_index == 0,
        jnp.concatenate([grad_own, grad_other], axis=2),
        jnp.concatenate([grad_other, grad_own], axis=2),
    ).reshape(tok_rows, -1)
    value_full = gather_seq(values_loc, seq_index, seq_devices)
    input_grad, value_full = lax.optimization_barrier((input_grad, value_full))
    dq, dk = attention(seeds, offset, pos, query_loc, grad_loc, key_full, value_full)
    key_grad = reduce_seq(dk, seq_index, seq_devices).astype(jnp.bfloat16)
    grads_own, input_cols, dq, key_grad = lax.optimization_barrier(
        (grads_own, input_cols, dq, key_grad)
    )
    query_grad = dq
    grads_other = lax.ppermute(grads_own, "core", swap)
    cols_own = lax.dynamic_index_in_dim(input_cols, core_index, 2, keepdims=False)
    cols_other = lax.dynamic_index_in_dim(input_cols, 1 - core_index, 2, keepdims=False)
    token_dims = (((0, 1, 2), (1, 0, 2)), ((), ()))
    summed = lax.dot_general(
        cols_own, grads_own, token_dims, preferred_element_type=jnp.float32
    ) + lax.dot_general(cols_other, grads_other, token_dims, preferred_element_type=jnp.float32)
    weight_grad = (summed * (1.0 / math.sqrt(fsdp_devices * seq_len))).astype(jnp.bfloat16)

    return (query_grad[None], key_grad[None], input_grad[None], weight_grad)


def solution(mesh):
    seq_devices, fsdp_devices = mesh.devices.shape
    chips = jax.sharding.Mesh(
        mesh.devices.reshape(seq_devices, fsdp_devices // 2, 2), ("seq",) + FSDP
    )
    return jax.shard_map(
        per_device,
        mesh=chips,
        in_specs=(
            P(FSDP, "seq", None),
            P(FSDP, "seq", None),
            P(FSDP, "seq", None),
            P(FSDP, "seq", None),
            P(FSDP, None),
            P(),
            P(("seq",) + FSDP, None),
        ),
        out_specs=(
            P(FSDP, "seq", None),
            P(FSDP, "seq", None),
            P(FSDP, "seq", None),
            P(("seq",) + FSDP, None),
        ),
        check_vma=False,
    )
```

```python
import functools
import math

import jax
import jax.numpy as jnp
from jax import lax
from jax.experimental import pallas as pl
from jax.experimental.pallas import tpu as pltpu
from jax.sharding import PartitionSpec as P

HD = 128
QH = 32
KVH = 4
ROWS = 128
FSDP = ("zx", "core")


drop_cut = 1677722
keep_scale = 1.0 / 0.9


def mixing(state):
    state = state ^ lax.shift_right_logical(state, jnp.full_like(state, 16))
    state = state * 2146121005
    state = state ^ lax.shift_right_logical(state, jnp.full_like(state, 15))
    state = state * 739982445
    state = state ^ lax.shift_right_logical(state, jnp.full_like(state, 16))
    return state


def attention_kernel(seeds_ref, offset_ref, pos_ref, q_ref, do_ref, k_ref, *refs, seq_len,
                     per_group, first):
    if first:
        (dv_ref,) = refs
    else:
        v_ref, dq_ref, dk_ref = refs
    g = pl.program_id(0)
    h = pl.program_id(1)
    head_seed = seeds_ref[g * per_group + h]
    inverse_root = 1.0 / math.sqrt(HD)
    last_dims = (((1,), (1,)), ((), ()))
    first_dims = (((0,), (0,)), ((), ()))
    acc_ref = dv_ref if first else dk_ref

    @pl.when(h == 0)
    def _():
        acc_ref[...] = jnp.zeros_like(acc_ref)

    q = q_ref[...]
    do = do_ref[...]
    k = k_ref[...]
    pos = pos_ref[...]
    rows_here = q.shape[0]
    scores = lax.dot_general(q, k, last_dims, preferred_element_type=jnp.float32) * inverse_root
    rows = lax.broadcasted_iota(jnp.int32, (rows_here, seq_len), 0) + offset_ref[0]
    cols = lax.broadcasted_iota(jnp.int32, (rows_here, seq_len), 1)
    visible = (cols <= rows) & (rows - cols <= pos)
    masked = jnp.where(visible, scores, -jnp.inf)
    row_max = jnp.max(masked, axis=1, keepdims=True)
    exp_terms = jnp.where(visible, jnp.exp(scores - row_max), 0.0)
    probs = exp_terms / jnp.sum(exp_terms, axis=1, keepdims=True)
    kept = (mixing(rows * seq_len + cols + head_seed) & 16777215) >= drop_cut
    if first:
        dropped = jnp.where(kept, probs * keep_scale, 0.0).astype(jnp.bfloat16)
        dv_ref[...] += lax.dot_general(dropped, do, first_dims, preferred_element_type=jnp.float32)
        return
    v = v_ref[...]
    raw = lax.dot_general(do, v, last_dims, preferred_element_type=jnp.float32)
    prob_grad = jnp.where(kept, raw * keep_scale, 0.0)
    row_delta = jnp.sum(probs * prob_grad, axis=1, keepdims=True)
    score_grad = (probs * (prob_grad - row_delta)).astype(jnp.bfloat16)
    dq = jnp.dot(score_grad, k, preferred_element_type=jnp.float32) * inverse_root
    dq_ref[...] = dq.astype(dq_ref.dtype)
    dk_ref[...] += (
        lax.dot_general(score_grad, q, first_dims, preferred_element_type=jnp.float32)
        * inverse_root
    )


def attention(seeds, offset, pos, queries, grads, keys, values):
    rows_here = queries.shape[0]
    seq_len = keys.shape[0]
    groups = keys.shape[1] // HD
    per_group = queries.shape[1] // HD // groups
    head_map = lambda g, h, s, o: (0, g * per_group + h)
    group_map = lambda g, h, s, o: (0, g)
    whole_map = lambda g, h, s, o: (0, 0)
    first = values is None
    kernel = functools.partial(
        attention_kernel, seq_len=seq_len, per_group=per_group, first=first
    )
    in_specs = [
        pl.BlockSpec((rows_here, 1), whole_map),
        pl.BlockSpec((rows_here, HD), head_map),
        pl.BlockSpec((rows_here, HD), head_map),
        pl.BlockSpec((seq_len, HD), group_map),
    ]
    operands = [seeds, offset, pos, queries, grads, keys]
    acc = jax.ShapeDtypeStruct(keys.shape, jnp.float32)
    if first:
        out_specs = [pl.BlockSpec((seq_len, HD), group_map)]
        out_shape = [acc]
    else:
        in_specs.append(pl.BlockSpec((seq_len, HD), group_map))
        operands.append(values)
        out_specs = [pl.BlockSpec((rows_here, HD), head_map), pl.BlockSpec((seq_len, HD), group_map)]
        out_shape = [jax.ShapeDtypeStruct(queries.shape, jnp.bfloat16), acc]
    return pl.pallas_call(
        kernel,
        grid_spec=pltpu.PrefetchScalarGridSpec(
            num_scalar_prefetch=2,
            grid=(groups, per_group),
            in_specs=in_specs,
            out_specs=out_specs,
        ),
        out_shape=out_shape,
        compiler_params=pltpu.CompilerParams(
            dimension_semantics=("arbitrary", "arbitrary"),
            vmem_limit_bytes=48 * 1024 * 1024,
        ),
    )(*operands)


def gather_seq(piece, seq_index, seq_devices):
    received = [piece]
    for shift in range(1, seq_devices):
        received.append(
            lax.ppermute(piece, "seq", [(i, (i + shift) % seq_devices) for i in range(seq_devices)])
        )
    order = (seq_index - jnp.arange(seq_devices, dtype=jnp.int32)) % seq_devices
    stacked = jnp.take(jnp.stack(received), order, axis=0)
    return stacked.reshape((seq_devices * piece.shape[0],) + piece.shape[1:])


def reduce_seq(partial, seq_index, seq_devices):
    blocks = partial.reshape((seq_devices, partial.shape[0] // seq_devices) + partial.shape[1:])
    summed = lax.dynamic_index_in_dim(blocks, seq_index, 0, keepdims=False)
    for shift in range(1, seq_devices):
        piece = lax.dynamic_index_in_dim(blocks, (seq_index + shift) % seq_devices, 0, keepdims=False)
        summed = summed + lax.ppermute(
            piece, "seq", [(i, (i + shift) % seq_devices) for i in range(seq_devices)]
        )
    return summed


def per_device(layer_input, queries, key_states, out_grad, doc_positions, drop_seed, value_weight):
    seq_devices = lax.axis_size("seq")
    zx_devices = lax.axis_size("zx")
    fsdp_devices = zx_devices * 2
    core_index = lax.axis_index("core")
    seq_index = lax.axis_index("seq")
    batch_index = lax.axis_index(FSDP)
    tok_rows = layer_input.shape[1]
    seq_len = tok_rows * seq_devices
    local_input = layer_input[0]
    block_rows = value_weight.shape[0]
    swap = [(0, 1), (1, 0)]
    weight_own = lax.all_gather(value_weight, ("seq", "zx"), axis=0, tiled=True)
    input_view = local_input.reshape(tok_rows, seq_devices * zx_devices, 2, block_rows)
    input_own = lax.dynamic_index_in_dim(input_view, core_index, 2, keepdims=False).reshape(
        tok_rows, -1
    )
    input_other = lax.dynamic_index_in_dim(input_view, 1 - core_index, 2, keepdims=False).reshape(
        tok_rows, -1
    )
    base_seed = mixing(drop_seed + batch_index * 1000003)
    seeds = mixing(base_seed ^ jnp.arange(QH, dtype=jnp.int32) * 1640531527)
    offset = (seq_index * tok_rows).reshape(1).astype(jnp.int32)
    pos = lax.dynamic_slice_in_dim(doc_positions[0], seq_index * tok_rows, tok_rows)[:, None]
    query_loc, grad_loc = queries[0], out_grad[0]
    key_full = gather_seq(key_states[0], seq_index, seq_devices)
    (dv,) = attention(seeds, offset, pos, query_loc, grad_loc, key_full, None)
    value_grad = reduce_seq(dv, seq_index, seq_devices).astype(jnp.bfloat16)
    grads_own = lax.all_gather(value_grad, "zx", axis=0, tiled=True)
    value_grad, weight_own, input_late = lax.optimization_barrier(
        (value_grad, weight_own, local_input)
    )
    weight_other = lax.ppermute(weight_own, "core", swap)
    input_cols = lax.all_to_all(
        input_late.reshape(tok_rows, seq_devices, fsdp_devices, block_rows),
        FSDP,
        split_axis=2,
        concat_axis=0,
        tiled=True,
    ).reshape(zx_devices, 2, tok_rows, seq_devices * block_rows)
    values_loc = (
        jnp.dot(input_own, weight_own, preferred_element_type=jnp.float32)
        + jnp.dot(input_other, weight_other, preferred_element_type=jnp.float32)
    ).astype(jnp.bfloat16)
    last_dims = (((1,), (1,)), ((), ()))
    grad_own = lax.dot_general(
        value_grad, weight_own, last_dims, preferred_element_type=jnp.float32
    ).astype(jnp.bfloat16).reshape(tok_rows, seq_devices * zx_devices, 1, block_rows)
    grad_other = lax.dot_general(
        value_grad, weight_other, last_dims, preferred_element_type=jnp.float32
    ).astype(jnp.bfloat16).reshape(tok_rows, seq_devices * zx_devices, 1, block_rows)
    input_grad = jnp.where(
        core_index == 0,
        jnp.concatenate([grad_own, grad_other], axis=2),
        jnp.concatenate([grad_other, grad_own], axis=2),
    ).reshape(tok_rows, -1)
    value_full = gather_seq(values_loc, seq_index, seq_devices)
    input_grad, value_full = lax.optimization_barrier((input_grad, value_full))
    dq, dk = attention(seeds, offset, pos, query_loc, grad_loc, key_full, value_full)
    key_grad = reduce_seq(dk, seq_index, seq_devices).astype(jnp.bfloat16)
    grads_own, input_cols, dq, key_grad = lax.optimization_barrier(
        (grads_own, input_cols, dq, key_grad)
    )
    query_grad = dq
    grads_other = lax.ppermute(grads_own, "core", swap)
    cols_own = lax.dynamic_index_in_dim(input_cols, core_index, 1, keepdims=False).reshape(
        zx_devices * tok_rows, -1
    )
    cols_other = lax.dynamic_index_in_dim(input_cols, 1 - core_index, 1, keepdims=False).reshape(
        zx_devices * tok_rows, -1
    )
    first_dims = (((0,), (0,)), ((), ()))
    partial = (
        lax.dot_general(cols_own, grads_own, first_dims, preferred_element_type=jnp.float32)
        + lax.dot_general(cols_other, grads_other, first_dims, preferred_element_type=jnp.float32)
    ).reshape(seq_devices, block_rows, KVH * HD)
    summed = lax.dynamic_index_in_dim(partial, seq_index, 0, keepdims=False)
    for shift in range(1, seq_devices):
        piece = lax.dynamic_index_in_dim(
            partial, (seq_index + shift) % seq_devices, 0, keepdims=False
        )
        summed = summed + lax.ppermute(
            piece.astype(jnp.bfloat16),
            "seq",
            [(i, (i + shift) % seq_devices) for i in range(seq_devices)],
        ).astype(jnp.float32)
    weight_grad = (summed * (1.0 / math.sqrt(fsdp_devices * seq_len))).astype(jnp.bfloat16)

    return (query_grad[None], key_grad[None], input_grad[None], weight_grad)


def solution(mesh):
    seq_devices, fsdp_devices = mesh.devices.shape
    chips = jax.sharding.Mesh(
        mesh.devices.reshape(seq_devices, fsdp_devices // 2, 2), ("seq",) + FSDP
    )
    return jax.shard_map(
        per_device,
        mesh=chips,
        in_specs=(
            P(FSDP, "seq", None),
            P(FSDP, "seq", None),
            P(FSDP, "seq", None),
            P(FSDP, "seq", None),
            P(FSDP, None),
            P(),
            P(("seq",) + FSDP, None),
        ),
        out_specs=(
            P(FSDP, "seq", None),
            P(FSDP, "seq", None),
            P(FSDP, "seq", None),
            P(("seq",) + FSDP, None),
        ),
        check_vma=False,
    )
```

```python
import functools
import math

import jax
import jax.numpy as jnp
from jax import lax
from jax.experimental import pallas as pl
from jax.experimental.pallas import tpu as pltpu
from jax.sharding import PartitionSpec as P

HD = 128
QH = 32
KVH = 4
ROWS = 128
FSDP = ("zx", "core")


drop_cut = 1677722
keep_scale = 1.0 / 0.9


def mixing(state):
    state = state ^ lax.shift_right_logical(state, jnp.full_like(state, 16))
    state = state * 2146121005
    state = state ^ lax.shift_right_logical(state, jnp.full_like(state, 15))
    state = state * 739982445
    state = state ^ lax.shift_right_logical(state, jnp.full_like(state, 16))
    return state


def attention_kernel(seeds_ref, offset_ref, pos_ref, q_ref, do_ref, k_ref, *refs, seq_len,
                     per_group, first):
    if first:
        (dv_ref,) = refs
    else:
        v_ref, dq_ref, dk_ref = refs
    g = pl.program_id(0)
    h = pl.program_id(1)
    head_seed = seeds_ref[g * per_group + h]
    inverse_root = 1.0 / math.sqrt(HD)
    last_dims = (((1,), (1,)), ((), ()))
    first_dims = (((0,), (0,)), ((), ()))
    acc_ref = dv_ref if first else dk_ref

    @pl.when(h == 0)
    def _():
        acc_ref[...] = jnp.zeros_like(acc_ref)

    q = q_ref[...]
    do = do_ref[...]
    k = k_ref[...]
    pos = pos_ref[...]
    rows_here = q.shape[0]
    scores = lax.dot_general(q, k, last_dims, preferred_element_type=jnp.float32) * inverse_root
    rows = lax.broadcasted_iota(jnp.int32, (rows_here, seq_len), 0) + offset_ref[0]
    cols = lax.broadcasted_iota(jnp.int32, (rows_here, seq_len), 1)
    visible = (cols <= rows) & (rows - cols <= pos)
    masked = jnp.where(visible, scores, -jnp.inf)
    row_max = jnp.max(masked, axis=1, keepdims=True)
    exp_terms = jnp.where(visible, jnp.exp(scores - row_max), 0.0)
    probs = exp_terms / jnp.sum(exp_terms, axis=1, keepdims=True)
    kept = (mixing(rows * seq_len + cols + head_seed) & 16777215) >= drop_cut
    if first:
        dropped = jnp.where(kept, probs * keep_scale, 0.0).astype(jnp.bfloat16)
        dv_ref[...] += lax.dot_general(dropped, do, first_dims, preferred_element_type=jnp.float32)
        return
    v = v_ref[...]
    raw = lax.dot_general(do, v, last_dims, preferred_element_type=jnp.float32)
    prob_grad = jnp.where(kept, raw * keep_scale, 0.0)
    row_delta = jnp.sum(probs * prob_grad, axis=1, keepdims=True)
    score_grad = (probs * (prob_grad - row_delta)).astype(jnp.bfloat16)
    dq = jnp.dot(score_grad, k, preferred_element_type=jnp.float32) * inverse_root
    dq_ref[...] = dq.astype(dq_ref.dtype)
    dk_ref[...] += (
        lax.dot_general(score_grad, q, first_dims, preferred_element_type=jnp.float32)
        * inverse_root
    )


def attention(seeds, offset, pos, queries, grads, keys, values):
    rows_here = queries.shape[0]
    seq_len = keys.shape[0]
    groups = keys.shape[1] // HD
    per_group = queries.shape[1] // HD // groups
    head_map = lambda g, h, s, o: (0, g * per_group + h)
    group_map = lambda g, h, s, o: (0, g)
    whole_map = lambda g, h, s, o: (0, 0)
    first = values is None
    kernel = functools.partial(
        attention_kernel, seq_len=seq_len, per_group=per_group, first=first
    )
    in_specs = [
        pl.BlockSpec((rows_here, 1), whole_map),
        pl.BlockSpec((rows_here, HD), head_map),
        pl.BlockSpec((rows_here, HD), head_map),
        pl.BlockSpec((seq_len, HD), group_map),
    ]
    operands = [seeds, offset, pos, queries, grads, keys]
    acc = jax.ShapeDtypeStruct(keys.shape, jnp.float32)
    if first:
        out_specs = [pl.BlockSpec((seq_len, HD), group_map)]
        out_shape = [acc]
    else:
        in_specs.append(pl.BlockSpec((seq_len, HD), group_map))
        operands.append(values)
        out_specs = [pl.BlockSpec((rows_here, HD), head_map), pl.BlockSpec((seq_len, HD), group_map)]
        out_shape = [jax.ShapeDtypeStruct(queries.shape, jnp.bfloat16), acc]
    return pl.pallas_call(
        kernel,
        grid_spec=pltpu.PrefetchScalarGridSpec(
            num_scalar_prefetch=2,
            grid=(groups, per_group),
            in_specs=in_specs,
            out_specs=out_specs,
        ),
        out_shape=out_shape,
        compiler_params=pltpu.CompilerParams(
            dimension_semantics=("arbitrary", "arbitrary"),
            vmem_limit_bytes=48 * 1024 * 1024,
        ),
    )(*operands)


def gather_seq(piece, seq_index, seq_devices):
    received = [piece]
    for shift in range(1, seq_devices):
        received.append(
            lax.ppermute(piece, "seq", [(i, (i + shift) % seq_devices) for i in range(seq_devices)])
        )
    order = (seq_index - jnp.arange(seq_devices, dtype=jnp.int32)) % seq_devices
    stacked = jnp.take(jnp.stack(received), order, axis=0)
    return stacked.reshape((seq_devices * piece.shape[0],) + piece.shape[1:])


def reduce_seq(partial, seq_index, seq_devices):
    blocks = partial.reshape((seq_devices, partial.shape[0] // seq_devices) + partial.shape[1:])
    summed = lax.dynamic_index_in_dim(blocks, seq_index, 0, keepdims=False)
    for shift in range(1, seq_devices):
        piece = lax.dynamic_index_in_dim(blocks, (seq_index + shift) % seq_devices, 0, keepdims=False)
        summed = summed + lax.ppermute(
            piece, "seq", [(i, (i + shift) % seq_devices) for i in range(seq_devices)]
        )
    return summed


def per_device(layer_input, queries, key_states, out_grad, doc_positions, drop_seed, value_weight):
    seq_devices = lax.axis_size("seq")
    zx_devices = lax.axis_size("zx")
    fsdp_devices = zx_devices * 2
    core_index = lax.axis_index("core")
    seq_index = lax.axis_index("seq")
    batch_index = lax.axis_index(FSDP)
    tok_rows = layer_input.shape[1]
    seq_len = tok_rows * seq_devices
    local_input = layer_input[0]
    block_rows = value_weight.shape[0]
    swap = [(0, 1), (1, 0)]
    weight_own = lax.all_gather(value_weight, ("seq", "zx"), axis=0, tiled=True)
    input_view = local_input.reshape(tok_rows, seq_devices * zx_devices, 2, block_rows)
    input_own = lax.dynamic_index_in_dim(input_view, core_index, 2, keepdims=False).reshape(
        tok_rows, -1
    )
    input_other = lax.dynamic_index_in_dim(input_view, 1 - core_index, 2, keepdims=False).reshape(
        tok_rows, -1
    )
    base_seed = mixing(drop_seed + batch_index * 1000003)
    seeds = mixing(base_seed ^ jnp.arange(QH, dtype=jnp.int32) * 1640531527)
    offset = (seq_index * tok_rows).reshape(1).astype(jnp.int32)
    pos = lax.dynamic_slice_in_dim(doc_positions[0], seq_index * tok_rows, tok_rows)[:, None]
    query_loc, grad_loc = queries[0], out_grad[0]
    key_full = gather_seq(key_states[0], seq_index, seq_devices)
    (dv,) = attention(seeds, offset, pos, query_loc, grad_loc, key_full, None)
    value_grad = reduce_seq(dv, seq_index, seq_devices).astype(jnp.bfloat16)
    grads_own = lax.all_gather(value_grad, "zx", axis=0, tiled=True)
    value_grad, weight_own, input_late = lax.optimization_barrier(
        (value_grad, weight_own, local_input)
    )
    weight_other = lax.ppermute(weight_own, "core", swap)
    input_cols = lax.all_to_all(
        input_late.reshape(tok_rows, seq_devices, fsdp_devices, block_rows),
        FSDP,
        split_axis=2,
        concat_axis=0,
        tiled=True,
    ).reshape(zx_devices, 2, tok_rows, seq_devices * block_rows)
    values_loc = (
        jnp.dot(input_own, weight_own, preferred_element_type=jnp.float32)
        + jnp.dot(input_other, weight_other, preferred_element_type=jnp.float32)
    ).astype(jnp.bfloat16)
    last_dims = (((1,), (1,)), ((), ()))
    grad_own = lax.dot_general(
        value_grad, weight_own, last_dims, preferred_element_type=jnp.float32
    ).astype(jnp.bfloat16).reshape(tok_rows, seq_devices * zx_devices, 1, block_rows)
    grad_other = lax.dot_general(
        value_grad, weight_other, last_dims, preferred_element_type=jnp.float32
    ).astype(jnp.bfloat16).reshape(tok_rows, seq_devices * zx_devices, 1, block_rows)
    input_grad = jnp.where(
        core_index == 0,
        jnp.concatenate([grad_own, grad_other], axis=2),
        jnp.concatenate([grad_other, grad_own], axis=2),
    ).reshape(tok_rows, -1)
    value_full = gather_seq(values_loc, seq_index, seq_devices)
    input_grad, value_full = lax.optimization_barrier((input_grad, value_full))
    dq, dk = attention(seeds, offset, pos, query_loc, grad_loc, key_full, value_full)
    key_grad = reduce_seq(dk, seq_index, seq_devices).astype(jnp.bfloat16)
    grads_own, input_cols, dq, key_grad = lax.optimization_barrier(
        (grads_own, input_cols, dq, key_grad)
    )
    query_grad = dq
    grads_other = lax.ppermute(grads_own, "core", swap)
    cols_own = lax.dynamic_index_in_dim(input_cols, core_index, 1, keepdims=False).reshape(
        zx_devices * tok_rows, -1
    )
    cols_other = lax.dynamic_index_in_dim(input_cols, 1 - core_index, 1, keepdims=False).reshape(
        zx_devices * tok_rows, -1
    )
    first_dims = (((0,), (0,)), ((), ()))

    def block_partial(block):
        start = block * block_rows
        return lax.dot_general(
            lax.dynamic_slice_in_dim(cols_own, start, block_rows, 1),
            grads_own,
            first_dims,
            preferred_element_type=jnp.float32,
        ) + lax.dot_general(
            lax.dynamic_slice_in_dim(cols_other, start, block_rows, 1),
            grads_other,
            first_dims,
            preferred_element_type=jnp.float32,
        )

    received = []
    for shift in range(1, seq_devices):
        piece = block_partial((seq_index + shift) % seq_devices)
        received.append(
            lax.ppermute(
                piece.astype(jnp.bfloat16),
                "seq",
                [(i, (i + shift) % seq_devices) for i in range(seq_devices)],
            )
        )
    summed = lax.optimization_barrier(block_partial(seq_index))
    for piece in received:
        summed = summed + piece.astype(jnp.float32)
    weight_grad = (summed * (1.0 / math.sqrt(fsdp_devices * seq_len))).astype(jnp.bfloat16)

    return (query_grad[None], key_grad[None], input_grad[None], weight_grad)


def solution(mesh):
    seq_devices, fsdp_devices = mesh.devices.shape
    chips = jax.sharding.Mesh(
        mesh.devices.reshape(seq_devices, fsdp_devices // 2, 2), ("seq",) + FSDP
    )
    return jax.shard_map(
        per_device,
        mesh=chips,
        in_specs=(
            P(FSDP, "seq", None),
            P(FSDP, "seq", None),
            P(FSDP, "seq", None),
            P(FSDP, "seq", None),
            P(FSDP, None),
            P(),
            P(("seq",) + FSDP, None),
        ),
        out_specs=(
            P(FSDP, "seq", None),
            P(FSDP, "seq", None),
            P(FSDP, "seq", None),
            P(("seq",) + FSDP, None),
        ),
        check_vma=False,
    )
```

```python
import functools
import math

import jax
import jax.numpy as jnp
from jax import lax
from jax.experimental import pallas as pl
from jax.experimental.pallas import tpu as pltpu
from jax.sharding import PartitionSpec as P

HD = 128
QH = 32
KVH = 4
ROWS = 128
FSDP = ("zx", "core")


drop_cut = 1677722
keep_scale = 1.0 / 0.9


def mixing(state):
    state = state ^ lax.shift_right_logical(state, jnp.full_like(state, 16))
    state = state * 2146121005
    state = state ^ lax.shift_right_logical(state, jnp.full_like(state, 15))
    state = state * 739982445
    state = state ^ lax.shift_right_logical(state, jnp.full_like(state, 16))
    return state


def attention_kernel(seeds_ref, offset_ref, pos_ref, q_ref, do_ref, k_ref, *refs, seq_len,
                     per_group, first):
    if first:
        (dv_ref,) = refs
    else:
        v_ref, dq_ref, dk_ref = refs
    g = pl.program_id(0)
    h = pl.program_id(1)
    head_seed = seeds_ref[g * per_group + h]
    inverse_root = 1.0 / math.sqrt(HD)
    last_dims = (((1,), (1,)), ((), ()))
    first_dims = (((0,), (0,)), ((), ()))
    acc_ref = dv_ref if first else dk_ref

    @pl.when(h == 0)
    def _():
        acc_ref[...] = jnp.zeros_like(acc_ref)

    q = q_ref[...]
    do = do_ref[...]
    k = k_ref[...]
    pos = pos_ref[...]
    rows_here = q.shape[0]
    scores = lax.dot_general(q, k, last_dims, preferred_element_type=jnp.float32) * inverse_root
    rows = lax.broadcasted_iota(jnp.int32, (rows_here, seq_len), 0) + offset_ref[0]
    cols = lax.broadcasted_iota(jnp.int32, (rows_here, seq_len), 1)
    visible = (cols <= rows) & (rows - cols <= pos)
    masked = jnp.where(visible, scores, -jnp.inf)
    row_max = jnp.max(masked, axis=1, keepdims=True)
    exp_terms = jnp.where(visible, jnp.exp(scores - row_max), 0.0)
    probs = exp_terms / jnp.sum(exp_terms, axis=1, keepdims=True)
    kept = (mixing(rows * seq_len + cols + head_seed) & 16777215) >= drop_cut
    if first:
        dropped = jnp.where(kept, probs * keep_scale, 0.0).astype(jnp.bfloat16)
        dv_ref[...] += lax.dot_general(dropped, do, first_dims, preferred_element_type=jnp.float32)
        return
    v = v_ref[...]
    raw = lax.dot_general(do, v, last_dims, preferred_element_type=jnp.float32)
    prob_grad = jnp.where(kept, raw * keep_scale, 0.0)
    row_delta = jnp.sum(probs * prob_grad, axis=1, keepdims=True)
    score_grad = (probs * (prob_grad - row_delta)).astype(jnp.bfloat16)
    dq = jnp.dot(score_grad, k, preferred_element_type=jnp.float32) * inverse_root
    dq_ref[...] = dq.astype(dq_ref.dtype)
    dk_ref[...] += (
        lax.dot_general(score_grad, q, first_dims, preferred_element_type=jnp.float32)
        * inverse_root
    )


def attention(seeds, offset, pos, queries, grads, keys, values):
    rows_here = queries.shape[0]
    seq_len = keys.shape[0]
    groups = keys.shape[1] // HD
    per_group = queries.shape[1] // HD // groups
    head_map = lambda g, h, s, o: (0, g * per_group + h)
    group_map = lambda g, h, s, o: (0, g)
    whole_map = lambda g, h, s, o: (0, 0)
    first = values is None
    kernel = functools.partial(
        attention_kernel, seq_len=seq_len, per_group=per_group, first=first
    )
    in_specs = [
        pl.BlockSpec((rows_here, 1), whole_map),
        pl.BlockSpec((rows_here, HD), head_map),
        pl.BlockSpec((rows_here, HD), head_map),
        pl.BlockSpec((seq_len, HD), group_map),
    ]
    operands = [seeds, offset, pos, queries, grads, keys]
    acc = jax.ShapeDtypeStruct(keys.shape, jnp.float32)
    if first:
        out_specs = [pl.BlockSpec((seq_len, HD), group_map)]
        out_shape = [acc]
    else:
        in_specs.append(pl.BlockSpec((seq_len, HD), group_map))
        operands.append(values)
        out_specs = [pl.BlockSpec((rows_here, HD), head_map), pl.BlockSpec((seq_len, HD), group_map)]
        out_shape = [jax.ShapeDtypeStruct(queries.shape, jnp.bfloat16), acc]
    return pl.pallas_call(
        kernel,
        grid_spec=pltpu.PrefetchScalarGridSpec(
            num_scalar_prefetch=2,
            grid=(groups, per_group),
            in_specs=in_specs,
            out_specs=out_specs,
        ),
        out_shape=out_shape,
        compiler_params=pltpu.CompilerParams(
            dimension_semantics=("arbitrary", "arbitrary"),
            vmem_limit_bytes=48 * 1024 * 1024,
        ),
    )(*operands)


def gather_seq(piece, seq_index, seq_devices):
    received = [piece]
    for shift in range(1, seq_devices):
        received.append(
            lax.ppermute(piece, "seq", [(i, (i + shift) % seq_devices) for i in range(seq_devices)])
        )
    order = (seq_index - jnp.arange(seq_devices, dtype=jnp.int32)) % seq_devices
    stacked = jnp.take(jnp.stack(received), order, axis=0)
    return stacked.reshape((seq_devices * piece.shape[0],) + piece.shape[1:])


def reduce_seq(partial, seq_index, seq_devices):
    blocks = partial.reshape((seq_devices, partial.shape[0] // seq_devices) + partial.shape[1:])
    summed = lax.dynamic_index_in_dim(blocks, seq_index, 0, keepdims=False)
    for shift in range(1, seq_devices):
        piece = lax.dynamic_index_in_dim(blocks, (seq_index + shift) % seq_devices, 0, keepdims=False)
        summed = summed + lax.ppermute(
            piece, "seq", [(i, (i + shift) % seq_devices) for i in range(seq_devices)]
        )
    return summed


def per_device(layer_input, queries, key_states, out_grad, doc_positions, drop_seed, value_weight):
    seq_devices = lax.axis_size("seq")
    zx_devices = lax.axis_size("zx")
    fsdp_devices = zx_devices * 2
    core_index = lax.axis_index("core")
    seq_index = lax.axis_index("seq")
    batch_index = lax.axis_index(FSDP)
    tok_rows = layer_input.shape[1]
    seq_len = tok_rows * seq_devices
    local_input = layer_input[0]
    block_rows = value_weight.shape[0]
    swap = [(0, 1), (1, 0)]
    weight_own = lax.all_gather(value_weight, ("seq", "zx"), axis=0, tiled=True)
    input_view = local_input.reshape(tok_rows, seq_devices * zx_devices, 2, block_rows)
    input_own = lax.dynamic_index_in_dim(input_view, core_index, 2, keepdims=False).reshape(
        tok_rows, -1
    )
    input_other = lax.dynamic_index_in_dim(input_view, 1 - core_index, 2, keepdims=False).reshape(
        tok_rows, -1
    )
    base_seed = mixing(drop_seed + batch_index * 1000003)
    seeds = mixing(base_seed ^ jnp.arange(QH, dtype=jnp.int32) * 1640531527)
    offset = (seq_index * tok_rows).reshape(1).astype(jnp.int32)
    pos = lax.dynamic_slice_in_dim(doc_positions[0], seq_index * tok_rows, tok_rows)[:, None]
    query_loc, grad_loc = queries[0], out_grad[0]
    key_full = gather_seq(key_states[0], seq_index, seq_devices)
    (dv,) = attention(seeds, offset, pos, query_loc, grad_loc, key_full, None)
    value_grad = reduce_seq(dv, seq_index, seq_devices).astype(jnp.bfloat16)
    grads_own = lax.all_gather(value_grad, "zx", axis=0, tiled=True)
    input_major = jnp.transpose(
        local_input.reshape(tok_rows, seq_devices, fsdp_devices, block_rows), (2, 0, 1, 3)
    )
    value_grad, weight_own, input_late = lax.optimization_barrier(
        (value_grad, weight_own, input_major)
    )
    weight_other = lax.ppermute(weight_own, "core", swap)
    input_cols = lax.all_to_all(
        input_late, FSDP, split_axis=0, concat_axis=0, tiled=True
    ).reshape(zx_devices, 2, tok_rows, seq_devices * block_rows)
    values_loc = (
        jnp.dot(input_own, weight_own, preferred_element_type=jnp.float32)
        + jnp.dot(input_other, weight_other, preferred_element_type=jnp.float32)
    ).astype(jnp.bfloat16)
    last_dims = (((1,), (1,)), ((), ()))
    grad_own = lax.dot_general(
        value_grad, weight_own, last_dims, preferred_element_type=jnp.float32
    ).astype(jnp.bfloat16).reshape(tok_rows, seq_devices * zx_devices, 1, block_rows)
    grad_other = lax.dot_general(
        value_grad, weight_other, last_dims, preferred_element_type=jnp.float32
    ).astype(jnp.bfloat16).reshape(tok_rows, seq_devices * zx_devices, 1, block_rows)
    input_grad = jnp.where(
        core_index == 0,
        jnp.concatenate([grad_own, grad_other], axis=2),
        jnp.concatenate([grad_other, grad_own], axis=2),
    ).reshape(tok_rows, -1)
    value_full = gather_seq(values_loc, seq_index, seq_devices)
    input_grad, value_full = lax.optimization_barrier((input_grad, value_full))
    dq, dk = attention(seeds, offset, pos, query_loc, grad_loc, key_full, value_full)
    key_grad = reduce_seq(dk, seq_index, seq_devices).astype(jnp.bfloat16)
    grads_own, input_cols, dq, key_grad = lax.optimization_barrier(
        (grads_own, input_cols, dq, key_grad)
    )
    query_grad = dq
    grads_other = lax.ppermute(grads_own, "core", swap)
    cols_own = lax.dynamic_index_in_dim(input_cols, core_index, 1, keepdims=False).reshape(
        zx_devices * tok_rows, -1
    )
    cols_other = lax.dynamic_index_in_dim(input_cols, 1 - core_index, 1, keepdims=False).reshape(
        zx_devices * tok_rows, -1
    )
    first_dims = (((0,), (0,)), ((), ()))
    partial = (
        lax.dot_general(cols_own, grads_own, first_dims, preferred_element_type=jnp.float32)
        + lax.dot_general(cols_other, grads_other, first_dims, preferred_element_type=jnp.float32)
    ).reshape(seq_devices, block_rows, KVH * HD)
    summed = lax.dynamic_index_in_dim(partial, seq_index, 0, keepdims=False)
    for shift in range(1, seq_devices):
        piece = lax.dynamic_index_in_dim(
            partial, (seq_index + shift) % seq_devices, 0, keepdims=False
        )
        summed = summed + lax.ppermute(
            piece.astype(jnp.bfloat16),
            "seq",
            [(i, (i + shift) % seq_devices) for i in range(seq_devices)],
        ).astype(jnp.float32)
    weight_grad = (summed * (1.0 / math.sqrt(fsdp_devices * seq_len))).astype(jnp.bfloat16)

    return (query_grad[None], key_grad[None], input_grad[None], weight_grad)


def solution(mesh):
    seq_devices, fsdp_devices = mesh.devices.shape
    chips = jax.sharding.Mesh(
        mesh.devices.reshape(seq_devices, fsdp_devices // 2, 2), ("seq",) + FSDP
    )
    return jax.shard_map(
        per_device,
        mesh=chips,
        in_specs=(
            P(FSDP, "seq", None),
            P(FSDP, "seq", None),
            P(FSDP, "seq", None),
            P(FSDP, "seq", None),
            P(FSDP, None),
            P(),
            P(("seq",) + FSDP, None),
        ),
        out_specs=(
            P(FSDP, "seq", None),
            P(FSDP, "seq", None),
            P(FSDP, "seq", None),
            P(("seq",) + FSDP, None),
        ),
        check_vma=False,
    )
```

```python
import functools
import math

import jax
import jax.numpy as jnp
from jax import lax
from jax.experimental import pallas as pl
from jax.experimental.pallas import tpu as pltpu
from jax.sharding import PartitionSpec as P

HD = 128
QH = 32
KVH = 4
ROWS = 128
FSDP = ("zx", "core")


drop_cut = 1677722
keep_scale = 1.0 / 0.9


def mixing(state):
    state = state ^ lax.shift_right_logical(state, jnp.full_like(state, 16))
    state = state * 2146121005
    state = state ^ lax.shift_right_logical(state, jnp.full_like(state, 15))
    state = state * 739982445
    state = state ^ lax.shift_right_logical(state, jnp.full_like(state, 16))
    return state


def attention_kernel(seeds_ref, offset_ref, pos_ref, q_ref, do_ref, k_ref, *refs, seq_len,
                     per_group, first):
    if first:
        (dv_ref,) = refs
    else:
        v_ref, dq_ref, dk_ref = refs
    g = pl.program_id(0)
    h = pl.program_id(1)
    head_seed = seeds_ref[g * per_group + h]
    inverse_root = 1.0 / math.sqrt(HD)
    last_dims = (((1,), (1,)), ((), ()))
    first_dims = (((0,), (0,)), ((), ()))
    acc_ref = dv_ref if first else dk_ref

    @pl.when(h == 0)
    def _():
        acc_ref[...] = jnp.zeros_like(acc_ref)

    q = q_ref[...]
    do = do_ref[...]
    k = k_ref[...]
    pos = pos_ref[...]
    rows_here = q.shape[0]
    scores = lax.dot_general(q, k, last_dims, preferred_element_type=jnp.float32) * inverse_root
    rows = lax.broadcasted_iota(jnp.int32, (rows_here, seq_len), 0) + offset_ref[0]
    cols = lax.broadcasted_iota(jnp.int32, (rows_here, seq_len), 1)
    visible = (cols <= rows) & (rows - cols <= pos)
    masked = jnp.where(visible, scores, -jnp.inf)
    row_max = jnp.max(masked, axis=1, keepdims=True)
    exp_terms = jnp.where(visible, jnp.exp(scores - row_max), 0.0)
    probs = exp_terms / jnp.sum(exp_terms, axis=1, keepdims=True)
    kept = (mixing(rows * seq_len + cols + head_seed) & 16777215) >= drop_cut
    if first:
        dropped = jnp.where(kept, probs * keep_scale, 0.0).astype(jnp.bfloat16)
        dv_ref[...] += lax.dot_general(dropped, do, first_dims, preferred_element_type=jnp.float32)
        return
    v = v_ref[...]
    raw = lax.dot_general(do, v, last_dims, preferred_element_type=jnp.float32)
    prob_grad = jnp.where(kept, raw * keep_scale, 0.0)
    row_delta = jnp.sum(probs * prob_grad, axis=1, keepdims=True)
    score_grad = (probs * (prob_grad - row_delta)).astype(jnp.bfloat16)
    dq = jnp.dot(score_grad, k, preferred_element_type=jnp.float32) * inverse_root
    dq_ref[...] = dq.astype(dq_ref.dtype)
    dk_ref[...] += (
        lax.dot_general(score_grad, q, first_dims, preferred_element_type=jnp.float32)
        * inverse_root
    )


def attention(seeds, offset, pos, queries, grads, keys, values):
    rows_here = queries.shape[0]
    seq_len = keys.shape[0]
    groups = keys.shape[1] // HD
    per_group = queries.shape[1] // HD // groups
    head_map = lambda g, h, s, o: (0, g * per_group + h)
    group_map = lambda g, h, s, o: (0, g)
    whole_map = lambda g, h, s, o: (0, 0)
    first = values is None
    kernel = functools.partial(
        attention_kernel, seq_len=seq_len, per_group=per_group, first=first
    )
    in_specs = [
        pl.BlockSpec((rows_here, 1), whole_map),
        pl.BlockSpec((rows_here, HD), head_map),
        pl.BlockSpec((rows_here, HD), head_map),
        pl.BlockSpec((seq_len, HD), group_map),
    ]
    operands = [seeds, offset, pos, queries, grads, keys]
    acc = jax.ShapeDtypeStruct(keys.shape, jnp.float32)
    if first:
        out_specs = [pl.BlockSpec((seq_len, HD), group_map)]
        out_shape = [acc]
    else:
        in_specs.append(pl.BlockSpec((seq_len, HD), group_map))
        operands.append(values)
        out_specs = [pl.BlockSpec((rows_here, HD), head_map), pl.BlockSpec((seq_len, HD), group_map)]
        out_shape = [jax.ShapeDtypeStruct(queries.shape, jnp.bfloat16), acc]
    return pl.pallas_call(
        kernel,
        grid_spec=pltpu.PrefetchScalarGridSpec(
            num_scalar_prefetch=2,
            grid=(groups, per_group),
            in_specs=in_specs,
            out_specs=out_specs,
        ),
        out_shape=out_shape,
        compiler_params=pltpu.CompilerParams(
            dimension_semantics=("arbitrary", "arbitrary"),
            vmem_limit_bytes=48 * 1024 * 1024,
        ),
    )(*operands)


def gather_seq(piece, seq_index, seq_devices):
    received = [piece]
    for shift in range(1, seq_devices):
        received.append(
            lax.ppermute(piece, "seq", [(i, (i + shift) % seq_devices) for i in range(seq_devices)])
        )
    order = (seq_index - jnp.arange(seq_devices, dtype=jnp.int32)) % seq_devices
    stacked = jnp.take(jnp.stack(received), order, axis=0)
    return stacked.reshape((seq_devices * piece.shape[0],) + piece.shape[1:])


def reduce_seq(partial, seq_index, seq_devices):
    blocks = partial.reshape((seq_devices, partial.shape[0] // seq_devices) + partial.shape[1:])
    summed = lax.dynamic_index_in_dim(blocks, seq_index, 0, keepdims=False)
    for shift in range(1, seq_devices):
        piece = lax.dynamic_index_in_dim(blocks, (seq_index + shift) % seq_devices, 0, keepdims=False)
        summed = summed + lax.ppermute(
            piece, "seq", [(i, (i + shift) % seq_devices) for i in range(seq_devices)]
        )
    return summed


def per_device(layer_input, queries, key_states, out_grad, doc_positions, drop_seed, value_weight):
    seq_devices = lax.axis_size("seq")
    zx_devices = lax.axis_size("zx")
    fsdp_devices = zx_devices * 2
    core_index = lax.axis_index("core")
    seq_index = lax.axis_index("seq")
    batch_index = lax.axis_index(FSDP)
    tok_rows = layer_input.shape[1]
    seq_len = tok_rows * seq_devices
    local_input = layer_input[0]
    block_rows = value_weight.shape[0]
    swap = [(0, 1), (1, 0)]
    weight_own = lax.all_gather(value_weight, ("zx", "seq"), axis=0, tiled=True)
    input_view = jnp.transpose(
        local_input.reshape(tok_rows, seq_devices, zx_devices, 2, block_rows), (0, 2, 1, 3, 4)
    ).reshape(tok_rows, zx_devices * seq_devices, 2, block_rows)
    input_own = lax.dynamic_index_in_dim(input_view, core_index, 2, keepdims=False).reshape(
        tok_rows, -1
    )
    input_other = lax.dynamic_index_in_dim(input_view, 1 - core_index, 2, keepdims=False).reshape(
        tok_rows, -1
    )
    base_seed = mixing(drop_seed + batch_index * 1000003)
    seeds = mixing(base_seed ^ jnp.arange(QH, dtype=jnp.int32) * 1640531527)
    offset = (seq_index * tok_rows).reshape(1).astype(jnp.int32)
    pos = lax.dynamic_slice_in_dim(doc_positions[0], seq_index * tok_rows, tok_rows)[:, None]
    query_loc, grad_loc = queries[0], out_grad[0]
    key_full = gather_seq(key_states[0], seq_index, seq_devices)
    (dv,) = attention(seeds, offset, pos, query_loc, grad_loc, key_full, None)
    value_grad = reduce_seq(dv, seq_index, seq_devices).astype(jnp.bfloat16)
    grads_own = lax.all_gather(value_grad, "zx", axis=0, tiled=True)
    value_grad, weight_own, input_late = lax.optimization_barrier(
        (value_grad, weight_own, local_input)
    )
    weight_other = lax.ppermute(weight_own, "core", swap)
    input_cols = lax.all_to_all(
        input_late.reshape(tok_rows, seq_devices, fsdp_devices, block_rows),
        FSDP,
        split_axis=2,
        concat_axis=0,
        tiled=True,
    ).reshape(zx_devices, 2, tok_rows, seq_devices * block_rows)
    values_loc = (
        jnp.dot(input_own, weight_own, preferred_element_type=jnp.float32)
        + jnp.dot(input_other, weight_other, preferred_element_type=jnp.float32)
    ).astype(jnp.bfloat16)
    last_dims = (((1,), (1,)), ((), ()))
    grad_own = lax.dot_general(
        value_grad, weight_own, last_dims, preferred_element_type=jnp.float32
    ).astype(jnp.bfloat16).reshape(tok_rows, seq_devices * zx_devices, 1, block_rows)
    grad_other = lax.dot_general(
        value_grad, weight_other, last_dims, preferred_element_type=jnp.float32
    ).astype(jnp.bfloat16).reshape(tok_rows, seq_devices * zx_devices, 1, block_rows)
    input_grad = jnp.where(
        core_index == 0,
        jnp.concatenate([grad_own, grad_other], axis=2),
        jnp.concatenate([grad_other, grad_own], axis=2),
    ).reshape(tok_rows, zx_devices, seq_devices, 2, block_rows)
    input_grad = jnp.transpose(input_grad, (0, 2, 1, 3, 4)).reshape(tok_rows, -1)
    value_full = gather_seq(values_loc, seq_index, seq_devices)
    input_grad, value_full = lax.optimization_barrier((input_grad, value_full))
    dq, dk = attention(seeds, offset, pos, query_loc, grad_loc, key_full, value_full)
    key_grad = reduce_seq(dk, seq_index, seq_devices).astype(jnp.bfloat16)
    grads_own, input_cols, dq, key_grad = lax.optimization_barrier(
        (grads_own, input_cols, dq, key_grad)
    )
    query_grad = dq
    grads_other = lax.ppermute(grads_own, "core", swap)
    cols_own = lax.dynamic_index_in_dim(input_cols, core_index, 1, keepdims=False).reshape(
        zx_devices * tok_rows, -1
    )
    cols_other = lax.dynamic_index_in_dim(input_cols, 1 - core_index, 1, keepdims=False).reshape(
        zx_devices * tok_rows, -1
    )
    first_dims = (((0,), (0,)), ((), ()))
    partial = (
        lax.dot_general(cols_own, grads_own, first_dims, preferred_element_type=jnp.float32)
        + lax.dot_general(cols_other, grads_other, first_dims, preferred_element_type=jnp.float32)
    ).reshape(seq_devices, block_rows, KVH * HD)
    summed = lax.dynamic_index_in_dim(partial, seq_index, 0, keepdims=False)
    for shift in range(1, seq_devices):
        piece = lax.dynamic_index_in_dim(
            partial, (seq_index + shift) % seq_devices, 0, keepdims=False
        )
        summed = summed + lax.ppermute(
            piece.astype(jnp.bfloat16),
            "seq",
            [(i, (i + shift) % seq_devices) for i in range(seq_devices)],
        ).astype(jnp.float32)
    weight_grad = (summed * (1.0 / math.sqrt(fsdp_devices * seq_len))).astype(jnp.bfloat16)

    return (query_grad[None], key_grad[None], input_grad[None], weight_grad)


def solution(mesh):
    seq_devices, fsdp_devices = mesh.devices.shape
    chips = jax.sharding.Mesh(
        mesh.devices.reshape(seq_devices, fsdp_devices // 2, 2), ("seq",) + FSDP
    )
    return jax.shard_map(
        per_device,
        mesh=chips,
        in_specs=(
            P(FSDP, "seq", None),
            P(FSDP, "seq", None),
            P(FSDP, "seq", None),
            P(FSDP, "seq", None),
            P(FSDP, None),
            P(),
            P(("seq",) + FSDP, None),
        ),
        out_specs=(
            P(FSDP, "seq", None),
            P(FSDP, "seq", None),
            P(FSDP, "seq", None),
            P(("seq",) + FSDP, None),
        ),
        check_vma=False,
    )
```

```python
import functools
import math

import jax
import jax.numpy as jnp
from jax import lax
from jax.experimental import pallas as pl
from jax.experimental.pallas import tpu as pltpu
from jax.sharding import PartitionSpec as P

HD = 128
QH = 32
KVH = 4
ROWS = 128
FSDP = ("z", "x", "core")


drop_cut = 1677722
keep_scale = 1.0 / 0.9


def mixing(state):
    state = state ^ lax.shift_right_logical(state, jnp.full_like(state, 16))
    state = state * 2146121005
    state = state ^ lax.shift_right_logical(state, jnp.full_like(state, 15))
    state = state * 739982445
    state = state ^ lax.shift_right_logical(state, jnp.full_like(state, 16))
    return state


def attention_kernel(seeds_ref, offset_ref, pos_ref, q_ref, do_ref, k_ref, *refs, seq_len,
                     per_group, first):
    if first:
        (dv_ref,) = refs
    else:
        v_ref, dq_ref, dk_ref = refs
    g = pl.program_id(0)
    h = pl.program_id(1)
    head_seed = seeds_ref[g * per_group + h]
    inverse_root = 1.0 / math.sqrt(HD)
    last_dims = (((1,), (1,)), ((), ()))
    first_dims = (((0,), (0,)), ((), ()))
    acc_ref = dv_ref if first else dk_ref

    @pl.when(h == 0)
    def _():
        acc_ref[...] = jnp.zeros_like(acc_ref)

    q = q_ref[...]
    do = do_ref[...]
    k = k_ref[...]
    pos = pos_ref[...]
    rows_here = q.shape[0]
    scores = lax.dot_general(q, k, last_dims, preferred_element_type=jnp.float32) * inverse_root
    rows = lax.broadcasted_iota(jnp.int32, (rows_here, seq_len), 0) + offset_ref[0]
    cols = lax.broadcasted_iota(jnp.int32, (rows_here, seq_len), 1)
    visible = (cols <= rows) & (rows - cols <= pos)
    masked = jnp.where(visible, scores, -jnp.inf)
    row_max = jnp.max(masked, axis=1, keepdims=True)
    exp_terms = jnp.where(visible, jnp.exp(scores - row_max), 0.0)
    probs = exp_terms / jnp.sum(exp_terms, axis=1, keepdims=True)
    kept = (mixing(rows * seq_len + cols + head_seed) & 16777215) >= drop_cut
    if first:
        dropped = jnp.where(kept, probs * keep_scale, 0.0).astype(jnp.bfloat16)
        dv_ref[...] += lax.dot_general(dropped, do, first_dims, preferred_element_type=jnp.float32)
        return
    v = v_ref[...]
    raw = lax.dot_general(do, v, last_dims, preferred_element_type=jnp.float32)
    prob_grad = jnp.where(kept, raw * keep_scale, 0.0)
    row_delta = jnp.sum(probs * prob_grad, axis=1, keepdims=True)
    score_grad = (probs * (prob_grad - row_delta)).astype(jnp.bfloat16)
    dq = jnp.dot(score_grad, k, preferred_element_type=jnp.float32) * inverse_root
    dq_ref[...] = dq.astype(dq_ref.dtype)
    dk_ref[...] += (
        lax.dot_general(score_grad, q, first_dims, preferred_element_type=jnp.float32)
        * inverse_root
    )


def attention(seeds, offset, pos, queries, grads, keys, values):
    rows_here = queries.shape[0]
    seq_len = keys.shape[0]
    groups = keys.shape[1] // HD
    per_group = queries.shape[1] // HD // groups
    head_map = lambda g, h, s, o: (0, g * per_group + h)
    group_map = lambda g, h, s, o: (0, g)
    whole_map = lambda g, h, s, o: (0, 0)
    first = values is None
    kernel = functools.partial(
        attention_kernel, seq_len=seq_len, per_group=per_group, first=first
    )
    in_specs = [
        pl.BlockSpec((rows_here, 1), whole_map),
        pl.BlockSpec((rows_here, HD), head_map),
        pl.BlockSpec((rows_here, HD), head_map),
        pl.BlockSpec((seq_len, HD), group_map),
    ]
    operands = [seeds, offset, pos, queries, grads, keys]
    acc = jax.ShapeDtypeStruct(keys.shape, jnp.float32)
    if first:
        out_specs = [pl.BlockSpec((seq_len, HD), group_map)]
        out_shape = [acc]
    else:
        in_specs.append(pl.BlockSpec((seq_len, HD), group_map))
        operands.append(values)
        out_specs = [pl.BlockSpec((rows_here, HD), head_map), pl.BlockSpec((seq_len, HD), group_map)]
        out_shape = [jax.ShapeDtypeStruct(queries.shape, jnp.bfloat16), acc]
    return pl.pallas_call(
        kernel,
        grid_spec=pltpu.PrefetchScalarGridSpec(
            num_scalar_prefetch=2,
            grid=(groups, per_group),
            in_specs=in_specs,
            out_specs=out_specs,
        ),
        out_shape=out_shape,
        compiler_params=pltpu.CompilerParams(
            dimension_semantics=("arbitrary", "arbitrary"),
            vmem_limit_bytes=48 * 1024 * 1024,
        ),
    )(*operands)


def gather_seq(piece, seq_index, seq_devices):
    received = [piece]
    for shift in range(1, seq_devices):
        received.append(
            lax.ppermute(piece, "seq", [(i, (i + shift) % seq_devices) for i in range(seq_devices)])
        )
    order = (seq_index - jnp.arange(seq_devices, dtype=jnp.int32)) % seq_devices
    stacked = jnp.take(jnp.stack(received), order, axis=0)
    return stacked.reshape((seq_devices * piece.shape[0],) + piece.shape[1:])


def reduce_seq(partial, seq_index, seq_devices):
    blocks = partial.reshape((seq_devices, partial.shape[0] // seq_devices) + partial.shape[1:])
    summed = lax.dynamic_index_in_dim(blocks, seq_index, 0, keepdims=False)
    for shift in range(1, seq_devices):
        piece = lax.dynamic_index_in_dim(blocks, (seq_index + shift) % seq_devices, 0, keepdims=False)
        summed = summed + lax.ppermute(
            piece, "seq", [(i, (i + shift) % seq_devices) for i in range(seq_devices)]
        )
    return summed


def per_device(layer_input, queries, key_states, out_grad, doc_positions, drop_seed, value_weight):
    seq_devices = lax.axis_size("seq")
    z_devices = lax.axis_size("z")
    x_devices = lax.axis_size("x")
    zx_devices = z_devices * x_devices
    fsdp_devices = zx_devices * 2
    core_index = lax.axis_index("core")
    seq_index = lax.axis_index("seq")
    batch_index = lax.axis_index(FSDP)
    tok_rows = layer_input.shape[1]
    seq_len = tok_rows * seq_devices
    local_input = layer_input[0]
    block_rows = value_weight.shape[0]
    swap = [(0, 1), (1, 0)]
    weight_own = lax.all_gather(value_weight, ("seq", "z", "x"), axis=0, tiled=True)
    input_view = local_input.reshape(tok_rows, seq_devices * zx_devices, 2, block_rows)
    input_own = lax.dynamic_index_in_dim(input_view, core_index, 2, keepdims=False).reshape(
        tok_rows, -1
    )
    input_other = lax.dynamic_index_in_dim(input_view, 1 - core_index, 2, keepdims=False).reshape(
        tok_rows, -1
    )
    base_seed = mixing(drop_seed + batch_index * 1000003)
    seeds = mixing(base_seed ^ jnp.arange(QH, dtype=jnp.int32) * 1640531527)
    offset = (seq_index * tok_rows).reshape(1).astype(jnp.int32)
    pos = lax.dynamic_slice_in_dim(doc_positions[0], seq_index * tok_rows, tok_rows)[:, None]
    query_loc, grad_loc = queries[0], out_grad[0]
    key_full = gather_seq(key_states[0], seq_index, seq_devices)
    (dv,) = attention(seeds, offset, pos, query_loc, grad_loc, key_full, None)
    value_grad = reduce_seq(dv, seq_index, seq_devices).astype(jnp.bfloat16)
    grads_own = lax.all_gather(value_grad, ("x", "z"), axis=0, tiled=True)
    grads_own = jnp.transpose(
        grads_own.reshape(x_devices, z_devices, tok_rows, KVH * HD), (1, 0, 2, 3)
    ).reshape(zx_devices * tok_rows, KVH * HD)
    value_grad, weight_own, input_late = lax.optimization_barrier(
        (value_grad, weight_own, local_input)
    )
    weight_other = lax.ppermute(weight_own, "core", swap)
    input_cols = lax.all_to_all(
        input_late.reshape(tok_rows, seq_devices, fsdp_devices, block_rows),
        FSDP,
        split_axis=2,
        concat_axis=0,
        tiled=True,
    ).reshape(zx_devices, 2, tok_rows, seq_devices * block_rows)
    values_loc = (
        jnp.dot(input_own, weight_own, preferred_element_type=jnp.float32)
        + jnp.dot(input_other, weight_other, preferred_element_type=jnp.float32)
    ).astype(jnp.bfloat16)
    last_dims = (((1,), (1,)), ((), ()))
    grad_own = lax.dot_general(
        value_grad, weight_own, last_dims, preferred_element_type=jnp.float32
    ).astype(jnp.bfloat16).reshape(tok_rows, seq_devices * zx_devices, 1, block_rows)
    grad_other = lax.dot_general(
        value_grad, weight_other, last_dims, preferred_element_type=jnp.float32
    ).astype(jnp.bfloat16).reshape(tok_rows, seq_devices * zx_devices, 1, block_rows)
    input_grad = jnp.where(
        core_index == 0,
        jnp.concatenate([grad_own, grad_other], axis=2),
        jnp.concatenate([grad_other, grad_own], axis=2),
    ).reshape(tok_rows, -1)
    value_full = gather_seq(values_loc, seq_index, seq_devices)
    input_grad, value_full = lax.optimization_barrier((input_grad, value_full))
    dq, dk = attention(seeds, offset, pos, query_loc, grad_loc, key_full, value_full)
    key_grad = reduce_seq(dk, seq_index, seq_devices).astype(jnp.bfloat16)
    grads_own, input_cols, dq, key_grad = lax.optimization_barrier(
        (grads_own, input_cols, dq, key_grad)
    )
    query_grad = dq
    grads_other = lax.ppermute(grads_own, "core", swap)
    cols_own = lax.dynamic_index_in_dim(input_cols, core_index, 1, keepdims=False).reshape(
        zx_devices * tok_rows, -1
    )
    cols_other = lax.dynamic_index_in_dim(input_cols, 1 - core_index, 1, keepdims=False).reshape(
        zx_devices * tok_rows, -1
    )
    first_dims = (((0,), (0,)), ((), ()))
    partial = (
        lax.dot_general(cols_own, grads_own, first_dims, preferred_element_type=jnp.float32)
        + lax.dot_general(cols_other, grads_other, first_dims, preferred_element_type=jnp.float32)
    ).reshape(seq_devices, block_rows, KVH * HD)
    summed = lax.dynamic_index_in_dim(partial, seq_index, 0, keepdims=False)
    for shift in range(1, seq_devices):
        piece = lax.dynamic_index_in_dim(
            partial, (seq_index + shift) % seq_devices, 0, keepdims=False
        )
        summed = summed + lax.ppermute(
            piece.astype(jnp.bfloat16),
            "seq",
            [(i, (i + shift) % seq_devices) for i in range(seq_devices)],
        ).astype(jnp.float32)
    weight_grad = (summed * (1.0 / math.sqrt(fsdp_devices * seq_len))).astype(jnp.bfloat16)

    return (query_grad[None], key_grad[None], input_grad[None], weight_grad)


def solution(mesh):
    seq_devices, fsdp_devices = mesh.devices.shape
    z_devices = len({device.coords[2] for device in mesh.devices.flat})
    chips = jax.sharding.Mesh(
        mesh.devices.reshape(seq_devices, z_devices, fsdp_devices // 2 // z_devices, 2),
        ("seq",) + FSDP,
    )
    return jax.shard_map(
        per_device,
        mesh=chips,
        in_specs=(
            P(FSDP, "seq", None),
            P(FSDP, "seq", None),
            P(FSDP, "seq", None),
            P(FSDP, "seq", None),
            P(FSDP, None),
            P(),
            P(("seq",) + FSDP, None),
        ),
        out_specs=(
            P(FSDP, "seq", None),
            P(FSDP, "seq", None),
            P(FSDP, "seq", None),
            P(("seq",) + FSDP, None),
        ),
        check_vma=False,
    )
```
